32 devices in a mesh: groups: 2 (over y), lon: 8 (over z, x), lat: 2 (over core).
Axes of the slice: x: 2, y: 2, z: 4, core: 2. Of those that a mesh axis runs over, the one named last changes fastest.
Arguments:
- acts: bfloat16 [4, 96, 256, 256], P('groups', 'lat', 'lon'), parts along dimension 0, may hold values from -6 to 6
- rates: int32 [256], replicated, may hold values from 1 to 4, as said below
- dw_kernel: bfloat16 [9, 256], replicated, may hold values from -2 to 2
- pw_weight: bfloat16 [256, 256], replicated, may hold values from -0.375 to 0.375
- head_weight: bfloat16 [256, 227], replicated, may hold values from -0.375 to 0.375
- teacher_tiles: bfloat16 [512, 8, 227], P(('groups', 'lon', 'lat')), parts along dimension 0, may hold values from -6 to 6
- tile_dest: int32 [512, 1], P(('groups', 'lon', 'lat')), parts along dimension 0, may hold values from 0 to 15; in each aligned block of 16 rows (0 to 15, 16 to 31, ...) at most 2 rows name the same one
- tile_start: int32 [512], P(('groups', 'lon', 'lat')), parts along dimension 0, may hold values from 0 to 3064, as said below
- tile_count: int32 [512], P(('groups', 'lon', 'lat')), parts along dimension 0, may hold values from 1 to 8
Outputs:
- grad_dw: float32 [18, 256], P('groups'), parts along dimension 0
- grad_pw: float32 [512, 256], P('groups'), parts along dimension 0
- grad_head: float32 [512, 227], P('groups'), parts along dimension 0
- mse: float32 [2], P('groups'), parts along dimension 0
The draws below stay inside these ranges and needn't reach their ends.
There are 2 independent parts, one for each index of `groups`. The reference program is written for one: setup_inputs(seed, part) draws one part's arguments, and reference() takes and returns one part's arrays. A program takes and returns all parts, laid end to end along the dimension named above; an argument that names none is the same for every part. Nothing has to cross between parts.
Inputs may be any that keep to these rules, and one draw needn't show every extreme that they name: The channels form 4 contiguous groups of 64 channels; all channels of a group share one rate, and the groups take the rates 1 to 4, each once, in an order that varies. `tile_dest`: among the 16 tiles of one teacher partition no destination is named more than 2 times. A tile's 8 cells lie in one row of one sample of its destination's block: tile_start mod 32 is at most 24.
All inputs are finite; a program needn't handle non-finite values.
Results may differ from the reference program's by a relative error of at most 0.0045.
Values may be sent and summed in bfloat16 or wider, within the bound.
No kernel may reach another device: no remote copies, remote signals or barrier semaphores. Data moves between devices by JAX's collectives and lax.ppermute only.
A program may use at most 64 MiB of HBM per device.

```python
import math
import jax
import jax.numpy as jnp
import numpy as np
from jax import lax

C = 256
CT = 227
B = 2
HB = 48
WB = 32
DMAX = 4
TILE = 8
CAP = 2
DEVS = 16
NT = 16
TILES_ALL = 256
H = 96
W = 256
N_LON = 8
N_LAT = 2


def draw_rates(key, part):
    group_rates = jax.random.permutation(jax.random.fold_in(key, 11), DMAX) + 1
    values = jnp.repeat(group_rates, C // DMAX)
    return values.astype(jnp.int32)


def draw_tile_start(key, part):
    sample_of = jax.random.randint(jax.random.fold_in(key, 21), (TILES_ALL,), 0, B)
    inner_row = jax.random.randint(jax.random.fold_in(key, 22), (TILES_ALL,), 0, HB)
    first_col = jax.random.randint(jax.random.fold_in(key, 23), (TILES_ALL,), 0, WB - TILE + 1)
    values = (sample_of * HB + inner_row) * WB + first_col
    order = jax.random.permutation(jax.random.fold_in(key, 24), TILES_ALL)
    values = values.at[order[0]].set(B * HB * WB - TILE).at[order[1]].set(0)
    return values.astype(jnp.int32)


def draw_tile_count(key, part):
    values = jax.random.randint(jax.random.fold_in(key, 31), (TILES_ALL,), 1, TILE + 1)
    order = jax.random.permutation(jax.random.fold_in(key, 32), TILES_ALL)
    values = values.at[order[0]].set(TILE).at[order[1]].set(1)
    return values.astype(jnp.int32)


def level_of(own_key, shape, split, smallest, top_value):
    def one(position, blocks):
        steps = jax.random.uniform(jax.random.fold_in(jax.random.fold_in(own_key, 6), position), (blocks,), jnp.float32, smallest / len(split), top_value / len(split))
        return jnp.repeat(jnp.exp(steps), shape[position] // blocks).reshape((-1,) + (1,) * (len(shape) - position - 1))

    level = one(*split[0])
    for cut in split[1:]:
        level = level * one(*cut)
    return level


def shared_out(rng, own, number, rows, count, top, reach, slope):
    order = jax.random.permutation(rng, count)
    packed, ordinary = portions_of(count, rows * top, reach, slope, True), portions_of(count, rows * top, reach, slope, False)
    places = jnp.arange(count)

    def named(sizes, rotation):
        used = int((sizes > 0).sum())
        fixed = max(1, used // 4)
        moved = fixed + (places - fixed + rotation * (used - fixed)) % max(1, count - fixed)
        return jnp.zeros((count,), jnp.int32).at[order[jnp.where(places < fixed, places, moved)]].set(jnp.asarray(sizes, jnp.int32))

    sizes = jnp.where(number % 4 == 0, named(packed, number // 4), named(ordinary, number - number // 4 - 1))
    mixed = jax.random.permutation(jax.random.fold_in(own, 3), count)
    donor, receiver = mixed[0:count // 2 * 2:2], mixed[1:count // 2 * 2:2]
    margin = jnp.minimum(sizes[donor] - 1, reach - sizes[receiver]) // 2
    margin = jnp.where((donor == order[0]) | (receiver == order[0]) | (sizes[receiver] == 0), 0, jnp.maximum(margin, 0))
    moved = jax.random.randint(jax.random.fold_in(own, 4), (count // 2,), 0, 1 << 20) % (margin + 1)
    sizes = sizes.at[donor].add(-moved).at[receiver].add(moved)
    members = jnp.searchsorted(jnp.cumsum(sizes), jnp.arange(rows * top), side="right").astype(jnp.int32)
    table = members.reshape(top, rows).T
    table = table[jax.random.permutation(jax.random.fold_in(own, 1), rows)]
    rotation = jax.random.randint(jax.random.fold_in(own, 2), (rows, 1), 0, top)
    return jnp.take_along_axis(table, (jnp.arange(top)[None, :] + rotation) % top, axis=1)


def portions_of(amount, total, bound, slope, full):
    weights = [(1 << 20) // math.isqrt(rank ** slope) + 1 for rank in range(1, amount + 1)]
    largest = bound if full else min(bound, max(-(-total // amount), total * weights[0] // sum(weights)))
    least = 1 if total - largest >= amount - 1 else 0
    holding, rest = [largest] + [least] * (amount - 1), total - largest - least * (amount - 1)
    while rest > 0:
        free = [i for i in range(1, amount) if holding[i] < largest] or [i for i in range(1, amount) if holding[i] < bound]
        mass, remaining = sum([weights[i] for i in free]), rest
        for i in free:
            addition = min(bound - holding[i], max(1, remaining * weights[i] // mass), rest)
            holding[i] = holding[i] + addition
            rest = rest - addition
    return np.array(holding)


def bell_draw(key, dims, spread, most, cuts=(), held_as=jnp.bfloat16):
    values = jax.random.normal(key, dims, jnp.float32) * spread
    if len(cuts) > 0:
        values = level_of(key, dims, cuts, -0.22, 0.18) * values
    return jnp.clip(values, min=-most, max=most).astype(held_as)


def setup_inputs(seed: int = 0, part: int = 0) -> dict:
    key_list = jax.random.split(jax.random.key(seed), 10)
    part_keys = jax.random.split(jax.random.fold_in(key_list[9], part), 10)
    acts = bell_draw(part_keys[0], (B, H, W, C), 1.0, 6.0, ((1, 2), (2, 8)))
    rates = draw_rates(jax.random.fold_in(key_list[9], 71), part)
    dw_kernel = bell_draw(key_list[2], (9, C), 9 ** -0.5, 2.0)
    pw_weight = bell_draw(key_list[3], (C, C), C ** -0.5, 0.375)
    head_weight = bell_draw(key_list[4], (C, CT), C ** -0.5, 0.375)
    teacher_tiles = bell_draw(part_keys[5], (TILES_ALL, TILE, CT), 1.0, 6.0, ((0, 16),))
    tile_dest_keys = jax.random.split(jax.random.fold_in(part_keys[6], 1), TILES_ALL // NT)
    tile_dest_turns = jax.random.permutation(jax.random.fold_in(part_keys[6], 3), TILES_ALL // NT)
    tile_dest = jax.vmap(lambda own, number: shared_out(jax.random.fold_in(part_keys[6], 2), own, number, NT, DEVS, 1, CAP, 2))(tile_dest_keys, tile_dest_turns).reshape((TILES_ALL, 1))
    tile_start = draw_tile_start(jax.random.fold_in(jax.random.fold_in(key_list[9], part), 71), part)
    tile_count = draw_tile_count(jax.random.fold_in(jax.random.fold_in(key_list[9], part), 71), part)
    return {"acts": acts, "rates": rates, "dw_kernel": dw_kernel, "pw_weight": pw_weight, "head_weight": head_weight, "teacher_tiles": teacher_tiles, "tile_dest": tile_dest, "tile_start": tile_start, "tile_count": tile_count}


def dilated(padded, kernel, onehot, grid_rows, grid_cols):
    accum_sum = padded[..., DMAX:DMAX + grid_rows, DMAX:DMAX + grid_cols, :].astype(jnp.float32) * kernel[4]
    for dilation in range(1, DMAX + 1):
        for tap_index in range(9):
            if tap_index == 4:
                continue
            row_shift = (tap_index // 3 - 1) * dilation
            col_shift = (tap_index % 3 - 1) * dilation
            shifted = padded[..., DMAX + row_shift:DMAX + row_shift + grid_rows, DMAX + col_shift:DMAX + col_shift + grid_cols, :].astype(jnp.float32)
            accum_sum = accum_sum + kernel[tap_index] * onehot[dilation - 1] * shifted
    return accum_sum

def dilated_grad(padded, grad_z, onehot, grid_rows, grid_cols):
    width = grad_z.shape[-1]
    tap_sums = []
    for tap_index in range(9):
        if tap_index == 4:
            center = padded[..., DMAX:DMAX + grid_rows, DMAX:DMAX + grid_cols, :].astype(jnp.float32)
            tap_sums.append(lax.optimization_barrier(jnp.sum((center * grad_z).reshape(-1, width), axis=0)))
            continue
        tap_sum = jnp.zeros((width,), jnp.float32)
        for dilation in range(1, DMAX + 1):
            row_shift = (tap_index // 3 - 1) * dilation
            col_shift = (tap_index % 3 - 1) * dilation
            shifted = padded[..., DMAX + row_shift:DMAX + row_shift + grid_rows, DMAX + col_shift:DMAX + col_shift + grid_cols, :].astype(jnp.float32)
            tap_sum = tap_sum + onehot[dilation - 1] * lax.optimization_barrier(jnp.sum((shifted * grad_z).reshape(-1, width), axis=0))
        tap_sums.append(tap_sum)
    return jnp.stack(tap_sums, axis=0)

def pad_sample(field):
    grid_cols = field.shape[1]
    wrapped = jnp.concatenate([field[:, grid_cols - DMAX:], field, field[:, :DMAX]], axis=1)
    return jnp.pad(wrapped, ((DMAX, DMAX), (0, 0), (0, 0)))

def reference(acts, rates, dw_kernel, pw_weight, head_weight, teacher_tiles, tile_dest, tile_start, tile_count):
    grid_rows = HB * N_LAT
    grid_cols = WB * N_LON
    kernel = dw_kernel.astype(jnp.float32)
    onehot = (rates[None, :] == jnp.arange(1, DMAX + 1, dtype=jnp.int32)[:, None]).astype(jnp.float32)

    def forward(sample):
        depthwise_out = dilated(pad_sample(sample), kernel, onehot, grid_rows, grid_cols).astype(jnp.bfloat16)
        preact = jnp.dot(depthwise_out.reshape(-1, C), pw_weight, preferred_element_type=jnp.float32)
        block_out = (sample.reshape(-1, C).astype(jnp.float32) + jax.nn.silu(preact)).astype(jnp.bfloat16)
        return (depthwise_out, block_out)
    depth_all, block_all = lax.map(forward, acts)
    block_flat = block_all.reshape(-1, C)
    destination = tile_dest[:, 0]
    dest_lon = destination // N_LAT
    dest_lat = destination % N_LAT
    sample_of = tile_start // (HB * WB)
    inner_row = tile_start // WB % HB
    first_col = tile_start % WB
    offsets = jnp.arange(TILE, dtype=jnp.int32)
    glob_row = dest_lat * HB + inner_row
    glob_col = (dest_lon * WB + first_col)[:, None] + offsets[None, :]
    cell_inner = glob_row[:, None] * grid_cols + glob_col
    cell_index = sample_of[:, None] * (grid_rows * grid_cols) + cell_inner
    is_valid = offsets[None, :] < tile_count[:, None]
    area_weight = jnp.cos(jnp.pi * ((glob_row.astype(jnp.float32) + 0.5) / grid_rows - 0.5))
    row_weight = jnp.where(is_valid, area_weight[:, None], jnp.float32(0.0)) / jnp.float32(TILES_ALL * TILE)
    row_weight = row_weight.reshape(-1, 1)
    y_rows = block_flat[cell_index.reshape(-1)]
    predicted = jnp.dot(y_rows, head_weight, preferred_element_type=jnp.float32)
    residual = predicted - teacher_tiles.reshape(-1, CT).astype(jnp.float32)
    loss_sum = jnp.sum(row_weight * residual * residual)
    grad_pred = (2.0 * row_weight * residual).astype(jnp.bfloat16)
    grad_head = lax.dot_general(y_rows, grad_pred, (((0,), (0,)), ((), ())), preferred_element_type=jnp.float32)
    grad_rows = jnp.dot(grad_pred, head_weight.T, preferred_element_type=jnp.float32)
    row_sample = jnp.broadcast_to(sample_of[:, None], (TILES_ALL, TILE)).reshape(-1)
    inner_flat = cell_inner.reshape(-1)

    def backward(carried, inputs):
        grad_dw, grad_pw = carried
        depthwise_out, sample, sample_index = inputs
        in_sample = (row_sample == sample_index)[:, None]
        grad_y = jnp.zeros((grid_rows * grid_cols, C), jnp.float32).at[inner_flat].add(jnp.where(in_sample, grad_rows, jnp.float32(0.0)))
        depth_flat = depthwise_out.reshape(-1, C)
        preact = jnp.dot(depth_flat, pw_weight, preferred_element_type=jnp.float32)
        sigmoid_u = jax.nn.sigmoid(preact)
        grad_u = (grad_y * sigmoid_u * (1.0 + preact * (1.0 - sigmoid_u))).astype(jnp.bfloat16)
        grad_pw = grad_pw + lax.dot_general(depth_flat, grad_u, (((0,), (0,)), ((), ())), preferred_element_type=jnp.float32)
        grad_z = jnp.dot(grad_u, pw_weight.T, preferred_element_type=jnp.float32).reshape(grid_rows, grid_cols, C)
        grad_dw = grad_dw + dilated_grad(pad_sample(sample), grad_z, onehot, grid_rows, grid_cols)
        return ((grad_dw, grad_pw), None)
    start = (jnp.zeros((9, C), jnp.float32), jnp.zeros((C, C), jnp.float32))
    (grad_dw, grad_pw), unused = lax.scan(backward, start, (depth_all, acts, jnp.arange(B, dtype=jnp.int32)))
    return (grad_dw, grad_pw, grad_head, (loss_sum / CT).reshape(1))
```

```python
import jax
import jax.numpy as jnp
from jax import lax
from jax.sharding import PartitionSpec as P

DMAX = 4
TILE = 8
CAP = 2


LANES = 128


def halve(x, axis, bit):
    count = lax.axis_size(axis)
    rows = x.shape[0] // 2
    upper = (lax.axis_index(axis) // bit) % 2
    keep = lax.dynamic_slice_in_dim(x, upper * rows, rows, 0)
    send = lax.dynamic_slice_in_dim(x, (1 - upper) * rows, rows, 0)
    return keep + lax.ppermute(send, axis, [(i, i ^ bit) for i in range(count)])


def double(x, axis, bit):
    count = lax.axis_size(axis)
    rows = x.shape[0]
    upper = (lax.axis_index(axis) // bit) % 2
    got = lax.ppermute(x, axis, [(i, i ^ bit) for i in range(count)])
    whole = jnp.zeros((2 * rows,) + x.shape[1:], x.dtype)
    whole = lax.dynamic_update_slice_in_dim(whole, x, upper * rows, 0)
    return lax.dynamic_update_slice_in_dim(whole, got, (1 - upper) * rows, 0)


def packed_sum(values, axes):
    steps = []
    rest = []
    for axis in axes:
        count = lax.axis_size(axis)
        if count & (count - 1):
            rest.append(axis)
            continue
        bit = 1
        while bit < count:
            steps.append((axis, bit))
            bit *= 2
    flat = jnp.concatenate([jnp.ravel(v).astype(jnp.float32) for v in values])
    unit = 8 * LANES * (2 ** len(steps))
    total = -(-flat.shape[0] // unit) * unit
    x = jnp.pad(flat, (0, total - flat.shape[0])).reshape(-1, LANES)
    for axis, bit in steps:
        x = halve(x, axis, bit)
    if rest:
        x = lax.psum(x, tuple(rest))
    for axis, bit in reversed(steps):
        x = double(x, axis, bit)
    flat = x.reshape(-1)
    out = []
    offset = 0
    for v in values:
        out.append(flat[offset : offset + v.size].reshape(v.shape))
        offset += v.size
    return tuple(out)


def padded_2(cells, sides, width, closed):
    for axis, dim in sides:
        count = lax.axis_size(axis)
        ends = count if closed else count - 1
        head = lax.slice_in_dim(cells, 0, width, axis=dim)
        tail = lax.slice_in_dim(cells, cells.shape[dim] - width, cells.shape[dim], axis=dim)
        cells = jnp.concatenate(
            [
                lax.ppermute(tail, axis, [(i, (i + 1) % count) for i in range(ends)]),
                cells,
                lax.ppermute(head, axis, [((i + 1) % count, i) for i in range(ends)]),
            ],
            axis=dim,
        )
    return cells


def tap_window(group_in, rate, tap_index, band_rows, block_cols):
    row_start = DMAX + (tap_index // 3 - 1) * rate
    col_start = DMAX + (tap_index % 3 - 1) * rate
    zero = jnp.int32(0)
    sizes = (group_in.shape[0], band_rows, block_cols, group_in.shape[3])
    return lax.dynamic_slice(group_in, (zero, row_start, col_start, zero), sizes)


def dilated(padded, kernel, rates, band_rows, block_cols):
    width = padded.shape[-1]
    group_width = width // DMAX
    outputs = []
    for group in range(DMAX):
        low = group * group_width
        group_in = padded[..., low : low + group_width]
        rate = rates[low]
        accum_sum = None
        for tap_index in range(9):
            window = tap_window(group_in, rate, tap_index, band_rows, block_cols)
            term = window.astype(jnp.float32) * kernel[tap_index, low : low + group_width]
            accum_sum = term if accum_sum is None else accum_sum + term
        outputs.append(accum_sum)
    return jnp.concatenate(outputs, axis=-1)


def dilated_grad(padded, grad_z, rates, band_rows, block_cols):
    width = padded.shape[-1]
    group_width = width // DMAX
    columns = []
    for group in range(DMAX):
        low = group * group_width
        group_in = padded[..., low : low + group_width]
        group_grad = grad_z[..., low : low + group_width]
        rate = rates[low]
        tap_sums = []
        for tap_index in range(9):
            window = tap_window(group_in, rate, tap_index, band_rows, block_cols)
            tap_sums.append(
                jnp.sum((window.astype(jnp.float32) * group_grad).reshape(-1, group_width), axis=0)
            )
        columns.append(jnp.stack(tap_sums, axis=0))
    return jnp.concatenate(columns, axis=1)


def local(
    acts, rates, dw_kernel, pw_weight, head_weight, teacher_tiles, tile_dest, tile_start, tile_count
):
    micro_batch, band_rows, block_cols, width = acts.shape
    teach_width = head_weight.shape[1]
    lat_index = lax.axis_index("lat")
    lat_count = lax.axis_size("lat")
    lon_count = lax.axis_size("lon")
    devices = lon_count * lat_count
    lon_padded = padded_2(acts, (("lon", 2),), DMAX, True)
    padded = padded_2(lon_padded, (("lat", 1),), DMAX, False)
    kernel = dw_kernel.astype(jnp.float32)
    depthwise_out = dilated(padded, kernel, rates, band_rows, block_cols).astype(jnp.bfloat16)
    depth_flat = depthwise_out.reshape(-1, width)
    preact = jnp.dot(depth_flat, pw_weight, preferred_element_type=jnp.float32)
    block_flat = (acts.reshape(-1, width).astype(jnp.float32) + jax.nn.silu(preact)).astype(
        jnp.bfloat16
    )
    tiles_here = teacher_tiles.shape[0]
    destination = tile_dest[:, 0]
    positions = jnp.arange(tiles_here, dtype=jnp.int32)
    same_dest = destination[:, None] == destination[None, :]
    earlier = positions[:, None] > positions[None, :]
    slot_rank = jnp.sum((same_dest & earlier).astype(jnp.int32), axis=1)
    slot_index = destination * CAP + slot_rank
    send_tiles = (
        jnp.zeros((devices * CAP, TILE, teach_width), jnp.bfloat16)
        .at[slot_index]
        .set(teacher_tiles)
    )
    send_start = jnp.zeros((devices * CAP,), jnp.int32).at[slot_index].set(tile_start)
    send_count = jnp.zeros((devices * CAP,), jnp.int32).at[slot_index].set(tile_count)
    recv_tiles, recv_start, recv_count = (
        lax.all_to_all(send_tiles, ("lon", "lat"), split_axis=0, concat_axis=0, tiled=True),
        lax.all_to_all(send_start, ("lon", "lat"), split_axis=0, concat_axis=0, tiled=True),
        lax.all_to_all(send_count, ("lon", "lat"), split_axis=0, concat_axis=0, tiled=True),
    )
    offsets = jnp.arange(TILE, dtype=jnp.int32)
    cell_index = recv_start[:, None] + offsets[None, :]
    is_valid = offsets[None, :] < recv_count[:, None]
    inner_row = recv_start // block_cols % band_rows
    glob_row = lat_index * band_rows + inner_row
    area_weight = jnp.cos(
        jnp.pi * ((glob_row.astype(jnp.float32) + 0.5) / (band_rows * lat_count) - 0.5)
    )
    row_weight = jnp.where(is_valid, area_weight[:, None], jnp.float32(0.0)) / jnp.float32(
        devices * tiles_here * TILE
    )
    row_weight = row_weight.reshape(-1, 1)
    cell_flat = cell_index.reshape(-1)
    y_rows = block_flat[cell_flat]
    predicted = jnp.dot(y_rows, head_weight, preferred_element_type=jnp.float32)
    residual = predicted - recv_tiles.reshape(-1, teach_width).astype(jnp.float32)
    loss_sum = jnp.sum(row_weight * residual * residual)
    grad_pred = (2.0 * row_weight * residual).astype(jnp.bfloat16)
    grad_head = lax.dot_general(
        y_rows, grad_pred, (((0,), (0,)), ((), ())), preferred_element_type=jnp.float32
    )
    grad_rows = jnp.dot(grad_pred, head_weight.T, preferred_element_type=jnp.float32)
    grad_y = jnp.zeros((block_flat.shape[0], width), jnp.float32).at[cell_flat].add(grad_rows)
    sigmoid_u = jax.nn.sigmoid(preact)
    grad_u = (grad_y * sigmoid_u * (1.0 + preact * (1.0 - sigmoid_u))).astype(jnp.bfloat16)
    grad_pw = lax.dot_general(
        depth_flat, grad_u, (((0,), (0,)), ((), ())), preferred_element_type=jnp.float32
    )
    grad_z = jnp.dot(grad_u, pw_weight.T, preferred_element_type=jnp.float32).reshape(
        micro_batch, band_rows, block_cols, width
    )
    grad_dw = dilated_grad(padded, grad_z, rates, band_rows, block_cols)
    grad_dw, grad_pw, grad_head, loss_sum = packed_sum(
        (grad_dw, grad_pw, grad_head, loss_sum), ("lat", "lon")
    )
    return (grad_dw, grad_pw, grad_head, (loss_sum / teach_width).reshape(1))


def solution(mesh):
    in_specs = (
        P("groups", "lat", "lon", None),
        P(),
        P(),
        P(),
        P(),
        P(("groups", "lon", "lat"), None, None),
        P(("groups", "lon", "lat"), None),
        P(("groups", "lon", "lat")),
        P(("groups", "lon", "lat")),
    )
    out_specs = (P("groups", None), P("groups", None), P("groups", None), P("groups"))
    return jax.shard_map(local, mesh=mesh, in_specs=in_specs, out_specs=out_specs, check_vma=False)
```

```python
import jax
import jax.numpy as jnp
from jax import lax
from jax.sharding import PartitionSpec as P

DMAX = 4
TILE = 8
CAP = 2
CHUNK = 32


LANES = 128


def halve(x, axis, bit):
    count = lax.axis_size(axis)
    rows = x.shape[0] // 2
    upper = (lax.axis_index(axis) // bit) % 2
    keep = lax.dynamic_slice_in_dim(x, upper * rows, rows, 0)
    send = lax.dynamic_slice_in_dim(x, (1 - upper) * rows, rows, 0)
    return keep + lax.ppermute(send, axis, [(i, i ^ bit) for i in range(count)])


def double(x, axis, bit):
    count = lax.axis_size(axis)
    rows = x.shape[0]
    upper = (lax.axis_index(axis) // bit) % 2
    got = lax.ppermute(x, axis, [(i, i ^ bit) for i in range(count)])
    whole = jnp.zeros((2 * rows,) + x.shape[1:], x.dtype)
    whole = lax.dynamic_update_slice_in_dim(whole, x, upper * rows, 0)
    return lax.dynamic_update_slice_in_dim(whole, got, (1 - upper) * rows, 0)


def packed_sum(values, axes):
    steps = []
    rest = []
    for axis in axes:
        count = lax.axis_size(axis)
        if count & (count - 1):
            rest.append(axis)
            continue
        bit = 1
        while bit < count:
            steps.append((axis, bit))
            bit *= 2
    flat = jnp.concatenate([jnp.ravel(v).astype(jnp.float32) for v in values])
    unit = 8 * LANES * (2 ** len(steps))
    total = -(-flat.shape[0] // unit) * unit
    x = jnp.pad(flat, (0, total - flat.shape[0])).reshape(-1, LANES)
    for axis, bit in steps:
        x = halve(x, axis, bit)
    if rest:
        x = lax.psum(x, tuple(rest))
    for axis, bit in reversed(steps):
        x = double(x, axis, bit)
    flat = x.reshape(-1)
    out = []
    offset = 0
    for v in values:
        out.append(flat[offset : offset + v.size].reshape(v.shape))
        offset += v.size
    return tuple(out)


def padded_2(cells, sides, width, closed):
    for axis, dim in sides:
        count = lax.axis_size(axis)
        ends = count if closed else count - 1
        head = lax.slice_in_dim(cells, 0, width, axis=dim)
        tail = lax.slice_in_dim(cells, cells.shape[dim] - width, cells.shape[dim], axis=dim)
        cells = jnp.concatenate(
            [
                lax.ppermute(tail, axis, [(i, (i + 1) % count) for i in range(ends)]),
                cells,
                lax.ppermute(head, axis, [((i + 1) % count, i) for i in range(ends)]),
            ],
            axis=dim,
        )
    return cells


def local(
    acts, rates, dw_kernel, pw_weight, head_weight, teacher_tiles, tile_dest, tile_start, tile_count
):
    micro_batch, band_rows, block_cols, width = acts.shape
    teach_width = head_weight.shape[1]
    lat_index = lax.axis_index("lat")
    lat_count = lax.axis_size("lat")
    lon_count = lax.axis_size("lon")
    devices = lon_count * lat_count
    lon_padded = padded_2(acts, (("lon", 2),), DMAX, True)
    padded = padded_2(lon_padded, (("lat", 1),), DMAX, False)
    tiles_here = teacher_tiles.shape[0]
    destination = tile_dest[:, 0]
    positions = jnp.arange(tiles_here, dtype=jnp.int32)
    same_dest = destination[:, None] == destination[None, :]
    earlier = positions[:, None] > positions[None, :]
    slot_rank = jnp.sum((same_dest & earlier).astype(jnp.int32), axis=1)
    slot_index = destination * CAP + slot_rank
    send_tiles = (
        jnp.zeros((devices * CAP, TILE, teach_width), jnp.bfloat16)
        .at[slot_index]
        .set(teacher_tiles)
    )
    send_start = jnp.zeros((devices * CAP,), jnp.int32).at[slot_index].set(tile_start)
    send_count = jnp.zeros((devices * CAP,), jnp.int32).at[slot_index].set(tile_count)
    recv_tiles, recv_start, recv_count = (
        lax.all_to_all(send_tiles, ("lon", "lat"), split_axis=0, concat_axis=0, tiled=True),
        lax.all_to_all(send_start, ("lon", "lat"), split_axis=0, concat_axis=0, tiled=True),
        lax.all_to_all(send_count, ("lon", "lat"), split_axis=0, concat_axis=0, tiled=True),
    )
    offsets = jnp.arange(TILE, dtype=jnp.int32)
    is_valid = offsets[None, :] < recv_count[:, None]
    sample_of = recv_start // (block_cols * band_rows)
    inner_row = recv_start // block_cols % band_rows
    first_col = recv_start % block_cols
    glob_row = lat_index * band_rows + inner_row
    area_weight = jnp.cos(
        jnp.pi * ((glob_row.astype(jnp.float32) + 0.5) / (band_rows * lat_count) - 0.5)
    )
    row_weight = jnp.where(is_valid, area_weight[:, None], jnp.float32(0.0)) / jnp.float32(
        devices * tiles_here * TILE
    )
    kernel = dw_kernel.astype(jnp.float32)
    onehot = (
        rates[None, :] == jnp.arange(1, DMAX + 1, dtype=jnp.int32)[:, None]
    ).astype(jnp.float32)
    span = 2 * DMAX + 1
    reach = TILE + 2 * DMAX

    def gather_windows(place):
        b, h, w = place
        return jax.vmap(
            lambda b, h, w: lax.dynamic_slice(
                padded, (b, h, w, jnp.int32(0)), (1, span, reach, width)
            )[0]
        )(b, h, w)

    def shifted(source, row_shift, col_shift):
        return source[:, DMAX + row_shift, DMAX + col_shift : DMAX + col_shift + TILE, :].astype(
            jnp.float32
        )

    def forward(windows, tiles, weight):
        center = shifted(windows, 0, 0)
        accum_sum = center * kernel[4]
        for dilation in range(1, DMAX + 1):
            for tap_index in range(9):
                if tap_index == 4:
                    continue
                row_shift = (tap_index // 3 - 1) * dilation
                col_shift = (tap_index % 3 - 1) * dilation
                accum_sum = accum_sum + kernel[tap_index] * onehot[dilation - 1] * shifted(
                    windows, row_shift, col_shift
                )
        depth_flat = accum_sum.astype(jnp.bfloat16).reshape(-1, width)
        preact = jnp.dot(depth_flat, pw_weight, preferred_element_type=jnp.float32)
        y_rows = (center.reshape(-1, width) + jax.nn.silu(preact)).astype(jnp.bfloat16)
        weight = weight.reshape(-1, 1)
        predicted = jnp.dot(y_rows, head_weight, preferred_element_type=jnp.float32)
        residual = predicted - tiles.reshape(-1, teach_width).astype(jnp.float32)
        loss_part = jnp.sum(weight * residual * residual)
        grad_pred = (2.0 * weight * residual).astype(jnp.bfloat16)
        head_part = lax.dot_general(
            y_rows, grad_pred, (((0,), (0,)), ((), ())), preferred_element_type=jnp.float32
        )
        grad_rows = jnp.dot(grad_pred, head_weight.T, preferred_element_type=jnp.float32)
        return depth_flat, preact, grad_rows, loss_part, head_part

    def backward(windows, depth_flat, grad_u):
        pw_part = lax.dot_general(
            depth_flat, grad_u, (((0,), (0,)), ((), ())), preferred_element_type=jnp.float32
        )
        grad_z = jnp.dot(grad_u, pw_weight.T, preferred_element_type=jnp.float32)
        grad_z = grad_z.reshape(windows.shape[0], TILE, width)
        tap_sums = []
        for tap_index in range(9):
            if tap_index == 4:
                part = shifted(windows, 0, 0) * grad_z
                tap_sums.append(jnp.sum(part.reshape(-1, width), axis=0))
                continue
            tap_sum = jnp.zeros((width,), jnp.float32)
            for dilation in range(1, DMAX + 1):
                row_shift = (tap_index // 3 - 1) * dilation
                col_shift = (tap_index % 3 - 1) * dilation
                part = shifted(windows, row_shift, col_shift) * grad_z
                part = jnp.sum(part.reshape(-1, width), axis=0)
                tap_sum = tap_sum + onehot[dilation - 1] * part
            tap_sums.append(tap_sum)
        return pw_part, jnp.stack(tap_sums, axis=0)

    slots = recv_start.shape[0]
    chunk = min(slots, CHUNK)
    chunks = slots // chunk
    place = (sample_of, inner_row, first_col)
    if chunks == 1:
        windows = gather_windows(place)
        depth_flat, preact, grad_rows, loss_sum, grad_head = forward(
            windows, recv_tiles, row_weight
        )
    else:
        split = lambda v: v.reshape((chunks, chunk) + v.shape[1:])
        outs = lax.map(
            lambda xs: forward(gather_windows(xs[0]), xs[1], xs[2]),
            (tuple(split(v) for v in place), split(recv_tiles), split(row_weight)),
        )
        depth_flat, preact, grad_rows = (v.reshape((-1, width)) for v in outs[:3])
        loss_sum, grad_head = jnp.sum(outs[3]), jnp.sum(outs[4], axis=0)
    cell = (recv_start[:, None] + offsets[None, :]).reshape(-1)
    row_ids = jnp.arange(cell.shape[0], dtype=jnp.int32)
    if cell.shape[0] <= 512:
        same_cell = cell[:, None] == cell[None, :]
        grad_y = jnp.dot(
            same_cell.astype(jnp.float32),
            grad_rows,
            precision=lax.Precision.HIGHEST,
            preferred_element_type=jnp.float32,
        )
        repeated = jnp.any(same_cell & (row_ids[None, :] < row_ids[:, None]), axis=1)
    else:
        cells_here = micro_batch * band_rows * block_cols
        grid = jnp.zeros((cells_here, width), jnp.float32).at[cell].add(grad_rows)
        grad_y = grid[cell]
        owner = jnp.full((cells_here,), cell.shape[0], jnp.int32).at[cell].min(row_ids)
        repeated = owner[cell] != row_ids
    sigmoid_u = jax.nn.sigmoid(preact)
    grad_u = (grad_y * sigmoid_u * (1.0 + preact * (1.0 - sigmoid_u))).astype(jnp.bfloat16)
    grad_u = jnp.where(repeated[:, None], jnp.zeros_like(grad_u), grad_u)
    if chunks == 1:
        windows_again, grad_u = lax.optimization_barrier((windows, grad_u))
        grad_pw, grad_dw = backward(windows_again, depth_flat, grad_u)
    else:
        rows_split = lambda v: v.reshape((chunks, chunk * TILE) + v.shape[1:])
        outs = lax.map(
            lambda xs: backward(gather_windows(xs[0]), xs[1], xs[2]),
            (tuple(split(v) for v in place), rows_split(depth_flat), rows_split(grad_u)),
        )
        grad_pw, grad_dw = jnp.sum(outs[0], axis=0), jnp.sum(outs[1], axis=0)
    grad_dw, grad_pw, grad_head, loss_sum = packed_sum(
        (grad_dw, grad_pw, grad_head, loss_sum), ("lat", "lon")
    )
    return (grad_dw, grad_pw, grad_head, (loss_sum / teach_width).reshape(1))


def solution(mesh):
    in_specs = (
        P("groups", "lat", "lon", None),
        P(),
        P(),
        P(),
        P(),
        P(("groups", "lon", "lat"), None, None),
        P(("groups", "lon", "lat"), None),
        P(("groups", "lon", "lat")),
        P(("groups", "lon", "lat")),
    )
    out_specs = (P("groups", None), P("groups", None), P("groups", None), P("groups"))
    return jax.shard_map(local, mesh=mesh, in_specs=in_specs, out_specs=out_specs, check_vma=False)
```

```python
import jax
import jax.numpy as jnp
from jax import lax
from jax.sharding import PartitionSpec as P

DMAX = 4
TILE = 8
CAP = 2
CHUNK = 32


LANES = 128


def halve(x, axis, bit):
    count = lax.axis_size(axis)
    rows = x.shape[0] // 2
    upper = (lax.axis_index(axis) // bit) % 2
    keep = lax.dynamic_slice_in_dim(x, upper * rows, rows, 0)
    send = lax.dynamic_slice_in_dim(x, (1 - upper) * rows, rows, 0)
    return keep + lax.ppermute(send, axis, [(i, i ^ bit) for i in range(count)])


def double(x, axis, bit):
    count = lax.axis_size(axis)
    rows = x.shape[0]
    upper = (lax.axis_index(axis) // bit) % 2
    got = lax.ppermute(x, axis, [(i, i ^ bit) for i in range(count)])
    whole = jnp.zeros((2 * rows,) + x.shape[1:], x.dtype)
    whole = lax.dynamic_update_slice_in_dim(whole, x, upper * rows, 0)
    return lax.dynamic_update_slice_in_dim(whole, got, (1 - upper) * rows, 0)


def packed_sum(values, axes):
    steps = []
    rest = []
    for axis in axes:
        count = lax.axis_size(axis)
        if count & (count - 1):
            rest.append(axis)
            continue
        bit = 1
        while bit < count:
            steps.append((axis, bit))
            bit *= 2
    flat = jnp.concatenate([jnp.ravel(v).astype(jnp.float32) for v in values])
    unit = 8 * LANES * (2 ** len(steps))
    total = -(-flat.shape[0] // unit) * unit
    x = jnp.pad(flat, (0, total - flat.shape[0])).reshape(-1, LANES)
    for axis, bit in steps:
        x = halve(x, axis, bit)
    if rest:
        x = lax.psum(x, tuple(rest))
    for axis, bit in reversed(steps):
        x = double(x, axis, bit)
    flat = x.reshape(-1)
    out = []
    offset = 0
    for v in values:
        out.append(flat[offset : offset + v.size].reshape(v.shape))
        offset += v.size
    return tuple(out)


def padded_2(cells, sides, width, closed):
    for axis, dim in sides:
        count = lax.axis_size(axis)
        ends = count if closed else count - 1
        head = lax.slice_in_dim(cells, 0, width, axis=dim)
        tail = lax.slice_in_dim(cells, cells.shape[dim] - width, cells.shape[dim], axis=dim)
        cells = jnp.concatenate(
            [
                lax.ppermute(tail, axis, [(i, (i + 1) % count) for i in range(ends)]),
                cells,
                lax.ppermute(head, axis, [((i + 1) % count, i) for i in range(ends)]),
            ],
            axis=dim,
        )
    return cells


def local(
    acts, rates, dw_kernel, pw_weight, head_weight, teacher_tiles, tile_dest, tile_start, tile_count
):
    micro_batch, band_rows, block_cols, width = acts.shape
    teach_width = head_weight.shape[1]
    lat_index = lax.axis_index("lat")
    lat_count = lax.axis_size("lat")
    lon_count = lax.axis_size("lon")
    devices = lon_count * lat_count
    lon_padded = padded_2(acts, (("lon", 2),), DMAX, True)
    padded = padded_2(lon_padded, (("lat", 1),), DMAX, False)
    tiles_here = teacher_tiles.shape[0]
    destination = tile_dest[:, 0]
    positions = jnp.arange(tiles_here, dtype=jnp.int32)
    same_dest = destination[:, None] == destination[None, :]
    earlier = positions[:, None] > positions[None, :]
    slot_rank = jnp.sum((same_dest & earlier).astype(jnp.int32), axis=1)
    slot_index = destination * CAP + slot_rank
    slots = devices * CAP
    base = 64
    column = jnp.zeros((tiles_here, TILE, 1), jnp.float32)
    column = column.at[:, 0, 0].set((tile_start // base).astype(jnp.float32))
    column = column.at[:, 1, 0].set((tile_start % base).astype(jnp.float32))
    column = column.at[:, 2, 0].set(tile_count.astype(jnp.float32))
    packed = jnp.concatenate([teacher_tiles, column.astype(jnp.bfloat16)], axis=2)
    chooser = (slot_index[None, :] == jnp.arange(slots, dtype=jnp.int32)[:, None]).astype(
        jnp.bfloat16
    )
    send = jnp.dot(
        chooser, packed.reshape(tiles_here, -1), preferred_element_type=jnp.float32
    ).astype(jnp.bfloat16)
    recv = lax.all_to_all(
        send.reshape(slots, TILE, teach_width + 1),
        ("lon", "lat"),
        split_axis=0,
        concat_axis=0,
        tiled=True,
    )
    recv_tiles = recv[:, :, :teach_width]
    meta = recv[:, :3, teach_width].astype(jnp.int32)
    recv_start = meta[:, 0] * base + meta[:, 1]
    recv_count = meta[:, 2]
    offsets = jnp.arange(TILE, dtype=jnp.int32)
    is_valid = offsets[None, :] < recv_count[:, None]
    sample_of = recv_start // (block_cols * band_rows)
    inner_row = recv_start // block_cols % band_rows
    first_col = recv_start % block_cols
    glob_row = lat_index * band_rows + inner_row
    area_weight = jnp.cos(
        jnp.pi * ((glob_row.astype(jnp.float32) + 0.5) / (band_rows * lat_count) - 0.5)
    )
    row_weight = jnp.where(is_valid, area_weight[:, None], jnp.float32(0.0)) / jnp.float32(
        devices * tiles_here * TILE
    )
    kernel = dw_kernel.astype(jnp.float32)
    onehot = (
        rates[None, :] == jnp.arange(1, DMAX + 1, dtype=jnp.int32)[:, None]
    ).astype(jnp.float32)
    span = 2 * DMAX + 1
    reach = TILE + 2 * DMAX

    def gather_windows(place):
        b, h, w = place
        return jax.vmap(
            lambda b, h, w: lax.dynamic_slice(
                padded, (b, h, w, jnp.int32(0)), (1, span, reach, width)
            )[0]
        )(b, h, w)

    def shifted(source, row_shift, col_shift):
        return source[:, DMAX + row_shift, DMAX + col_shift : DMAX + col_shift + TILE, :].astype(
            jnp.float32
        )

    def forward(windows, tiles, weight):
        center = shifted(windows, 0, 0)
        accum_sum = center * kernel[4]
        for dilation in range(1, DMAX + 1):
            for tap_index in range(9):
                if tap_index == 4:
                    continue
                row_shift = (tap_index // 3 - 1) * dilation
                col_shift = (tap_index % 3 - 1) * dilation
                accum_sum = accum_sum + kernel[tap_index] * onehot[dilation - 1] * shifted(
                    windows, row_shift, col_shift
                )
        depth_flat = accum_sum.astype(jnp.bfloat16).reshape(-1, width)
        preact = jnp.dot(depth_flat, pw_weight, preferred_element_type=jnp.float32)
        y_rows = (center.reshape(-1, width) + jax.nn.silu(preact)).astype(jnp.bfloat16)
        weight = weight.reshape(-1, 1)
        predicted = jnp.dot(y_rows, head_weight, preferred_element_type=jnp.float32)
        residual = predicted - tiles.reshape(-1, teach_width).astype(jnp.float32)
        loss_part = jnp.sum(weight * residual * residual)
        grad_pred = (2.0 * weight * residual).astype(jnp.bfloat16)
        head_part = lax.dot_general(
            y_rows, grad_pred, (((0,), (0,)), ((), ())), preferred_element_type=jnp.float32
        )
        grad_rows = jnp.dot(grad_pred, head_weight.T, preferred_element_type=jnp.float32)
        return depth_flat, preact, grad_rows, loss_part, head_part

    def backward(windows, depth_flat, grad_u):
        pw_part = lax.dot_general(
            depth_flat, grad_u, (((0,), (0,)), ((), ())), preferred_element_type=jnp.float32
        )
        grad_z = jnp.dot(grad_u, pw_weight.T, preferred_element_type=jnp.float32)
        grad_z = grad_z.reshape(windows.shape[0], TILE, width)
        tap_sums = []
        for tap_index in range(9):
            if tap_index == 4:
                part = shifted(windows, 0, 0) * grad_z
                tap_sums.append(jnp.sum(part.reshape(-1, width), axis=0))
                continue
            tap_sum = jnp.zeros((width,), jnp.float32)
            for dilation in range(1, DMAX + 1):
                row_shift = (tap_index // 3 - 1) * dilation
                col_shift = (tap_index % 3 - 1) * dilation
                part = shifted(windows, row_shift, col_shift) * grad_z
                part = jnp.sum(part.reshape(-1, width), axis=0)
                tap_sum = tap_sum + onehot[dilation - 1] * part
            tap_sums.append(tap_sum)
        return pw_part, jnp.stack(tap_sums, axis=0)

    slots = recv_start.shape[0]
    chunk = min(slots, CHUNK)
    chunks = slots // chunk
    place = (sample_of, inner_row, first_col)
    if chunks == 1:
        windows = gather_windows(place)
        depth_flat, preact, grad_rows, loss_sum, grad_head = forward(
            windows, recv_tiles, row_weight
        )
    else:
        split = lambda v: v.reshape((chunks, chunk) + v.shape[1:])
        outs = lax.map(
            lambda xs: forward(gather_windows(xs[0]), xs[1], xs[2]),
            (tuple(split(v) for v in place), split(recv_tiles), split(row_weight)),
        )
        depth_flat, preact, grad_rows = (v.reshape((-1, width)) for v in outs[:3])
        loss_sum, grad_head = jnp.sum(outs[3]), jnp.sum(outs[4], axis=0)
    cell = (recv_start[:, None] + offsets[None, :]).reshape(-1)
    row_ids = jnp.arange(cell.shape[0], dtype=jnp.int32)
    if cell.shape[0] <= 512:
        same_cell = cell[:, None] == cell[None, :]
        grad_y = jnp.dot(
            same_cell.astype(jnp.float32),
            grad_rows,
            precision=lax.Precision.HIGHEST,
            preferred_element_type=jnp.float32,
        )
        repeated = jnp.any(same_cell & (row_ids[None, :] < row_ids[:, None]), axis=1)
    else:
        cells_here = micro_batch * band_rows * block_cols
        grid = jnp.zeros((cells_here, width), jnp.float32).at[cell].add(grad_rows)
        grad_y = grid[cell]
        owner = jnp.full((cells_here,), cell.shape[0], jnp.int32).at[cell].min(row_ids)
        repeated = owner[cell] != row_ids
    sigmoid_u = jax.nn.sigmoid(preact)
    grad_u = (grad_y * sigmoid_u * (1.0 + preact * (1.0 - sigmoid_u))).astype(jnp.bfloat16)
    grad_u = jnp.where(repeated[:, None], jnp.zeros_like(grad_u), grad_u)
    if chunks == 1:
        windows_again, grad_u = lax.optimization_barrier((windows, grad_u))
        grad_pw, grad_dw = backward(windows_again, depth_flat, grad_u)
    else:
        rows_split = lambda v: v.reshape((chunks, chunk * TILE) + v.shape[1:])
        outs = lax.map(
            lambda xs: backward(gather_windows(xs[0]), xs[1], xs[2]),
            (tuple(split(v) for v in place), rows_split(depth_flat), rows_split(grad_u)),
        )
        grad_pw, grad_dw = jnp.sum(outs[0], axis=0), jnp.sum(outs[1], axis=0)
    grad_dw, grad_pw, grad_head, loss_sum = packed_sum(
        (grad_dw, grad_pw, grad_head, loss_sum), ("lat", "lon")
    )
    return (grad_dw, grad_pw, grad_head, (loss_sum / teach_width).reshape(1))


def solution(mesh):
    in_specs = (
        P("groups", "lat", "lon", None),
        P(),
        P(),
        P(),
        P(),
        P(("groups", "lon", "lat"), None, None),
        P(("groups", "lon", "lat"), None),
        P(("groups", "lon", "lat")),
        P(("groups", "lon", "lat")),
    )
    out_specs = (P("groups", None), P("groups", None), P("groups", None), P("groups"))
    return jax.shard_map(local, mesh=mesh, in_specs=in_specs, out_specs=out_specs, check_vma=False)
```

```python
import jax
import jax.numpy as jnp
from jax import lax
from jax.sharding import PartitionSpec as P

DMAX = 4
TILE = 8
CAP = 2
CHUNK = 32


LANES = 128


def halve(x, axis, bit):
    count = lax.axis_size(axis)
    rows = x.shape[0] // 2
    upper = (lax.axis_index(axis) // bit) % 2
    keep = lax.dynamic_slice_in_dim(x, upper * rows, rows, 0)
    send = lax.dynamic_slice_in_dim(x, (1 - upper) * rows, rows, 0)
    return keep + lax.ppermute(send, axis, [(i, i ^ bit) for i in range(count)])


def double(x, axis, bit):
    count = lax.axis_size(axis)
    rows = x.shape[0]
    upper = (lax.axis_index(axis) // bit) % 2
    got = lax.ppermute(x, axis, [(i, i ^ bit) for i in range(count)])
    whole = jnp.zeros((2 * rows,) + x.shape[1:], x.dtype)
    whole = lax.dynamic_update_slice_in_dim(whole, x, upper * rows, 0)
    return lax.dynamic_update_slice_in_dim(whole, got, (1 - upper) * rows, 0)


def exchange_sum(x, axes):
    for axis in axes:
        count = lax.axis_size(axis)
        if count & (count - 1):
            x = lax.psum(x, axis)
            continue
        bit = 1
        while bit < count:
            x = x + lax.ppermute(x, axis, [(i, i ^ bit) for i in range(count)])
            bit *= 2
    return x


def packed_sum(values, axes):
    steps = []
    rest = []
    for axis in axes:
        count = lax.axis_size(axis)
        if count & (count - 1):
            rest.append(axis)
            continue
        bit = 1
        while bit < count:
            steps.append((axis, bit))
            bit *= 2
    flat = jnp.concatenate([jnp.ravel(v).astype(jnp.float32) for v in values])
    unit = 8 * LANES * (2 ** len(steps))
    total = -(-flat.shape[0] // unit) * unit
    x = jnp.pad(flat, (0, total - flat.shape[0])).reshape(-1, LANES)
    for axis, bit in steps:
        x = halve(x, axis, bit)
    if rest:
        x = lax.psum(x, tuple(rest))
    for axis, bit in reversed(steps):
        x = double(x, axis, bit)
    flat = x.reshape(-1)
    out = []
    offset = 0
    for v in values:
        out.append(flat[offset : offset + v.size].reshape(v.shape))
        offset += v.size
    return tuple(out)


def padded_2(cells, sides, width, closed):
    for axis, dim in sides:
        count = lax.axis_size(axis)
        ends = count if closed else count - 1
        head = lax.slice_in_dim(cells, 0, width, axis=dim)
        tail = lax.slice_in_dim(cells, cells.shape[dim] - width, cells.shape[dim], axis=dim)
        cells = jnp.concatenate(
            [
                lax.ppermute(tail, axis, [(i, (i + 1) % count) for i in range(ends)]),
                cells,
                lax.ppermute(head, axis, [((i + 1) % count, i) for i in range(ends)]),
            ],
            axis=dim,
        )
    return cells


def local(
    acts, rates, dw_kernel, pw_weight, head_weight, teacher_tiles, tile_dest, tile_start, tile_count
):
    micro_batch, band_rows, block_cols, width = acts.shape
    teach_width = head_weight.shape[1]
    lat_index = lax.axis_index("lat")
    lat_count = lax.axis_size("lat")
    lon_count = lax.axis_size("lon")
    devices = lon_count * lat_count
    lon_padded = padded_2(acts, (("lon", 2),), DMAX, True)
    padded = padded_2(lon_padded, (("lat", 1),), DMAX, False)
    tiles_here = teacher_tiles.shape[0]
    destination = tile_dest[:, 0]
    positions = jnp.arange(tiles_here, dtype=jnp.int32)
    same_dest = destination[:, None] == destination[None, :]
    earlier = positions[:, None] > positions[None, :]
    slot_rank = jnp.sum((same_dest & earlier).astype(jnp.int32), axis=1)
    slot_index = destination * CAP + slot_rank
    slots = devices * CAP
    base = 64
    column = jnp.zeros((tiles_here, TILE, 1), jnp.float32)
    column = column.at[:, 0, 0].set((tile_start // base).astype(jnp.float32))
    column = column.at[:, 1, 0].set((tile_start % base).astype(jnp.float32))
    column = column.at[:, 2, 0].set(tile_count.astype(jnp.float32))
    packed = jnp.concatenate([teacher_tiles, column.astype(jnp.bfloat16)], axis=2)
    chooser = (slot_index[None, :] == jnp.arange(slots, dtype=jnp.int32)[:, None]).astype(
        jnp.bfloat16
    )
    send = jnp.dot(
        chooser, packed.reshape(tiles_here, -1), preferred_element_type=jnp.float32
    ).astype(jnp.bfloat16)
    recv = lax.all_to_all(
        send.reshape(slots, TILE, teach_width + 1),
        ("lon", "lat"),
        split_axis=0,
        concat_axis=0,
        tiled=True,
    )
    recv_tiles = recv[:, :, :teach_width]
    meta = recv[:, :3, teach_width].astype(jnp.int32)
    recv_start = meta[:, 0] * base + meta[:, 1]
    recv_count = meta[:, 2]
    offsets = jnp.arange(TILE, dtype=jnp.int32)
    is_valid = offsets[None, :] < recv_count[:, None]
    sample_of = recv_start // (block_cols * band_rows)
    inner_row = recv_start // block_cols % band_rows
    first_col = recv_start % block_cols
    glob_row = lat_index * band_rows + inner_row
    area_weight = jnp.cos(
        jnp.pi * ((glob_row.astype(jnp.float32) + 0.5) / (band_rows * lat_count) - 0.5)
    )
    row_weight = jnp.where(is_valid, area_weight[:, None], jnp.float32(0.0)) / jnp.float32(
        devices * tiles_here * TILE
    )
    kernel = dw_kernel.astype(jnp.float32)
    onehot = (
        rates[None, :] == jnp.arange(1, DMAX + 1, dtype=jnp.int32)[:, None]
    ).astype(jnp.float32)
    span = 2 * DMAX + 1
    reach = TILE + 2 * DMAX

    def gather_windows(place):
        b, h, w = place
        return jax.vmap(
            lambda b, h, w: lax.dynamic_slice(
                padded, (b, h, w, jnp.int32(0)), (1, span, reach, width)
            )[0]
        )(b, h, w)

    def shifted(source, row_shift, col_shift):
        return source[:, DMAX + row_shift, DMAX + col_shift : DMAX + col_shift + TILE, :].astype(
            jnp.float32
        )

    def forward(windows, tiles, weight):
        center = shifted(windows, 0, 0)
        accum_sum = center * kernel[4]
        for dilation in range(1, DMAX + 1):
            for tap_index in range(9):
                if tap_index == 4:
                    continue
                row_shift = (tap_index // 3 - 1) * dilation
                col_shift = (tap_index % 3 - 1) * dilation
                accum_sum = accum_sum + kernel[tap_index] * onehot[dilation - 1] * shifted(
                    windows, row_shift, col_shift
                )
        depth_flat = accum_sum.astype(jnp.bfloat16).reshape(-1, width)
        preact = jnp.dot(depth_flat, pw_weight, preferred_element_type=jnp.float32)
        y_rows = (center.reshape(-1, width) + jax.nn.silu(preact)).astype(jnp.bfloat16)
        weight = weight.reshape(-1, 1)
        predicted = jnp.dot(y_rows, head_weight, preferred_element_type=jnp.float32)
        residual = predicted - tiles.reshape(-1, teach_width).astype(jnp.float32)
        loss_part = jnp.sum(weight * residual * residual)
        grad_pred = (2.0 * weight * residual).astype(jnp.bfloat16)
        head_part = lax.dot_general(
            y_rows, grad_pred, (((0,), (0,)), ((), ())), preferred_element_type=jnp.float32
        )
        grad_rows = jnp.dot(grad_pred, head_weight.T, preferred_element_type=jnp.float32)
        return depth_flat, preact, grad_rows, loss_part, head_part

    def backward(windows, depth_flat, grad_u):
        pw_part = lax.dot_general(
            depth_flat, grad_u, (((0,), (0,)), ((), ())), preferred_element_type=jnp.float32
        )
        grad_z = jnp.dot(grad_u, pw_weight.T, preferred_element_type=jnp.float32)
        grad_z = grad_z.reshape(windows.shape[0], TILE, width)
        tap_sums = []
        for tap_index in range(9):
            if tap_index == 4:
                part = shifted(windows, 0, 0) * grad_z
                tap_sums.append(jnp.sum(part.reshape(-1, width), axis=0))
                continue
            tap_sum = jnp.zeros((width,), jnp.float32)
            for dilation in range(1, DMAX + 1):
                row_shift = (tap_index // 3 - 1) * dilation
                col_shift = (tap_index % 3 - 1) * dilation
                part = shifted(windows, row_shift, col_shift) * grad_z
                part = jnp.sum(part.reshape(-1, width), axis=0)
                tap_sum = tap_sum + onehot[dilation - 1] * part
            tap_sums.append(tap_sum)
        return pw_part, jnp.stack(tap_sums, axis=0)

    slots = recv_start.shape[0]
    chunk = min(slots, CHUNK)
    chunks = slots // chunk
    place = (sample_of, inner_row, first_col)
    if chunks == 1:
        windows = gather_windows(place)
        depth_flat, preact, grad_rows, loss_sum, grad_head = forward(
            windows, recv_tiles, row_weight
        )
    else:
        split = lambda v: v.reshape((chunks, chunk) + v.shape[1:])
        outs = lax.map(
            lambda xs: forward(gather_windows(xs[0]), xs[1], xs[2]),
            (tuple(split(v) for v in place), split(recv_tiles), split(row_weight)),
        )
        depth_flat, preact, grad_rows = (v.reshape((-1, width)) for v in outs[:3])
        loss_sum, grad_head = jnp.sum(outs[3]), jnp.sum(outs[4], axis=0)
    cell = (recv_start[:, None] + offsets[None, :]).reshape(-1)
    row_ids = jnp.arange(cell.shape[0], dtype=jnp.int32)
    if cell.shape[0] <= 512:
        same_cell = cell[:, None] == cell[None, :]
        grad_y = jnp.dot(
            same_cell.astype(jnp.float32),
            grad_rows,
            precision=lax.Precision.HIGHEST,
            preferred_element_type=jnp.float32,
        )
        repeated = jnp.any(same_cell & (row_ids[None, :] < row_ids[:, None]), axis=1)
    else:
        cells_here = micro_batch * band_rows * block_cols
        grid = jnp.zeros((cells_here, width), jnp.float32).at[cell].add(grad_rows)
        grad_y = grid[cell]
        owner = jnp.full((cells_here,), cell.shape[0], jnp.int32).at[cell].min(row_ids)
        repeated = owner[cell] != row_ids
    sigmoid_u = jax.nn.sigmoid(preact)
    grad_u = (grad_y * sigmoid_u * (1.0 + preact * (1.0 - sigmoid_u))).astype(jnp.bfloat16)
    grad_u = jnp.where(repeated[:, None], jnp.zeros_like(grad_u), grad_u)
    if chunks == 1:
        windows_again, grad_u = lax.optimization_barrier((windows, grad_u))
        grad_pw, grad_dw = backward(windows_again, depth_flat, grad_u)
    else:
        rows_split = lambda v: v.reshape((chunks, chunk * TILE) + v.shape[1:])
        outs = lax.map(
            lambda xs: backward(gather_windows(xs[0]), xs[1], xs[2]),
            (tuple(split(v) for v in place), rows_split(depth_flat), rows_split(grad_u)),
        )
        grad_pw, grad_dw = jnp.sum(outs[0], axis=0), jnp.sum(outs[1], axis=0)
    grad_pw, grad_head, loss_sum = packed_sum((grad_pw, grad_head, loss_sum), ("lat", "lon"))
    grad_dw = exchange_sum(grad_dw, ("lat", "lon"))
    return (grad_dw, grad_pw, grad_head, (loss_sum / teach_width).reshape(1))


def solution(mesh):
    in_specs = (
        P("groups", "lat", "lon", None),
        P(),
        P(),
        P(),
        P(),
        P(("groups", "lon", "lat"), None, None),
        P(("groups", "lon", "lat"), None),
        P(("groups", "lon", "lat")),
        P(("groups", "lon", "lat")),
    )
    out_specs = (P("groups", None), P("groups", None), P("groups", None), P("groups"))
    return jax.shard_map(local, mesh=mesh, in_specs=in_specs, out_specs=out_specs, check_vma=False)
```

```python
import jax
import jax.numpy as jnp
from jax import lax
from jax.sharding import PartitionSpec as P

DMAX = 4
TILE = 8
CAP = 2
CHUNK = 32


LANES = 128


def halve(x, axis, bit):
    count = lax.axis_size(axis)
    rows = x.shape[0] // 2
    upper = (lax.axis_index(axis) // bit) % 2
    keep = lax.dynamic_slice_in_dim(x, upper * rows, rows, 0)
    send = lax.dynamic_slice_in_dim(x, (1 - upper) * rows, rows, 0)
    return keep + lax.ppermute(send, axis, [(i, i ^ bit) for i in range(count)])


def double(x, axis, bit):
    count = lax.axis_size(axis)
    rows = x.shape[0]
    upper = (lax.axis_index(axis) // bit) % 2
    got = lax.ppermute(x, axis, [(i, i ^ bit) for i in range(count)])
    whole = jnp.zeros((2 * rows,) + x.shape[1:], x.dtype)
    whole = lax.dynamic_update_slice_in_dim(whole, x, upper * rows, 0)
    return lax.dynamic_update_slice_in_dim(whole, got, (1 - upper) * rows, 0)


def as_rows(values, unit):
    flat = jnp.concatenate([jnp.ravel(v).astype(jnp.float32) for v in values])
    total = -(-flat.shape[0] // unit) * unit
    return jnp.pad(flat, (0, total - flat.shape[0])).reshape(-1, LANES)


def from_rows(x, values):
    flat = x.reshape(-1)
    out = []
    offset = 0
    for v in values:
        out.append(flat[offset : offset + v.size].reshape(v.shape))
        offset += v.size
    return tuple(out)


def packed_sum(values, axes, late):
    steps = []
    rest = []
    for axis in axes:
        count = lax.axis_size(axis)
        if count & (count - 1):
            rest.append(axis)
            continue
        bit = 1
        while bit < count:
            steps.append((axis, bit))
            bit *= 2
    x = as_rows(values, 8 * LANES * (2 ** len(steps)))
    for axis, bit in steps:
        x = halve(x, axis, bit)
    extra = as_rows((late,), 8 * LANES)
    if rest:
        x, extra = lax.psum((x, extra), tuple(rest))
    for axis, bit in reversed(steps):
        count = lax.axis_size(axis)
        rows = x.shape[0]
        upper = (lax.axis_index(axis) // bit) % 2
        got = lax.ppermute(
            jnp.concatenate([x, extra]), axis, [(i, i ^ bit) for i in range(count)]
        )
        extra = extra + got[rows:]
        whole = jnp.zeros((2 * rows,) + x.shape[1:], x.dtype)
        whole = lax.dynamic_update_slice_in_dim(whole, x, upper * rows, 0)
        x = lax.dynamic_update_slice_in_dim(whole, got[:rows], (1 - upper) * rows, 0)
    return from_rows(x, values), from_rows(extra, (late,))[0]


def padded_2(cells, sides, width, closed):
    for axis, dim in sides:
        count = lax.axis_size(axis)
        ends = count if closed else count - 1
        head = lax.slice_in_dim(cells, 0, width, axis=dim)
        tail = lax.slice_in_dim(cells, cells.shape[dim] - width, cells.shape[dim], axis=dim)
        cells = jnp.concatenate(
            [
                lax.ppermute(tail, axis, [(i, (i + 1) % count) for i in range(ends)]),
                cells,
                lax.ppermute(head, axis, [((i + 1) % count, i) for i in range(ends)]),
            ],
            axis=dim,
        )
    return cells


def local(
    acts, rates, dw_kernel, pw_weight, head_weight, teacher_tiles, tile_dest, tile_start, tile_count
):
    micro_batch, band_rows, block_cols, width = acts.shape
    teach_width = head_weight.shape[1]
    lat_index = lax.axis_index("lat")
    lat_count = lax.axis_size("lat")
    lon_count = lax.axis_size("lon")
    devices = lon_count * lat_count
    lon_padded = padded_2(acts, (("lon", 2),), DMAX, True)
    padded = padded_2(lon_padded, (("lat", 1),), DMAX, False)
    tiles_here = teacher_tiles.shape[0]
    destination = tile_dest[:, 0]
    positions = jnp.arange(tiles_here, dtype=jnp.int32)
    same_dest = destination[:, None] == destination[None, :]
    earlier = positions[:, None] > positions[None, :]
    slot_rank = jnp.sum((same_dest & earlier).astype(jnp.int32), axis=1)
    slot_index = destination * CAP + slot_rank
    slots = devices * CAP
    base = 64
    column = jnp.zeros((tiles_here, TILE, 1), jnp.float32)
    column = column.at[:, 0, 0].set((tile_start // base).astype(jnp.float32))
    column = column.at[:, 1, 0].set((tile_start % base).astype(jnp.float32))
    column = column.at[:, 2, 0].set(tile_count.astype(jnp.float32))
    packed = jnp.concatenate([teacher_tiles, column.astype(jnp.bfloat16)], axis=2)
    chooser = (slot_index[None, :] == jnp.arange(slots, dtype=jnp.int32)[:, None]).astype(
        jnp.bfloat16
    )
    send = jnp.dot(
        chooser, packed.reshape(tiles_here, -1), preferred_element_type=jnp.float32
    ).astype(jnp.bfloat16)
    recv = lax.all_to_all(
        send.reshape(slots, TILE, teach_width + 1),
        ("lon", "lat"),
        split_axis=0,
        concat_axis=0,
        tiled=True,
    )
    recv_tiles = recv[:, :, :teach_width]
    meta = recv[:, :3, teach_width].astype(jnp.int32)
    recv_start = meta[:, 0] * base + meta[:, 1]
    recv_count = meta[:, 2]
    offsets = jnp.arange(TILE, dtype=jnp.int32)
    is_valid = offsets[None, :] < recv_count[:, None]
    sample_of = recv_start // (block_cols * band_rows)
    inner_row = recv_start // block_cols % band_rows
    first_col = recv_start % block_cols
    glob_row = lat_index * band_rows + inner_row
    area_weight = jnp.cos(
        jnp.pi * ((glob_row.astype(jnp.float32) + 0.5) / (band_rows * lat_count) - 0.5)
    )
    row_weight = jnp.where(is_valid, area_weight[:, None], jnp.float32(0.0)) / jnp.float32(
        devices * tiles_here * TILE
    )
    kernel = dw_kernel.astype(jnp.float32)
    onehot = (
        rates[None, :] == jnp.arange(1, DMAX + 1, dtype=jnp.int32)[:, None]
    ).astype(jnp.float32)
    span = 2 * DMAX + 1
    reach = TILE + 2 * DMAX

    def gather_windows(place):
        b, h, w = place
        return jax.vmap(
            lambda b, h, w: lax.dynamic_slice(
                padded, (b, h, w, jnp.int32(0)), (1, span, reach, width)
            )[0]
        )(b, h, w)

    def shifted(source, row_shift, col_shift):
        return source[:, DMAX + row_shift, DMAX + col_shift : DMAX + col_shift + TILE, :].astype(
            jnp.float32
        )

    def forward(windows, tiles, weight):
        center = shifted(windows, 0, 0)
        accum_sum = center * kernel[4]
        for dilation in range(1, DMAX + 1):
            for tap_index in range(9):
                if tap_index == 4:
                    continue
                row_shift = (tap_index // 3 - 1) * dilation
                col_shift = (tap_index % 3 - 1) * dilation
                accum_sum = accum_sum + kernel[tap_index] * onehot[dilation - 1] * shifted(
                    windows, row_shift, col_shift
                )
        depth_flat = accum_sum.astype(jnp.bfloat16).reshape(-1, width)
        preact = jnp.dot(depth_flat, pw_weight, preferred_element_type=jnp.float32)
        y_rows = (center.reshape(-1, width) + jax.nn.silu(preact)).astype(jnp.bfloat16)
        weight = weight.reshape(-1, 1)
        predicted = jnp.dot(y_rows, head_weight, preferred_element_type=jnp.float32)
        residual = predicted - tiles.reshape(-1, teach_width).astype(jnp.float32)
        loss_part = jnp.sum(weight * residual * residual)
        grad_pred = (2.0 * weight * residual).astype(jnp.bfloat16)
        head_part = lax.dot_general(
            y_rows, grad_pred, (((0,), (0,)), ((), ())), preferred_element_type=jnp.float32
        )
        grad_rows = jnp.dot(grad_pred, head_weight.T, preferred_element_type=jnp.float32)
        return depth_flat, preact, grad_rows, loss_part, head_part

    def backward(windows, depth_flat, grad_u):
        pw_part = lax.dot_general(
            depth_flat, grad_u, (((0,), (0,)), ((), ())), preferred_element_type=jnp.float32
        )
        grad_z = jnp.dot(grad_u, pw_weight.T, preferred_element_type=jnp.float32)
        grad_z = grad_z.reshape(windows.shape[0], TILE, width)
        tap_sums = []
        for tap_index in range(9):
            if tap_index == 4:
                part = shifted(windows, 0, 0) * grad_z
                tap_sums.append(jnp.sum(part.reshape(-1, width), axis=0))
                continue
            tap_sum = jnp.zeros((width,), jnp.float32)
            for dilation in range(1, DMAX + 1):
                row_shift = (tap_index // 3 - 1) * dilation
                col_shift = (tap_index % 3 - 1) * dilation
                part = shifted(windows, row_shift, col_shift) * grad_z
                part = jnp.sum(part.reshape(-1, width), axis=0)
                tap_sum = tap_sum + onehot[dilation - 1] * part
            tap_sums.append(tap_sum)
        return pw_part, jnp.stack(tap_sums, axis=0)

    slots = recv_start.shape[0]
    chunk = min(slots, CHUNK)
    chunks = slots // chunk
    place = (sample_of, inner_row, first_col)
    if chunks == 1:
        windows = gather_windows(place)
        depth_flat, preact, grad_rows, loss_sum, grad_head = forward(
            windows, recv_tiles, row_weight
        )
    else:
        split = lambda v: v.reshape((chunks, chunk) + v.shape[1:])
        outs = lax.map(
            lambda xs: forward(gather_windows(xs[0]), xs[1], xs[2]),
            (tuple(split(v) for v in place), split(recv_tiles), split(row_weight)),
        )
        depth_flat, preact, grad_rows = (v.reshape((-1, width)) for v in outs[:3])
        loss_sum, grad_head = jnp.sum(outs[3]), jnp.sum(outs[4], axis=0)
    cell = (recv_start[:, None] + offsets[None, :]).reshape(-1)
    row_ids = jnp.arange(cell.shape[0], dtype=jnp.int32)
    if cell.shape[0] <= 512:
        same_cell = cell[:, None] == cell[None, :]
        grad_y = jnp.dot(
            same_cell.astype(jnp.float32),
            grad_rows,
            precision=lax.Precision.HIGHEST,
            preferred_element_type=jnp.float32,
        )
        repeated = jnp.any(same_cell & (row_ids[None, :] < row_ids[:, None]), axis=1)
    else:
        cells_here = micro_batch * band_rows * block_cols
        grid = jnp.zeros((cells_here, width), jnp.float32).at[cell].add(grad_rows)
        grad_y = grid[cell]
        owner = jnp.full((cells_here,), cell.shape[0], jnp.int32).at[cell].min(row_ids)
        repeated = owner[cell] != row_ids
    sigmoid_u = jax.nn.sigmoid(preact)
    grad_u = (grad_y * sigmoid_u * (1.0 + preact * (1.0 - sigmoid_u))).astype(jnp.bfloat16)
    grad_u = jnp.where(repeated[:, None], jnp.zeros_like(grad_u), grad_u)
    if chunks == 1:
        windows_again, grad_u = lax.optimization_barrier((windows, grad_u))
        grad_pw, grad_dw = backward(windows_again, depth_flat, grad_u)
    else:
        rows_split = lambda v: v.reshape((chunks, chunk * TILE) + v.shape[1:])
        outs = lax.map(
            lambda xs: backward(gather_windows(xs[0]), xs[1], xs[2]),
            (tuple(split(v) for v in place), rows_split(depth_flat), rows_split(grad_u)),
        )
        grad_pw, grad_dw = jnp.sum(outs[0], axis=0), jnp.sum(outs[1], axis=0)
    (grad_pw, grad_head, loss_sum), grad_dw = packed_sum(
        (grad_pw, grad_head, loss_sum), ("lat", "lon"), grad_dw
    )
    return (grad_dw, grad_pw, grad_head, (loss_sum / teach_width).reshape(1))


def solution(mesh):
    in_specs = (
        P("groups", "lat", "lon", None),
        P(),
        P(),
        P(),
        P(),
        P(("groups", "lon", "lat"), None, None),
        P(("groups", "lon", "lat"), None),
        P(("groups", "lon", "lat")),
        P(("groups", "lon", "lat")),
    )
    out_specs = (P("groups", None), P("groups", None), P("groups", None), P("groups"))
    return jax.shard_map(local, mesh=mesh, in_specs=in_specs, out_specs=out_specs, check_vma=False)
```

```python
import jax
import jax.numpy as jnp
from jax import lax
from jax.sharding import PartitionSpec as P

DMAX = 4
TILE = 8
CAP = 2
CHUNK = 32


LANES = 128


def halve(x, axis, bit):
    count = lax.axis_size(axis)
    rows = x.shape[0] // 2
    upper = (lax.axis_index(axis) // bit) % 2
    keep = lax.dynamic_slice_in_dim(x, upper * rows, rows, 0)
    send = lax.dynamic_slice_in_dim(x, (1 - upper) * rows, rows, 0)
    return keep + lax.ppermute(send, axis, [(i, i ^ bit) for i in range(count)])


def double(x, axis, bit):
    count = lax.axis_size(axis)
    rows = x.shape[0]
    upper = (lax.axis_index(axis) // bit) % 2
    got = lax.ppermute(x, axis, [(i, i ^ bit) for i in range(count)])
    whole = jnp.zeros((2 * rows,) + x.shape[1:], x.dtype)
    whole = lax.dynamic_update_slice_in_dim(whole, x, upper * rows, 0)
    return lax.dynamic_update_slice_in_dim(whole, got, (1 - upper) * rows, 0)


def packed_sum(values, axes):
    steps = []
    rest = []
    for axis in axes:
        count = lax.axis_size(axis)
        if count & (count - 1):
            rest.append(axis)
            continue
        bit = 1
        while bit < count:
            steps.append((axis, bit))
            bit *= 2
    flat = jnp.concatenate([jnp.ravel(v).astype(jnp.float32) for v in values])
    unit = 8 * LANES * (2 ** len(steps))
    total = -(-flat.shape[0] // unit) * unit
    x = jnp.pad(flat, (0, total - flat.shape[0])).reshape(-1, LANES)
    for axis, bit in steps:
        x = halve(x, axis, bit)
    if rest:
        x = lax.psum(x, tuple(rest))
    for axis, bit in reversed(steps):
        x = double(x, axis, bit)
    flat = x.reshape(-1)
    out = []
    offset = 0
    for v in values:
        out.append(flat[offset : offset + v.size].reshape(v.shape))
        offset += v.size
    return tuple(out)


def halo_padded(cells, width):
    lon_count = lax.axis_size("lon")
    lat_count = lax.axis_size("lat")
    both = ("lon", "lat")

    def flat(lon, lat):
        return lon * lat_count + lat

    def send(piece, lon_step, lat_step):
        pairs = []
        for lon in range(lon_count):
            for lat in range(lat_count):
                to_lat = lat + lat_step
                if 0 <= to_lat < lat_count:
                    pairs.append((flat(lon, lat), flat((lon + lon_step) % lon_count, to_lat)))
        return lax.ppermute(piece, both, pairs)

    rows, cols = cells.shape[1], cells.shape[2]
    top = lambda v: v[:, :width]
    bottom = lambda v: v[:, rows - width :]
    left = lambda v: v[:, :, :width]
    right = lambda v: v[:, :, cols - width :]
    west = send(right(cells), 1, 0)
    east = send(left(cells), -1, 0)
    north = send(bottom(cells), 0, 1)
    south = send(top(cells), 0, -1)
    north_west = send(right(bottom(cells)), 1, 1)
    north_east = send(left(bottom(cells)), -1, 1)
    south_west = send(right(top(cells)), 1, -1)
    south_east = send(left(top(cells)), -1, -1)
    upper = jnp.concatenate([north_west, north, north_east], axis=2)
    middle = jnp.concatenate([west, cells, east], axis=2)
    lower = jnp.concatenate([south_west, south, south_east], axis=2)
    return jnp.concatenate([upper, middle, lower], axis=1)


def padded_2(cells, sides, width, closed):
    for axis, dim in sides:
        count = lax.axis_size(axis)
        ends = count if closed else count - 1
        head = lax.slice_in_dim(cells, 0, width, axis=dim)
        tail = lax.slice_in_dim(cells, cells.shape[dim] - width, cells.shape[dim], axis=dim)
        cells = jnp.concatenate(
            [
                lax.ppermute(tail, axis, [(i, (i + 1) % count) for i in range(ends)]),
                cells,
                lax.ppermute(head, axis, [((i + 1) % count, i) for i in range(ends)]),
            ],
            axis=dim,
        )
    return cells


def local(
    acts, rates, dw_kernel, pw_weight, head_weight, teacher_tiles, tile_dest, tile_start, tile_count
):
    micro_batch, band_rows, block_cols, width = acts.shape
    teach_width = head_weight.shape[1]
    lat_index = lax.axis_index("lat")
    lat_count = lax.axis_size("lat")
    lon_count = lax.axis_size("lon")
    devices = lon_count * lat_count
    padded = halo_padded(acts, DMAX)
    tiles_here = teacher_tiles.shape[0]
    destination = tile_dest[:, 0]
    positions = jnp.arange(tiles_here, dtype=jnp.int32)
    same_dest = destination[:, None] == destination[None, :]
    earlier = positions[:, None] > positions[None, :]
    slot_rank = jnp.sum((same_dest & earlier).astype(jnp.int32), axis=1)
    slot_index = destination * CAP + slot_rank
    slots = devices * CAP
    base = 64
    column = jnp.zeros((tiles_here, TILE, 1), jnp.float32)
    column = column.at[:, 0, 0].set((tile_start // base).astype(jnp.float32))
    column = column.at[:, 1, 0].set((tile_start % base).astype(jnp.float32))
    column = column.at[:, 2, 0].set(tile_count.astype(jnp.float32))
    packed = jnp.concatenate([teacher_tiles, column.astype(jnp.bfloat16)], axis=2)
    chooser = (slot_index[None, :] == jnp.arange(slots, dtype=jnp.int32)[:, None]).astype(
        jnp.bfloat16
    )
    send = jnp.dot(
        chooser, packed.reshape(tiles_here, -1), preferred_element_type=jnp.float32
    ).astype(jnp.bfloat16)
    recv = lax.all_to_all(
        send.reshape(slots, TILE, teach_width + 1),
        ("lon", "lat"),
        split_axis=0,
        concat_axis=0,
        tiled=True,
    )
    recv_tiles = recv[:, :, :teach_width]
    meta = recv[:, :3, teach_width].astype(jnp.int32)
    recv_start = meta[:, 0] * base + meta[:, 1]
    recv_count = meta[:, 2]
    offsets = jnp.arange(TILE, dtype=jnp.int32)
    is_valid = offsets[None, :] < recv_count[:, None]
    sample_of = recv_start // (block_cols * band_rows)
    inner_row = recv_start // block_cols % band_rows
    first_col = recv_start % block_cols
    glob_row = lat_index * band_rows + inner_row
    area_weight = jnp.cos(
        jnp.pi * ((glob_row.astype(jnp.float32) + 0.5) / (band_rows * lat_count) - 0.5)
    )
    row_weight = jnp.where(is_valid, area_weight[:, None], jnp.float32(0.0)) / jnp.float32(
        devices * tiles_here * TILE
    )
    kernel = dw_kernel.astype(jnp.float32)
    onehot = (
        rates[None, :] == jnp.arange(1, DMAX + 1, dtype=jnp.int32)[:, None]
    ).astype(jnp.float32)
    span = 2 * DMAX + 1
    reach = TILE + 2 * DMAX

    def gather_windows(place):
        b, h, w = place
        return jax.vmap(
            lambda b, h, w: lax.dynamic_slice(
                padded, (b, h, w, jnp.int32(0)), (1, span, reach, width)
            )[0]
        )(b, h, w)

    def shifted(source, row_shift, col_shift):
        return source[:, DMAX + row_shift, DMAX + col_shift : DMAX + col_shift + TILE, :].astype(
            jnp.float32
        )

    def forward(windows, tiles, weight):
        center = shifted(windows, 0, 0)
        accum_sum = center * kernel[4]
        for dilation in range(1, DMAX + 1):
            for tap_index in range(9):
                if tap_index == 4:
                    continue
                row_shift = (tap_index // 3 - 1) * dilation
                col_shift = (tap_index % 3 - 1) * dilation
                accum_sum = accum_sum + kernel[tap_index] * onehot[dilation - 1] * shifted(
                    windows, row_shift, col_shift
                )
        depth_flat = accum_sum.astype(jnp.bfloat16).reshape(-1, width)
        preact = jnp.dot(depth_flat, pw_weight, preferred_element_type=jnp.float32)
        y_rows = (center.reshape(-1, width) + jax.nn.silu(preact)).astype(jnp.bfloat16)
        weight = weight.reshape(-1, 1)
        predicted = jnp.dot(y_rows, head_weight, preferred_element_type=jnp.float32)
        residual = predicted - tiles.reshape(-1, teach_width).astype(jnp.float32)
        loss_part = jnp.sum(weight * residual * residual)
        grad_pred = (2.0 * weight * residual).astype(jnp.bfloat16)
        head_part = lax.dot_general(
            y_rows, grad_pred, (((0,), (0,)), ((), ())), preferred_element_type=jnp.float32
        )
        grad_rows = jnp.dot(grad_pred, head_weight.T, preferred_element_type=jnp.float32)
        return depth_flat, preact, grad_rows, loss_part, head_part

    def backward(windows, depth_flat, grad_u):
        pw_part = lax.dot_general(
            depth_flat, grad_u, (((0,), (0,)), ((), ())), preferred_element_type=jnp.float32
        )
        grad_z = jnp.dot(grad_u, pw_weight.T, preferred_element_type=jnp.float32)
        grad_z = grad_z.reshape(windows.shape[0], TILE, width)
        tap_sums = []
        for tap_index in range(9):
            if tap_index == 4:
                part = shifted(windows, 0, 0) * grad_z
                tap_sums.append(jnp.sum(part.reshape(-1, width), axis=0))
                continue
            tap_sum = jnp.zeros((width,), jnp.float32)
            for dilation in range(1, DMAX + 1):
                row_shift = (tap_index // 3 - 1) * dilation
                col_shift = (tap_index % 3 - 1) * dilation
                part = shifted(windows, row_shift, col_shift) * grad_z
                part = jnp.sum(part.reshape(-1, width), axis=0)
                tap_sum = tap_sum + onehot[dilation - 1] * part
            tap_sums.append(tap_sum)
        return pw_part, jnp.stack(tap_sums, axis=0)

    slots = recv_start.shape[0]
    chunk = min(slots, CHUNK)
    chunks = slots // chunk
    place = (sample_of, inner_row, first_col)
    if chunks == 1:
        windows = gather_windows(place)
        depth_flat, preact, grad_rows, loss_sum, grad_head = forward(
            windows, recv_tiles, row_weight
        )
    else:
        split = lambda v: v.reshape((chunks, chunk) + v.shape[1:])
        outs = lax.map(
            lambda xs: forward(gather_windows(xs[0]), xs[1], xs[2]),
            (tuple(split(v) for v in place), split(recv_tiles), split(row_weight)),
        )
        depth_flat, preact, grad_rows = (v.reshape((-1, width)) for v in outs[:3])
        loss_sum, grad_head = jnp.sum(outs[3]), jnp.sum(outs[4], axis=0)
    cell = (recv_start[:, None] + offsets[None, :]).reshape(-1)
    row_ids = jnp.arange(cell.shape[0], dtype=jnp.int32)
    if cell.shape[0] <= 512:
        same_cell = cell[:, None] == cell[None, :]
        grad_y = jnp.dot(
            same_cell.astype(jnp.float32),
            grad_rows,
            precision=lax.Precision.HIGHEST,
            preferred_element_type=jnp.float32,
        )
        repeated = jnp.any(same_cell & (row_ids[None, :] < row_ids[:, None]), axis=1)
    else:
        cells_here = micro_batch * band_rows * block_cols
        grid = jnp.zeros((cells_here, width), jnp.float32).at[cell].add(grad_rows)
        grad_y = grid[cell]
        owner = jnp.full((cells_here,), cell.shape[0], jnp.int32).at[cell].min(row_ids)
        repeated = owner[cell] != row_ids
    sigmoid_u = jax.nn.sigmoid(preact)
    grad_u = (grad_y * sigmoid_u * (1.0 + preact * (1.0 - sigmoid_u))).astype(jnp.bfloat16)
    grad_u = jnp.where(repeated[:, None], jnp.zeros_like(grad_u), grad_u)
    if chunks == 1:
        windows_again, grad_u = lax.optimization_barrier((windows, grad_u))
        grad_pw, grad_dw = backward(windows_again, depth_flat, grad_u)
    else:
        rows_split = lambda v: v.reshape((chunks, chunk * TILE) + v.shape[1:])
        outs = lax.map(
            lambda xs: backward(gather_windows(xs[0]), xs[1], xs[2]),
            (tuple(split(v) for v in place), rows_split(depth_flat), rows_split(grad_u)),
        )
        grad_pw, grad_dw = jnp.sum(outs[0], axis=0), jnp.sum(outs[1], axis=0)
    grad_dw, grad_pw, grad_head, loss_sum = packed_sum(
        (grad_dw, grad_pw, grad_head, loss_sum), ("lat", "lon")
    )
    return (grad_dw, grad_pw, grad_head, (loss_sum / teach_width).reshape(1))


def solution(mesh):
    in_specs = (
        P("groups", "lat", "lon", None),
        P(),
        P(),
        P(),
        P(),
        P(("groups", "lon", "lat"), None, None),
        P(("groups", "lon", "lat"), None),
        P(("groups", "lon", "lat")),
        P(("groups", "lon", "lat")),
    )
    out_specs = (P("groups", None), P("groups", None), P("groups", None), P("groups"))
    return jax.shard_map(local, mesh=mesh, in_specs=in_specs, out_specs=out_specs, check_vma=False)
```

```python
import jax
import jax.numpy as jnp
from jax import lax
from jax.sharding import PartitionSpec as P

DMAX = 4
TILE = 8
CAP = 2
CHUNK = 32


LANES = 128


def halve(x, axis, bit):
    count = lax.axis_size(axis)
    rows = x.shape[0] // 2
    upper = (lax.axis_index(axis) // bit) % 2
    keep = lax.dynamic_slice_in_dim(x, upper * rows, rows, 0)
    send = lax.dynamic_slice_in_dim(x, (1 - upper) * rows, rows, 0)
    return keep + lax.ppermute(send, axis, [(i, i ^ bit) for i in range(count)])


def double(x, axis, bit):
    count = lax.axis_size(axis)
    rows = x.shape[0]
    upper = (lax.axis_index(axis) // bit) % 2
    got = lax.ppermute(x, axis, [(i, i ^ bit) for i in range(count)])
    whole = jnp.zeros((2 * rows,) + x.shape[1:], x.dtype)
    whole = lax.dynamic_update_slice_in_dim(whole, x, upper * rows, 0)
    return lax.dynamic_update_slice_in_dim(whole, got, (1 - upper) * rows, 0)


def packed_sum(values, axes):
    steps = []
    rest = []
    for axis in axes:
        count = lax.axis_size(axis)
        if count & (count - 1):
            rest.append(axis)
            continue
        bit = 1
        while bit < count:
            steps.append((axis, bit))
            bit *= 2
    flat = jnp.concatenate([jnp.ravel(v).astype(jnp.float32) for v in values])
    unit = 8 * LANES * (2 ** len(steps))
    total = -(-flat.shape[0] // unit) * unit
    x = jnp.pad(flat, (0, total - flat.shape[0])).reshape(-1, LANES)
    for axis, bit in steps:
        x = halve(x, axis, bit)
    if rest:
        x = lax.psum(x, tuple(rest))
    for axis, bit in reversed(steps):
        x = double(x, axis, bit)
    flat = x.reshape(-1)
    out = []
    offset = 0
    for v in values:
        out.append(flat[offset : offset + v.size].reshape(v.shape))
        offset += v.size
    return tuple(out)


def padded_2(cells, sides, width, closed):
    for axis, dim in sides:
        count = lax.axis_size(axis)
        ends = count if closed else count - 1
        head = lax.slice_in_dim(cells, 0, width, axis=dim)
        tail = lax.slice_in_dim(cells, cells.shape[dim] - width, cells.shape[dim], axis=dim)
        cells = jnp.concatenate(
            [
                lax.ppermute(tail, axis, [(i, (i + 1) % count) for i in range(ends)]),
                cells,
                lax.ppermute(head, axis, [((i + 1) % count, i) for i in range(ends)]),
            ],
            axis=dim,
        )
    return cells


def local(
    acts, rates, dw_kernel, pw_weight, head_weight, teacher_tiles, tile_dest, tile_start, tile_count
):
    micro_batch, band_rows, block_cols, width = acts.shape
    teach_width = head_weight.shape[1]
    lat_index = lax.axis_index("lat")
    lat_count = lax.axis_size("lat")
    lon_count = lax.axis_size("lon")
    devices = lon_count * lat_count
    lon_padded = padded_2(acts, (("lon", 2),), DMAX, True)
    padded = padded_2(lon_padded, (("lat", 1),), DMAX, False)
    tiles_here = teacher_tiles.shape[0]
    destination = tile_dest[:, 0]
    positions = jnp.arange(tiles_here, dtype=jnp.int32)
    same_dest = destination[:, None] == destination[None, :]
    earlier = positions[:, None] > positions[None, :]
    slot_rank = jnp.sum((same_dest & earlier).astype(jnp.int32), axis=1)
    slot_index = destination * CAP + slot_rank
    slots = devices * CAP
    base = 64
    column = jnp.zeros((tiles_here, TILE, 1), jnp.float32)
    column = column.at[:, 0, 0].set((tile_start // base).astype(jnp.float32))
    column = column.at[:, 1, 0].set((tile_start % base).astype(jnp.float32))
    column = column.at[:, 2, 0].set(tile_count.astype(jnp.float32))
    packed = jnp.concatenate([teacher_tiles, column.astype(jnp.bfloat16)], axis=2)
    chooser = (slot_index[None, :] == jnp.arange(slots, dtype=jnp.int32)[:, None]).astype(
        jnp.bfloat16
    )
    send = jnp.dot(
        chooser, packed.reshape(tiles_here, -1), preferred_element_type=jnp.float32
    ).astype(jnp.bfloat16)
    recv = lax.all_to_all(
        send.reshape(slots, TILE, teach_width + 1),
        ("lon", "lat"),
        split_axis=0,
        concat_axis=0,
        tiled=True,
    )
    recv_tiles = recv[:, :, :teach_width]
    meta = recv[:, :3, teach_width].astype(jnp.int32)
    recv_start = meta[:, 0] * base + meta[:, 1]
    recv_count = meta[:, 2]
    offsets = jnp.arange(TILE, dtype=jnp.int32)
    is_valid = offsets[None, :] < recv_count[:, None]
    sample_of = recv_start // (block_cols * band_rows)
    inner_row = recv_start // block_cols % band_rows
    first_col = recv_start % block_cols
    glob_row = lat_index * band_rows + inner_row
    area_weight = jnp.cos(
        jnp.pi * ((glob_row.astype(jnp.float32) + 0.5) / (band_rows * lat_count) - 0.5)
    )
    row_weight = jnp.where(is_valid, area_weight[:, None], jnp.float32(0.0)) / jnp.float32(
        devices * tiles_here * TILE
    )
    kernel = dw_kernel.astype(jnp.float32)
    onehot = (
        rates[None, :] == jnp.arange(1, DMAX + 1, dtype=jnp.int32)[:, None]
    ).astype(jnp.float32)
    span = 2 * DMAX + 1
    reach = TILE + 2 * DMAX

    padded_rows = padded.reshape((-1,) + padded.shape[2:])
    rows_per_sample = padded.shape[1]

    def gather_windows(place):
        b, h, w = place
        return jax.vmap(
            lambda row, w: lax.dynamic_slice(
                padded_rows, (row, w, jnp.int32(0)), (span, reach, width)
            )
        )(b * rows_per_sample + h, w)

    def shifted(source, row_shift, col_shift):
        return source[:, DMAX + row_shift, DMAX + col_shift : DMAX + col_shift + TILE, :].astype(
            jnp.float32
        )

    def forward(windows, tiles, weight):
        center = shifted(windows, 0, 0)
        accum_sum = center * kernel[4]
        for dilation in range(1, DMAX + 1):
            for tap_index in range(9):
                if tap_index == 4:
                    continue
                row_shift = (tap_index // 3 - 1) * dilation
                col_shift = (tap_index % 3 - 1) * dilation
                accum_sum = accum_sum + kernel[tap_index] * onehot[dilation - 1] * shifted(
                    windows, row_shift, col_shift
                )
        depth_flat = accum_sum.astype(jnp.bfloat16).reshape(-1, width)
        preact = jnp.dot(depth_flat, pw_weight, preferred_element_type=jnp.float32)
        y_rows = (center.reshape(-1, width) + jax.nn.silu(preact)).astype(jnp.bfloat16)
        weight = weight.reshape(-1, 1)
        predicted = jnp.dot(y_rows, head_weight, preferred_element_type=jnp.float32)
        residual = predicted - tiles.reshape(-1, teach_width).astype(jnp.float32)
        loss_part = jnp.sum(weight * residual * residual)
        grad_pred = (2.0 * weight * residual).astype(jnp.bfloat16)
        head_part = lax.dot_general(
            y_rows, grad_pred, (((0,), (0,)), ((), ())), preferred_element_type=jnp.float32
        )
        grad_rows = jnp.dot(grad_pred, head_weight.T, preferred_element_type=jnp.float32)
        return depth_flat, preact, grad_rows, loss_part, head_part

    def backward(windows, depth_flat, grad_u):
        pw_part = lax.dot_general(
            depth_flat, grad_u, (((0,), (0,)), ((), ())), preferred_element_type=jnp.float32
        )
        grad_z = jnp.dot(grad_u, pw_weight.T, preferred_element_type=jnp.float32)
        grad_z = grad_z.reshape(windows.shape[0], TILE, width)
        tap_sums = []
        for tap_index in range(9):
            if tap_index == 4:
                part = shifted(windows, 0, 0) * grad_z
                tap_sums.append(jnp.sum(part.reshape(-1, width), axis=0))
                continue
            tap_sum = jnp.zeros((width,), jnp.float32)
            for dilation in range(1, DMAX + 1):
                row_shift = (tap_index // 3 - 1) * dilation
                col_shift = (tap_index % 3 - 1) * dilation
                part = shifted(windows, row_shift, col_shift) * grad_z
                part = jnp.sum(part.reshape(-1, width), axis=0)
                tap_sum = tap_sum + onehot[dilation - 1] * part
            tap_sums.append(tap_sum)
        return pw_part, jnp.stack(tap_sums, axis=0)

    slots = recv_start.shape[0]
    chunk = min(slots, CHUNK)
    chunks = slots // chunk
    place = (sample_of, inner_row, first_col)
    if chunks == 1:
        windows = gather_windows(place)
        depth_flat, preact, grad_rows, loss_sum, grad_head = forward(
            windows, recv_tiles, row_weight
        )
    else:
        split = lambda v: v.reshape((chunks, chunk) + v.shape[1:])
        outs = lax.map(
            lambda xs: forward(gather_windows(xs[0]), xs[1], xs[2]),
            (tuple(split(v) for v in place), split(recv_tiles), split(row_weight)),
        )
        depth_flat, preact, grad_rows = (v.reshape((-1, width)) for v in outs[:3])
        loss_sum, grad_head = jnp.sum(outs[3]), jnp.sum(outs[4], axis=0)
    cell = (recv_start[:, None] + offsets[None, :]).reshape(-1)
    row_ids = jnp.arange(cell.shape[0], dtype=jnp.int32)
    if cell.shape[0] <= 512:
        same_cell = cell[:, None] == cell[None, :]
        grad_y = jnp.dot(
            same_cell.astype(jnp.float32),
            grad_rows,
            precision=lax.Precision.HIGHEST,
            preferred_element_type=jnp.float32,
        )
        repeated = jnp.any(same_cell & (row_ids[None, :] < row_ids[:, None]), axis=1)
    else:
        cells_here = micro_batch * band_rows * block_cols
        grid = jnp.zeros((cells_here, width), jnp.float32).at[cell].add(grad_rows)
        grad_y = grid[cell]
        owner = jnp.full((cells_here,), cell.shape[0], jnp.int32).at[cell].min(row_ids)
        repeated = owner[cell] != row_ids
    sigmoid_u = jax.nn.sigmoid(preact)
    grad_u = (grad_y * sigmoid_u * (1.0 + preact * (1.0 - sigmoid_u))).astype(jnp.bfloat16)
    grad_u = jnp.where(repeated[:, None], jnp.zeros_like(grad_u), grad_u)
    if chunks == 1:
        windows_again, grad_u = lax.optimization_barrier((windows, grad_u))
        grad_pw, grad_dw = backward(windows_again, depth_flat, grad_u)
    else:
        rows_split = lambda v: v.reshape((chunks, chunk * TILE) + v.shape[1:])
        outs = lax.map(
            lambda xs: backward(gather_windows(xs[0]), xs[1], xs[2]),
            (tuple(split(v) for v in place), rows_split(depth_flat), rows_split(grad_u)),
        )
        grad_pw, grad_dw = jnp.sum(outs[0], axis=0), jnp.sum(outs[1], axis=0)
    grad_dw, grad_pw, grad_head, loss_sum = packed_sum(
        (grad_dw, grad_pw, grad_head, loss_sum), ("lat", "lon")
    )
    return (grad_dw, grad_pw, grad_head, (loss_sum / teach_width).reshape(1))


def solution(mesh):
    in_specs = (
        P("groups", "lat", "lon", None),
        P(),
        P(),
        P(),
        P(),
        P(("groups", "lon", "lat"), None, None),
        P(("groups", "lon", "lat"), None),
        P(("groups", "lon", "lat")),
        P(("groups", "lon", "lat")),
    )
    out_specs = (P("groups", None), P("groups", None), P("groups", None), P("groups"))
    return jax.shard_map(local, mesh=mesh, in_specs=in_specs, out_specs=out_specs, check_vma=False)
```

```python
import jax
import jax.numpy as jnp
from jax import lax
from jax.sharding import PartitionSpec as P

DMAX = 4
TILE = 8
CAP = 2
CHUNK = 32


LANES = 128
EXCHANGED = 2


def halve(x, axis, bit):
    count = lax.axis_size(axis)
    rows = x.shape[0] // 2
    upper = (lax.axis_index(axis) // bit) % 2
    keep = lax.dynamic_slice_in_dim(x, upper * rows, rows, 0)
    send = lax.dynamic_slice_in_dim(x, (1 - upper) * rows, rows, 0)
    return keep + lax.ppermute(send, axis, [(i, i ^ bit) for i in range(count)])


def double(x, axis, bit):
    count = lax.axis_size(axis)
    rows = x.shape[0]
    upper = (lax.axis_index(axis) // bit) % 2
    got = lax.ppermute(x, axis, [(i, i ^ bit) for i in range(count)])
    whole = jnp.zeros((2 * rows,) + x.shape[1:], x.dtype)
    whole = lax.dynamic_update_slice_in_dim(whole, x, upper * rows, 0)
    return lax.dynamic_update_slice_in_dim(whole, got, (1 - upper) * rows, 0)


def packed_sum(values, axes):
    steps = []
    rest = []
    for axis in axes:
        count = lax.axis_size(axis)
        if count & (count - 1):
            rest.append(axis)
            continue
        bit = 1
        while bit < count:
            steps.append((axis, bit))
            bit *= 2
    flat = jnp.concatenate([jnp.ravel(v).astype(jnp.float32) for v in values])
    unit = 8 * LANES * (2 ** len(steps))
    total = -(-flat.shape[0] // unit) * unit
    x = jnp.pad(flat, (0, total - flat.shape[0])).reshape(-1, LANES)
    halved = steps[: max(0, len(steps) - EXCHANGED)]
    for axis, bit in halved:
        x = halve(x, axis, bit)
    for axis, bit in steps[len(halved) :]:
        count = lax.axis_size(axis)
        x = x + lax.ppermute(x, axis, [(i, i ^ bit) for i in range(count)])
    if rest:
        x = lax.psum(x, tuple(rest))
    for axis, bit in reversed(halved):
        x = double(x, axis, bit)
    flat = x.reshape(-1)
    out = []
    offset = 0
    for v in values:
        out.append(flat[offset : offset + v.size].reshape(v.shape))
        offset += v.size
    return tuple(out)


def padded_2(cells, sides, width, closed):
    for axis, dim in sides:
        count = lax.axis_size(axis)
        ends = count if closed else count - 1
        head = lax.slice_in_dim(cells, 0, width, axis=dim)
        tail = lax.slice_in_dim(cells, cells.shape[dim] - width, cells.shape[dim], axis=dim)
        cells = jnp.concatenate(
            [
                lax.ppermute(tail, axis, [(i, (i + 1) % count) for i in range(ends)]),
                cells,
                lax.ppermute(head, axis, [((i + 1) % count, i) for i in range(ends)]),
            ],
            axis=dim,
        )
    return cells


def local(
    acts, rates, dw_kernel, pw_weight, head_weight, teacher_tiles, tile_dest, tile_start, tile_count
):
    micro_batch, band_rows, block_cols, width = acts.shape
    teach_width = head_weight.shape[1]
    lat_index = lax.axis_index("lat")
    lat_count = lax.axis_size("lat")
    lon_count = lax.axis_size("lon")
    devices = lon_count * lat_count
    lon_padded = padded_2(acts, (("lon", 2),), DMAX, True)
    padded = padded_2(lon_padded, (("lat", 1),), DMAX, False)
    tiles_here = teacher_tiles.shape[0]
    destination = tile_dest[:, 0]
    positions = jnp.arange(tiles_here, dtype=jnp.int32)
    same_dest = destination[:, None] == destination[None, :]
    earlier = positions[:, None] > positions[None, :]
    slot_rank = jnp.sum((same_dest & earlier).astype(jnp.int32), axis=1)
    slot_index = destination * CAP + slot_rank
    slots = devices * CAP
    base = 64
    column = jnp.zeros((tiles_here, TILE, 1), jnp.float32)
    column = column.at[:, 0, 0].set((tile_start // base).astype(jnp.float32))
    column = column.at[:, 1, 0].set((tile_start % base).astype(jnp.float32))
    column = column.at[:, 2, 0].set(tile_count.astype(jnp.float32))
    packed = jnp.concatenate([teacher_tiles, column.astype(jnp.bfloat16)], axis=2)
    chooser = (slot_index[None, :] == jnp.arange(slots, dtype=jnp.int32)[:, None]).astype(
        jnp.bfloat16
    )
    send = jnp.dot(
        chooser, packed.reshape(tiles_here, -1), preferred_element_type=jnp.float32
    ).astype(jnp.bfloat16)
    recv = lax.all_to_all(
        send.reshape(slots, TILE, teach_width + 1),
        ("lon", "lat"),
        split_axis=0,
        concat_axis=0,
        tiled=True,
    )
    recv_tiles = recv[:, :, :teach_width]
    meta = recv[:, :3, teach_width].astype(jnp.int32)
    recv_start = meta[:, 0] * base + meta[:, 1]
    recv_count = meta[:, 2]
    offsets = jnp.arange(TILE, dtype=jnp.int32)
    is_valid = offsets[None, :] < recv_count[:, None]
    sample_of = recv_start // (block_cols * band_rows)
    inner_row = recv_start // block_cols % band_rows
    first_col = recv_start % block_cols
    glob_row = lat_index * band_rows + inner_row
    area_weight = jnp.cos(
        jnp.pi * ((glob_row.astype(jnp.float32) + 0.5) / (band_rows * lat_count) - 0.5)
    )
    row_weight = jnp.where(is_valid, area_weight[:, None], jnp.float32(0.0)) / jnp.float32(
        devices * tiles_here * TILE
    )
    kernel = dw_kernel.astype(jnp.float32)
    onehot = (
        rates[None, :] == jnp.arange(1, DMAX + 1, dtype=jnp.int32)[:, None]
    ).astype(jnp.float32)
    span = 2 * DMAX + 1
    reach = TILE + 2 * DMAX

    def gather_windows(place):
        b, h, w = place
        return jax.vmap(
            lambda b, h, w: lax.dynamic_slice(
                padded, (b, h, w, jnp.int32(0)), (1, span, reach, width)
            )[0]
        )(b, h, w)

    def shifted(source, row_shift, col_shift):
        return source[:, DMAX + row_shift, DMAX + col_shift : DMAX + col_shift + TILE, :].astype(
            jnp.float32
        )

    def forward(windows, tiles, weight):
        center = shifted(windows, 0, 0)
        accum_sum = center * kernel[4]
        for dilation in range(1, DMAX + 1):
            for tap_index in range(9):
                if tap_index == 4:
                    continue
                row_shift = (tap_index // 3 - 1) * dilation
                col_shift = (tap_index % 3 - 1) * dilation
                accum_sum = accum_sum + kernel[tap_index] * onehot[dilation - 1] * shifted(
                    windows, row_shift, col_shift
                )
        depth_flat = accum_sum.astype(jnp.bfloat16).reshape(-1, width)
        preact = jnp.dot(depth_flat, pw_weight, preferred_element_type=jnp.float32)
        y_rows = (center.reshape(-1, width) + jax.nn.silu(preact)).astype(jnp.bfloat16)
        weight = weight.reshape(-1, 1)
        predicted = jnp.dot(y_rows, head_weight, preferred_element_type=jnp.float32)
        residual = predicted - tiles.reshape(-1, teach_width).astype(jnp.float32)
        loss_part = jnp.sum(weight * residual * residual)
        grad_pred = (2.0 * weight * residual).astype(jnp.bfloat16)
        head_part = lax.dot_general(
            y_rows, grad_pred, (((0,), (0,)), ((), ())), preferred_element_type=jnp.float32
        )
        grad_rows = jnp.dot(grad_pred, head_weight.T, preferred_element_type=jnp.float32)
        return depth_flat, preact, grad_rows, loss_part, head_part

    def backward(windows, depth_flat, grad_u):
        pw_part = lax.dot_general(
            depth_flat, grad_u, (((0,), (0,)), ((), ())), preferred_element_type=jnp.float32
        )
        grad_z = jnp.dot(grad_u, pw_weight.T, preferred_element_type=jnp.float32)
        grad_z = grad_z.reshape(windows.shape[0], TILE, width)
        tap_sums = []
        for tap_index in range(9):
            if tap_index == 4:
                part = shifted(windows, 0, 0) * grad_z
                tap_sums.append(jnp.sum(part.reshape(-1, width), axis=0))
                continue
            tap_sum = jnp.zeros((width,), jnp.float32)
            for dilation in range(1, DMAX + 1):
                row_shift = (tap_index // 3 - 1) * dilation
                col_shift = (tap_index % 3 - 1) * dilation
                part = shifted(windows, row_shift, col_shift) * grad_z
                part = jnp.sum(part.reshape(-1, width), axis=0)
                tap_sum = tap_sum + onehot[dilation - 1] * part
            tap_sums.append(tap_sum)
        return pw_part, jnp.stack(tap_sums, axis=0)

    slots = recv_start.shape[0]
    chunk = min(slots, CHUNK)
    chunks = slots // chunk
    place = (sample_of, inner_row, first_col)
    if chunks == 1:
        windows = gather_windows(place)
        depth_flat, preact, grad_rows, loss_sum, grad_head = forward(
            windows, recv_tiles, row_weight
        )
    else:
        split = lambda v: v.reshape((chunks, chunk) + v.shape[1:])
        outs = lax.map(
            lambda xs: forward(gather_windows(xs[0]), xs[1], xs[2]),
            (tuple(split(v) for v in place), split(recv_tiles), split(row_weight)),
        )
        depth_flat, preact, grad_rows = (v.reshape((-1, width)) for v in outs[:3])
        loss_sum, grad_head = jnp.sum(outs[3]), jnp.sum(outs[4], axis=0)
    cell = (recv_start[:, None] + offsets[None, :]).reshape(-1)
    row_ids = jnp.arange(cell.shape[0], dtype=jnp.int32)
    if cell.shape[0] <= 512:
        same_cell = cell[:, None] == cell[None, :]
        grad_y = jnp.dot(
            same_cell.astype(jnp.float32),
            grad_rows,
            precision=lax.Precision.HIGHEST,
            preferred_element_type=jnp.float32,
        )
        repeated = jnp.any(same_cell & (row_ids[None, :] < row_ids[:, None]), axis=1)
    else:
        cells_here = micro_batch * band_rows * block_cols
        grid = jnp.zeros((cells_here, width), jnp.float32).at[cell].add(grad_rows)
        grad_y = grid[cell]
        owner = jnp.full((cells_here,), cell.shape[0], jnp.int32).at[cell].min(row_ids)
        repeated = owner[cell] != row_ids
    sigmoid_u = jax.nn.sigmoid(preact)
    grad_u = (grad_y * sigmoid_u * (1.0 + preact * (1.0 - sigmoid_u))).astype(jnp.bfloat16)
    grad_u = jnp.where(repeated[:, None], jnp.zeros_like(grad_u), grad_u)
    if chunks == 1:
        windows_again, grad_u = lax.optimization_barrier((windows, grad_u))
        grad_pw, grad_dw = backward(windows_again, depth_flat, grad_u)
    else:
        rows_split = lambda v: v.reshape((chunks, chunk * TILE) + v.shape[1:])
        outs = lax.map(
            lambda xs: backward(gather_windows(xs[0]), xs[1], xs[2]),
            (tuple(split(v) for v in place), rows_split(depth_flat), rows_split(grad_u)),
        )
        grad_pw, grad_dw = jnp.sum(outs[0], axis=0), jnp.sum(outs[1], axis=0)
    grad_dw, grad_pw, grad_head, loss_sum = packed_sum(
        (grad_dw, grad_pw, grad_head, loss_sum), ("lat", "lon")
    )
    return (grad_dw, grad_pw, grad_head, (loss_sum / teach_width).reshape(1))


def solution(mesh):
    in_specs = (
        P("groups", "lat", "lon", None),
        P(),
        P(),
        P(),
        P(),
        P(("groups", "lon", "lat"), None, None),
        P(("groups", "lon", "lat"), None),
        P(("groups", "lon", "lat")),
        P(("groups", "lon", "lat")),
    )
    out_specs = (P("groups", None), P("groups", None), P("groups", None), P("groups"))
    return jax.shard_map(local, mesh=mesh, in_specs=in_specs, out_specs=out_specs, check_vma=False)
```

```python
import jax
import jax.numpy as jnp
from jax import lax
from jax.sharding import PartitionSpec as P

DMAX = 4
TILE = 8
CAP = 2
CHUNK = 32


LANES = 128
EXCHANGED = 2


def halve(x, axis, bit):
    count = lax.axis_size(axis)
    rows = x.shape[0] // 2
    upper = (lax.axis_index(axis) // bit) % 2
    keep = lax.dynamic_slice_in_dim(x, upper * rows, rows, 0)
    send = lax.dynamic_slice_in_dim(x, (1 - upper) * rows, rows, 0)
    return keep + lax.ppermute(send, axis, [(i, i ^ bit) for i in range(count)])


def double(x, axis, bit):
    count = lax.axis_size(axis)
    rows = x.shape[0]
    upper = (lax.axis_index(axis) // bit) % 2
    got = lax.ppermute(x, axis, [(i, i ^ bit) for i in range(count)])
    whole = jnp.zeros((2 * rows,) + x.shape[1:], x.dtype)
    whole = lax.dynamic_update_slice_in_dim(whole, x, upper * rows, 0)
    return lax.dynamic_update_slice_in_dim(whole, got, (1 - upper) * rows, 0)


def packed_sum(values, axes):
    steps = []
    rest = []
    for axis in axes:
        count = lax.axis_size(axis)
        if count & (count - 1):
            rest.append(axis)
            continue
        bit = 1
        while bit < count:
            steps.append((axis, bit))
            bit *= 2
    blocks = [jnp.reshape(v, (-1, v.shape[-1]) if v.ndim else (1, 1)) for v in values]
    cols = -(-max(blk.shape[1] for blk in blocks) // LANES) * LANES
    blocks = [
        jnp.pad(blk.astype(jnp.float32), ((0, 0), (0, cols - blk.shape[1]))) for blk in blocks
    ]
    x = jnp.concatenate(blocks, axis=0)
    halvings = max(0, len(steps) - EXCHANGED)
    unit = 8 * (2**halvings)
    x = jnp.pad(x, ((0, -(-x.shape[0] // unit) * unit - x.shape[0]), (0, 0)))
    halved = steps[: max(0, len(steps) - EXCHANGED)]
    for axis, bit in halved:
        x = halve(x, axis, bit)
    for axis, bit in steps[len(halved) :]:
        count = lax.axis_size(axis)
        x = x + lax.ppermute(x, axis, [(i, i ^ bit) for i in range(count)])
    if rest:
        x = lax.psum(x, tuple(rest))
    for axis, bit in reversed(halved):
        x = double(x, axis, bit)
    out = []
    offset = 0
    for v, blk in zip(values, blocks):
        rows = blk.shape[0]
        width = v.shape[-1] if v.ndim else 1
        out.append(x[offset : offset + rows, :width].reshape(v.shape))
        offset += rows
    return tuple(out)


def padded_2(cells, sides, width, closed):
    for axis, dim in sides:
        count = lax.axis_size(axis)
        ends = count if closed else count - 1
        head = lax.slice_in_dim(cells, 0, width, axis=dim)
        tail = lax.slice_in_dim(cells, cells.shape[dim] - width, cells.shape[dim], axis=dim)
        cells = jnp.concatenate(
            [
                lax.ppermute(tail, axis, [(i, (i + 1) % count) for i in range(ends)]),
                cells,
                lax.ppermute(head, axis, [((i + 1) % count, i) for i in range(ends)]),
            ],
            axis=dim,
        )
    return cells


def local(
    acts, rates, dw_kernel, pw_weight, head_weight, teacher_tiles, tile_dest, tile_start, tile_count
):
    micro_batch, band_rows, block_cols, width = acts.shape
    teach_width = head_weight.shape[1]
    lat_index = lax.axis_index("lat")
    lat_count = lax.axis_size("lat")
    lon_count = lax.axis_size("lon")
    devices = lon_count * lat_count
    lon_padded = padded_2(acts, (("lon", 2),), DMAX, True)
    padded = padded_2(lon_padded, (("lat", 1),), DMAX, False)
    tiles_here = teacher_tiles.shape[0]
    destination = tile_dest[:, 0]
    positions = jnp.arange(tiles_here, dtype=jnp.int32)
    same_dest = destination[:, None] == destination[None, :]
    earlier = positions[:, None] > positions[None, :]
    slot_rank = jnp.sum((same_dest & earlier).astype(jnp.int32), axis=1)
    slot_index = destination * CAP + slot_rank
    slots = devices * CAP
    base = 64
    column = jnp.zeros((tiles_here, TILE, 1), jnp.float32)
    column = column.at[:, 0, 0].set((tile_start // base).astype(jnp.float32))
    column = column.at[:, 1, 0].set((tile_start % base).astype(jnp.float32))
    column = column.at[:, 2, 0].set(tile_count.astype(jnp.float32))
    packed = jnp.concatenate([teacher_tiles, column.astype(jnp.bfloat16)], axis=2)
    chooser = (slot_index[None, :] == jnp.arange(slots, dtype=jnp.int32)[:, None]).astype(
        jnp.bfloat16
    )
    send = jnp.dot(
        chooser, packed.reshape(tiles_here, -1), preferred_element_type=jnp.float32
    ).astype(jnp.bfloat16)
    recv = lax.all_to_all(
        send.reshape(slots, TILE, teach_width + 1),
        ("lon", "lat"),
        split_axis=0,
        concat_axis=0,
        tiled=True,
    )
    recv_tiles = recv[:, :, :teach_width]
    meta = recv[:, :3, teach_width].astype(jnp.int32)
    recv_start = meta[:, 0] * base + meta[:, 1]
    recv_count = meta[:, 2]
    offsets = jnp.arange(TILE, dtype=jnp.int32)
    is_valid = offsets[None, :] < recv_count[:, None]
    sample_of = recv_start // (block_cols * band_rows)
    inner_row = recv_start // block_cols % band_rows
    first_col = recv_start % block_cols
    glob_row = lat_index * band_rows + inner_row
    area_weight = jnp.cos(
        jnp.pi * ((glob_row.astype(jnp.float32) + 0.5) / (band_rows * lat_count) - 0.5)
    )
    row_weight = jnp.where(is_valid, area_weight[:, None], jnp.float32(0.0)) / jnp.float32(
        devices * tiles_here * TILE
    )
    kernel = dw_kernel.astype(jnp.float32)
    onehot = (
        rates[None, :] == jnp.arange(1, DMAX + 1, dtype=jnp.int32)[:, None]
    ).astype(jnp.float32)
    span = 2 * DMAX + 1
    reach = TILE + 2 * DMAX

    def gather_windows(place):
        b, h, w = place
        return jax.vmap(
            lambda b, h, w: lax.dynamic_slice(
                padded, (b, h, w, jnp.int32(0)), (1, span, reach, width)
            )[0]
        )(b, h, w)

    def shifted(source, row_shift, col_shift):
        return source[:, DMAX + row_shift, DMAX + col_shift : DMAX + col_shift + TILE, :].astype(
            jnp.float32
        )

    def forward(windows, tiles, weight):
        center = shifted(windows, 0, 0)
        accum_sum = center * kernel[4]
        for dilation in range(1, DMAX + 1):
            for tap_index in range(9):
                if tap_index == 4:
                    continue
                row_shift = (tap_index // 3 - 1) * dilation
                col_shift = (tap_index % 3 - 1) * dilation
                accum_sum = accum_sum + kernel[tap_index] * onehot[dilation - 1] * shifted(
                    windows, row_shift, col_shift
                )
        depth_flat = accum_sum.astype(jnp.bfloat16).reshape(-1, width)
        preact = jnp.dot(depth_flat, pw_weight, preferred_element_type=jnp.float32)
        y_rows = (center.reshape(-1, width) + jax.nn.silu(preact)).astype(jnp.bfloat16)
        weight = weight.reshape(-1, 1)
        predicted = jnp.dot(y_rows, head_weight, preferred_element_type=jnp.float32)
        residual = predicted - tiles.reshape(-1, teach_width).astype(jnp.float32)
        loss_part = jnp.sum(weight * residual * residual)
        grad_pred = (2.0 * weight * residual).astype(jnp.bfloat16)
        head_part = lax.dot_general(
            y_rows, grad_pred, (((0,), (0,)), ((), ())), preferred_element_type=jnp.float32
        )
        grad_rows = jnp.dot(grad_pred, head_weight.T, preferred_element_type=jnp.float32)
        return depth_flat, preact, grad_rows, loss_part, head_part

    def backward(windows, depth_flat, grad_u):
        pw_part = lax.dot_general(
            depth_flat, grad_u, (((0,), (0,)), ((), ())), preferred_element_type=jnp.float32
        )
        grad_z = jnp.dot(grad_u, pw_weight.T, preferred_element_type=jnp.float32)
        grad_z = grad_z.reshape(windows.shape[0], TILE, width)
        tap_sums = []
        for tap_index in range(9):
            if tap_index == 4:
                part = shifted(windows, 0, 0) * grad_z
                tap_sums.append(jnp.sum(part.reshape(-1, width), axis=0))
                continue
            tap_sum = jnp.zeros((width,), jnp.float32)
            for dilation in range(1, DMAX + 1):
                row_shift = (tap_index // 3 - 1) * dilation
                col_shift = (tap_index % 3 - 1) * dilation
                part = shifted(windows, row_shift, col_shift) * grad_z
                part = jnp.sum(part.reshape(-1, width), axis=0)
                tap_sum = tap_sum + onehot[dilation - 1] * part
            tap_sums.append(tap_sum)
        return pw_part, jnp.stack(tap_sums, axis=0)

    slots = recv_start.shape[0]
    chunk = min(slots, CHUNK)
    chunks = slots // chunk
    place = (sample_of, inner_row, first_col)
    if chunks == 1:
        windows = gather_windows(place)
        depth_flat, preact, grad_rows, loss_sum, grad_head = forward(
            windows, recv_tiles, row_weight
        )
    else:
        split = lambda v: v.reshape((chunks, chunk) + v.shape[1:])
        outs = lax.map(
            lambda xs: forward(gather_windows(xs[0]), xs[1], xs[2]),
            (tuple(split(v) for v in place), split(recv_tiles), split(row_weight)),
        )
        depth_flat, preact, grad_rows = (v.reshape((-1, width)) for v in outs[:3])
        loss_sum, grad_head = jnp.sum(outs[3]), jnp.sum(outs[4], axis=0)
    cell = (recv_start[:, None] + offsets[None, :]).reshape(-1)
    row_ids = jnp.arange(cell.shape[0], dtype=jnp.int32)
    if cell.shape[0] <= 512:
        same_cell = cell[:, None] == cell[None, :]
        grad_y = jnp.dot(
            same_cell.astype(jnp.float32),
            grad_rows,
            precision=lax.Precision.HIGHEST,
            preferred_element_type=jnp.float32,
        )
        repeated = jnp.any(same_cell & (row_ids[None, :] < row_ids[:, None]), axis=1)
    else:
        cells_here = micro_batch * band_rows * block_cols
        grid = jnp.zeros((cells_here, width), jnp.float32).at[cell].add(grad_rows)
        grad_y = grid[cell]
        owner = jnp.full((cells_here,), cell.shape[0], jnp.int32).at[cell].min(row_ids)
        repeated = owner[cell] != row_ids
    sigmoid_u = jax.nn.sigmoid(preact)
    grad_u = (grad_y * sigmoid_u * (1.0 + preact * (1.0 - sigmoid_u))).astype(jnp.bfloat16)
    grad_u = jnp.where(repeated[:, None], jnp.zeros_like(grad_u), grad_u)
    if chunks == 1:
        windows_again, grad_u = lax.optimization_barrier((windows, grad_u))
        grad_pw, grad_dw = backward(windows_again, depth_flat, grad_u)
    else:
        rows_split = lambda v: v.reshape((chunks, chunk * TILE) + v.shape[1:])
        outs = lax.map(
            lambda xs: backward(gather_windows(xs[0]), xs[1], xs[2]),
            (tuple(split(v) for v in place), rows_split(depth_flat), rows_split(grad_u)),
        )
        grad_pw, grad_dw = jnp.sum(outs[0], axis=0), jnp.sum(outs[1], axis=0)
    grad_pw, grad_head, grad_dw, loss_sum = packed_sum(
        (grad_pw, grad_head, grad_dw, loss_sum), ("lat", "lon")
    )
    return (grad_dw, grad_pw, grad_head, (loss_sum / teach_width).reshape(1))


def solution(mesh):
    in_specs = (
        P("groups", "lat", "lon", None),
        P(),
        P(),
        P(),
        P(),
        P(("groups", "lon", "lat"), None, None),
        P(("groups", "lon", "lat"), None),
        P(("groups", "lon", "lat")),
        P(("groups", "lon", "lat")),
    )
    out_specs = (P("groups", None), P("groups", None), P("groups", None), P("groups"))
    return jax.shard_map(local, mesh=mesh, in_specs=in_specs, out_specs=out_specs, check_vma=False)
```

```python
import jax
import jax.numpy as jnp
from jax import lax
from jax.experimental import pallas as pl
from jax.experimental.pallas import tpu as pltpu
from jax.sharding import PartitionSpec as P

DMAX = 4
TILE = 8
CAP = 2
CHUNK = 32


LANES = 128
EXCHANGED = 2


def tap_list():
    taps = [(0, 0)]
    for dilation in range(1, DMAX + 1):
        for tap_index in range(9):
            if tap_index == 4:
                continue
            taps.append(((tap_index // 3 - 1) * dilation, (tap_index % 3 - 1) * dilation))
    return taps

def conv_kernel(win_ref, coef_ref, out_ref):
    taps = tap_list()
    def body(s, carry):
        acc = None
        for i, (rs, cs) in enumerate(taps):
            term = coef_ref[i : i + 1, :] * win_ref[s, DMAX + rs, pl.ds(DMAX + cs, TILE), :]
            acc = term if acc is None else acc + term
        out_ref[s] = acc
        return carry
    lax.fori_loop(0, win_ref.shape[0], body, 0)

def taps_conv(win, coef):
    slots, _, _, width = win.shape
    return pl.pallas_call(
        conv_kernel,
        out_shape=jax.ShapeDtypeStruct((slots, TILE, width), jnp.float32),
        in_specs=[pl.BlockSpec(memory_space=pltpu.VMEM)] * 2,
        out_specs=pl.BlockSpec(memory_space=pltpu.VMEM),
    )(win, coef)

def grad_kernel(win_ref, gz_ref, out_ref):
    taps = tap_list()
    out_ref[...] = jnp.zeros_like(out_ref)
    def body(s, carry):
        gz = gz_ref[s]
        for i, (rs, cs) in enumerate(taps):
            out_ref[i] += win_ref[s, DMAX + rs, pl.ds(DMAX + cs, TILE), :] * gz
        return carry
    lax.fori_loop(0, win_ref.shape[0], body, 0)

def taps_grad(win, gz):
    slots, _, _, width = win.shape
    return pl.pallas_call(
        grad_kernel,
        out_shape=jax.ShapeDtypeStruct((len(tap_list()), TILE, width), jnp.float32),
        in_specs=[pl.BlockSpec(memory_space=pltpu.VMEM)] * 2,
        out_specs=pl.BlockSpec(memory_space=pltpu.VMEM),
    )(win, gz)


def halve(x, axis, bit):
    count = lax.axis_size(axis)
    rows = x.shape[0] // 2
    upper = (lax.axis_index(axis) // bit) % 2
    keep = lax.dynamic_slice_in_dim(x, upper * rows, rows, 0)
    send = lax.dynamic_slice_in_dim(x, (1 - upper) * rows, rows, 0)
    return keep + lax.ppermute(send, axis, [(i, i ^ bit) for i in range(count)])


def double(x, axis, bit):
    count = lax.axis_size(axis)
    rows = x.shape[0]
    upper = (lax.axis_index(axis) // bit) % 2
    got = lax.ppermute(x, axis, [(i, i ^ bit) for i in range(count)])
    whole = jnp.zeros((2 * rows,) + x.shape[1:], x.dtype)
    whole = lax.dynamic_update_slice_in_dim(whole, x, upper * rows, 0)
    return lax.dynamic_update_slice_in_dim(whole, got, (1 - upper) * rows, 0)


def packed_sum(values, axes):
    steps = []
    rest = []
    for axis in axes:
        count = lax.axis_size(axis)
        if count & (count - 1):
            rest.append(axis)
            continue
        bit = 1
        while bit < count:
            steps.append((axis, bit))
            bit *= 2
    flat = jnp.concatenate([jnp.ravel(v).astype(jnp.float32) for v in values])
    unit = 8 * LANES * (2 ** len(steps))
    total = -(-flat.shape[0] // unit) * unit
    x = jnp.pad(flat, (0, total - flat.shape[0])).reshape(-1, LANES)
    halved = steps[: max(0, len(steps) - EXCHANGED)]
    for axis, bit in halved:
        x = halve(x, axis, bit)
    for axis, bit in steps[len(halved) :]:
        count = lax.axis_size(axis)
        x = x + lax.ppermute(x, axis, [(i, i ^ bit) for i in range(count)])
    if rest:
        x = lax.psum(x, tuple(rest))
    for axis, bit in reversed(halved):
        x = double(x, axis, bit)
    flat = x.reshape(-1)
    out = []
    offset = 0
    for v in values:
        out.append(flat[offset : offset + v.size].reshape(v.shape))
        offset += v.size
    return tuple(out)


def padded_2(cells, sides, width, closed):
    for axis, dim in sides:
        count = lax.axis_size(axis)
        ends = count if closed else count - 1
        head = lax.slice_in_dim(cells, 0, width, axis=dim)
        tail = lax.slice_in_dim(cells, cells.shape[dim] - width, cells.shape[dim], axis=dim)
        cells = jnp.concatenate(
            [
                lax.ppermute(tail, axis, [(i, (i + 1) % count) for i in range(ends)]),
                cells,
                lax.ppermute(head, axis, [((i + 1) % count, i) for i in range(ends)]),
            ],
            axis=dim,
        )
    return cells


def local(
    acts, rates, dw_kernel, pw_weight, head_weight, teacher_tiles, tile_dest, tile_start, tile_count
):
    micro_batch, band_rows, block_cols, width = acts.shape
    teach_width = head_weight.shape[1]
    lat_index = lax.axis_index("lat")
    lat_count = lax.axis_size("lat")
    lon_count = lax.axis_size("lon")
    devices = lon_count * lat_count
    lon_padded = padded_2(acts, (("lon", 2),), DMAX, True)
    padded = padded_2(lon_padded, (("lat", 1),), DMAX, False)
    tiles_here = teacher_tiles.shape[0]
    destination = tile_dest[:, 0]
    positions = jnp.arange(tiles_here, dtype=jnp.int32)
    same_dest = destination[:, None] == destination[None, :]
    earlier = positions[:, None] > positions[None, :]
    slot_rank = jnp.sum((same_dest & earlier).astype(jnp.int32), axis=1)
    slot_index = destination * CAP + slot_rank
    slots = devices * CAP
    base = 64
    column = jnp.zeros((tiles_here, TILE, 1), jnp.float32)
    column = column.at[:, 0, 0].set((tile_start // base).astype(jnp.float32))
    column = column.at[:, 1, 0].set((tile_start % base).astype(jnp.float32))
    column = column.at[:, 2, 0].set(tile_count.astype(jnp.float32))
    packed = jnp.concatenate([teacher_tiles, column.astype(jnp.bfloat16)], axis=2)
    chooser = (slot_index[None, :] == jnp.arange(slots, dtype=jnp.int32)[:, None]).astype(
        jnp.bfloat16
    )
    send = jnp.dot(
        chooser, packed.reshape(tiles_here, -1), preferred_element_type=jnp.float32
    ).astype(jnp.bfloat16)
    recv = lax.all_to_all(
        send.reshape(slots, TILE, teach_width + 1),
        ("lon", "lat"),
        split_axis=0,
        concat_axis=0,
        tiled=True,
    )
    recv_tiles = recv[:, :, :teach_width]
    meta = recv[:, :3, teach_width].astype(jnp.int32)
    recv_start = meta[:, 0] * base + meta[:, 1]
    recv_count = meta[:, 2]
    offsets = jnp.arange(TILE, dtype=jnp.int32)
    is_valid = offsets[None, :] < recv_count[:, None]
    sample_of = recv_start // (block_cols * band_rows)
    inner_row = recv_start // block_cols % band_rows
    first_col = recv_start % block_cols
    glob_row = lat_index * band_rows + inner_row
    area_weight = jnp.cos(
        jnp.pi * ((glob_row.astype(jnp.float32) + 0.5) / (band_rows * lat_count) - 0.5)
    )
    row_weight = jnp.where(is_valid, area_weight[:, None], jnp.float32(0.0)) / jnp.float32(
        devices * tiles_here * TILE
    )
    kernel = dw_kernel.astype(jnp.float32)
    onehot = (
        rates[None, :] == jnp.arange(1, DMAX + 1, dtype=jnp.int32)[:, None]
    ).astype(jnp.float32)
    span = 2 * DMAX + 1
    reach = TILE + 2 * DMAX

    def gather_windows(place):
        b, h, w = place
        return jax.vmap(
            lambda b, h, w: lax.dynamic_slice(
                padded, (b, h, w, jnp.int32(0)), (1, span, reach, width)
            )[0]
        )(b, h, w)

    def shifted(source, row_shift, col_shift):
        return source[:, DMAX + row_shift, DMAX + col_shift : DMAX + col_shift + TILE, :].astype(
            jnp.float32
        )

    coef_rows = [kernel[4]]
    for dilation in range(1, DMAX + 1):
        for tap_index in range(9):
            if tap_index != 4:
                coef_rows.append(kernel[tap_index] * onehot[dilation - 1])
    coef = jnp.stack(coef_rows)

    def forward(windows, tiles, weight):
        center = shifted(windows, 0, 0)
        accum_sum = taps_conv(windows.astype(jnp.float32), coef)
        depth_flat = accum_sum.astype(jnp.bfloat16).reshape(-1, width)
        preact = jnp.dot(depth_flat, pw_weight, preferred_element_type=jnp.float32)
        y_rows = (center.reshape(-1, width) + jax.nn.silu(preact)).astype(jnp.bfloat16)
        weight = weight.reshape(-1, 1)
        predicted = jnp.dot(y_rows, head_weight, preferred_element_type=jnp.float32)
        residual = predicted - tiles.reshape(-1, teach_width).astype(jnp.float32)
        loss_part = jnp.sum(weight * residual * residual)
        grad_pred = (2.0 * weight * residual).astype(jnp.bfloat16)
        head_part = lax.dot_general(
            y_rows, grad_pred, (((0,), (0,)), ((), ())), preferred_element_type=jnp.float32
        )
        grad_rows = jnp.dot(grad_pred, head_weight.T, preferred_element_type=jnp.float32)
        return depth_flat, preact, grad_rows, loss_part, head_part

    def backward(windows, depth_flat, grad_u):
        pw_part = lax.dot_general(
            depth_flat, grad_u, (((0,), (0,)), ((), ())), preferred_element_type=jnp.float32
        )
        grad_z = jnp.dot(grad_u, pw_weight.T, preferred_element_type=jnp.float32)
        grad_z = grad_z.reshape(windows.shape[0], TILE, width)
        parts = jnp.sum(taps_grad(windows.astype(jnp.float32), grad_z), axis=1)
        tap_sums = []
        row = 1
        rows_of = {}
        for dilation in range(1, DMAX + 1):
            for tap_index in range(9):
                if tap_index != 4:
                    rows_of[(dilation, tap_index)] = row
                    row += 1
        for tap_index in range(9):
            if tap_index == 4:
                tap_sums.append(parts[0])
                continue
            tap_sum = jnp.zeros((width,), jnp.float32)
            for dilation in range(1, DMAX + 1):
                tap_sum = tap_sum + onehot[dilation - 1] * parts[rows_of[(dilation, tap_index)]]
            tap_sums.append(tap_sum)
        return pw_part, jnp.stack(tap_sums, axis=0)

    slots = recv_start.shape[0]
    chunk = min(slots, CHUNK)
    chunks = slots // chunk
    place = (sample_of, inner_row, first_col)
    if chunks == 1:
        windows = gather_windows(place)
        depth_flat, preact, grad_rows, loss_sum, grad_head = forward(
            windows, recv_tiles, row_weight
        )
    else:
        split = lambda v: v.reshape((chunks, chunk) + v.shape[1:])
        outs = lax.map(
            lambda xs: forward(gather_windows(xs[0]), xs[1], xs[2]),
            (tuple(split(v) for v in place), split(recv_tiles), split(row_weight)),
        )
        depth_flat, preact, grad_rows = (v.reshape((-1, width)) for v in outs[:3])
        loss_sum, grad_head = jnp.sum(outs[3]), jnp.sum(outs[4], axis=0)
    cell = (recv_start[:, None] + offsets[None, :]).reshape(-1)
    row_ids = jnp.arange(cell.shape[0], dtype=jnp.int32)
    if cell.shape[0] <= 512:
        same_cell = cell[:, None] == cell[None, :]
        grad_y = jnp.dot(
            same_cell.astype(jnp.float32),
            grad_rows,
            precision=lax.Precision.HIGHEST,
            preferred_element_type=jnp.float32,
        )
        repeated = jnp.any(same_cell & (row_ids[None, :] < row_ids[:, None]), axis=1)
    else:
        cells_here = micro_batch * band_rows * block_cols
        grid = jnp.zeros((cells_here, width), jnp.float32).at[cell].add(grad_rows)
        grad_y = grid[cell]
        owner = jnp.full((cells_here,), cell.shape[0], jnp.int32).at[cell].min(row_ids)
        repeated = owner[cell] != row_ids
    sigmoid_u = jax.nn.sigmoid(preact)
    grad_u = (grad_y * sigmoid_u * (1.0 + preact * (1.0 - sigmoid_u))).astype(jnp.bfloat16)
    grad_u = jnp.where(repeated[:, None], jnp.zeros_like(grad_u), grad_u)
    if chunks == 1:
        windows_again, grad_u = lax.optimization_barrier((windows, grad_u))
        grad_pw, grad_dw = backward(windows_again, depth_flat, grad_u)
    else:
        rows_split = lambda v: v.reshape((chunks, chunk * TILE) + v.shape[1:])
        outs = lax.map(
            lambda xs: backward(gather_windows(xs[0]), xs[1], xs[2]),
            (tuple(split(v) for v in place), rows_split(depth_flat), rows_split(grad_u)),
        )
        grad_pw, grad_dw = jnp.sum(outs[0], axis=0), jnp.sum(outs[1], axis=0)
    grad_dw, grad_pw, grad_head, loss_sum = packed_sum(
        (grad_dw, grad_pw, grad_head, loss_sum), ("lat", "lon")
    )
    return (grad_dw, grad_pw, grad_head, (loss_sum / teach_width).reshape(1))


def solution(mesh):
    in_specs = (
        P("groups", "lat", "lon", None),
        P(),
        P(),
        P(),
        P(),
        P(("groups", "lon", "lat"), None, None),
        P(("groups", "lon", "lat"), None),
        P(("groups", "lon", "lat")),
        P(("groups", "lon", "lat")),
    )
    out_specs = (P("groups", None), P("groups", None), P("groups", None), P("groups"))
    return jax.shard_map(local, mesh=mesh, in_specs=in_specs, out_specs=out_specs, check_vma=False)
```

```python
import jax
import jax.numpy as jnp
from jax import lax
from jax.sharding import PartitionSpec as P

DMAX = 4
TILE = 8
CAP = 2
CHUNK = 32


LANES = 128
EXCHANGED = 2


def halve(x, axis, bit):
    count = lax.axis_size(axis)
    rows = x.shape[0] // 2
    upper = (lax.axis_index(axis) // bit) % 2
    keep = lax.dynamic_slice_in_dim(x, upper * rows, rows, 0)
    send = lax.dynamic_slice_in_dim(x, (1 - upper) * rows, rows, 0)
    return keep + lax.ppermute(send, axis, [(i, i ^ bit) for i in range(count)])


def double(x, axis, bit):
    count = lax.axis_size(axis)
    rows = x.shape[0]
    upper = (lax.axis_index(axis) // bit) % 2
    got = lax.ppermute(x, axis, [(i, i ^ bit) for i in range(count)])
    whole = jnp.zeros((2 * rows,) + x.shape[1:], x.dtype)
    whole = lax.dynamic_update_slice_in_dim(whole, x, upper * rows, 0)
    return lax.dynamic_update_slice_in_dim(whole, got, (1 - upper) * rows, 0)


def packed_sum(values, axes):
    steps = []
    rest = []
    for axis in axes:
        count = lax.axis_size(axis)
        if count & (count - 1):
            rest.append(axis)
            continue
        bit = 1
        while bit < count:
            steps.append((axis, bit))
            bit *= 2
    flat = jnp.concatenate([jnp.ravel(v).astype(jnp.float32) for v in values])
    unit = 8 * LANES * (2 ** len(steps))
    total = -(-flat.shape[0] // unit) * unit
    x = jnp.pad(flat, (0, total - flat.shape[0])).reshape(-1, LANES)
    halved = steps[: max(0, len(steps) - EXCHANGED)]
    for axis, bit in halved:
        x = halve(x, axis, bit)
    for axis, bit in steps[len(halved) :]:
        count = lax.axis_size(axis)
        x = x + lax.ppermute(x, axis, [(i, i ^ bit) for i in range(count)])
    if rest:
        x = lax.psum(x, tuple(rest))
    for axis, bit in reversed(halved):
        x = double(x, axis, bit)
    flat = x.reshape(-1)
    out = []
    offset = 0
    for v in values:
        out.append(flat[offset : offset + v.size].reshape(v.shape))
        offset += v.size
    return tuple(out)


def padded_2(cells, sides, width, closed):
    for axis, dim in sides:
        count = lax.axis_size(axis)
        ends = count if closed else count - 1
        head = lax.slice_in_dim(cells, 0, width, axis=dim)
        tail = lax.slice_in_dim(cells, cells.shape[dim] - width, cells.shape[dim], axis=dim)
        cells = jnp.concatenate(
            [
                lax.ppermute(tail, axis, [(i, (i + 1) % count) for i in range(ends)]),
                cells,
                lax.ppermute(head, axis, [((i + 1) % count, i) for i in range(ends)]),
            ],
            axis=dim,
        )
    return cells


def local(
    acts, rates, dw_kernel, pw_weight, head_weight, teacher_tiles, tile_dest, tile_start, tile_count
):
    micro_batch, band_rows, block_cols, width = acts.shape
    teach_width = head_weight.shape[1]
    lat_index = lax.axis_index("lat")
    lat_count = lax.axis_size("lat")
    lon_count = lax.axis_size("lon")
    devices = lon_count * lat_count
    lon_padded = padded_2(acts, (("lon", 2),), DMAX, True)
    padded = padded_2(lon_padded, (("lat", 1),), DMAX, False)
    tiles_here = teacher_tiles.shape[0]
    destination = tile_dest[:, 0]
    positions = jnp.arange(tiles_here, dtype=jnp.int32)
    same_dest = destination[:, None] == destination[None, :]
    earlier = positions[:, None] > positions[None, :]
    slot_rank = jnp.sum((same_dest & earlier).astype(jnp.int32), axis=1)
    slot_index = destination * CAP + slot_rank
    slots = devices * CAP
    base = 64
    blank = jnp.zeros_like(tile_count)
    column = jnp.stack(
        [tile_start // base, tile_start % base, tile_count] + [blank] * (TILE - 3), axis=1
    )
    packed = jnp.concatenate([teacher_tiles, column.astype(jnp.bfloat16)[:, :, None]], axis=2)
    chooser = (slot_index[None, :] == jnp.arange(slots, dtype=jnp.int32)[:, None]).astype(
        jnp.bfloat16
    )
    send = jnp.dot(
        chooser, packed.reshape(tiles_here, -1), preferred_element_type=jnp.float32
    ).astype(jnp.bfloat16)
    recv = lax.all_to_all(
        send.reshape(slots, TILE, teach_width + 1),
        ("lon", "lat"),
        split_axis=0,
        concat_axis=0,
        tiled=True,
    )
    recv_tiles = recv[:, :, :teach_width]
    meta = recv[:, :3, teach_width].astype(jnp.int32)
    recv_start = meta[:, 0] * base + meta[:, 1]
    recv_count = meta[:, 2]
    offsets = jnp.arange(TILE, dtype=jnp.int32)
    is_valid = offsets[None, :] < recv_count[:, None]
    sample_of = recv_start // (block_cols * band_rows)
    inner_row = recv_start // block_cols % band_rows
    first_col = recv_start % block_cols
    glob_row = lat_index * band_rows + inner_row
    area_weight = jnp.cos(
        jnp.pi * ((glob_row.astype(jnp.float32) + 0.5) / (band_rows * lat_count) - 0.5)
    )
    row_weight = jnp.where(is_valid, area_weight[:, None], jnp.float32(0.0)) / jnp.float32(
        devices * tiles_here * TILE
    )
    kernel = dw_kernel.astype(jnp.float32)
    onehot = (
        rates[None, :] == jnp.arange(1, DMAX + 1, dtype=jnp.int32)[:, None]
    ).astype(jnp.float32)
    span = 2 * DMAX + 1
    reach = TILE + 2 * DMAX

    def gather_windows(place):
        b, h, w = place
        return jax.vmap(
            lambda b, h, w: lax.dynamic_slice(
                padded, (b, h, w, jnp.int32(0)), (1, span, reach, width)
            )[0]
        )(b, h, w)

    def shifted(source, row_shift, col_shift):
        return source[:, DMAX + row_shift, DMAX + col_shift : DMAX + col_shift + TILE, :].astype(
            jnp.float32
        )

    def forward(windows, tiles, weight):
        center = shifted(windows, 0, 0)
        accum_sum = center * kernel[4]
        for dilation in range(1, DMAX + 1):
            for tap_index in range(9):
                if tap_index == 4:
                    continue
                row_shift = (tap_index // 3 - 1) * dilation
                col_shift = (tap_index % 3 - 1) * dilation
                accum_sum = accum_sum + kernel[tap_index] * onehot[dilation - 1] * shifted(
                    windows, row_shift, col_shift
                )
        depth_flat = accum_sum.astype(jnp.bfloat16).reshape(-1, width)
        preact = jnp.dot(depth_flat, pw_weight, preferred_element_type=jnp.float32)
        y_rows = (center.reshape(-1, width) + jax.nn.silu(preact)).astype(jnp.bfloat16)
        weight = weight.reshape(-1, 1)
        predicted = jnp.dot(y_rows, head_weight, preferred_element_type=jnp.float32)
        residual = predicted - tiles.reshape(-1, teach_width).astype(jnp.float32)
        loss_part = jnp.sum(weight * residual * residual)
        grad_pred = (2.0 * weight * residual).astype(jnp.bfloat16)
        head_part = lax.dot_general(
            y_rows, grad_pred, (((0,), (0,)), ((), ())), preferred_element_type=jnp.float32
        )
        grad_rows = jnp.dot(grad_pred, head_weight.T, preferred_element_type=jnp.float32)
        return depth_flat, preact, grad_rows, loss_part, head_part

    def backward(windows, depth_flat, grad_u):
        pw_part = lax.dot_general(
            depth_flat, grad_u, (((0,), (0,)), ((), ())), preferred_element_type=jnp.float32
        )
        grad_z = jnp.dot(grad_u, pw_weight.T, preferred_element_type=jnp.float32)
        grad_z = grad_z.reshape(windows.shape[0], TILE, width)
        tap_sums = []
        for tap_index in range(9):
            if tap_index == 4:
                part = shifted(windows, 0, 0) * grad_z
                tap_sums.append(jnp.sum(part.reshape(-1, width), axis=0))
                continue
            tap_sum = jnp.zeros((width,), jnp.float32)
            for dilation in range(1, DMAX + 1):
                row_shift = (tap_index // 3 - 1) * dilation
                col_shift = (tap_index % 3 - 1) * dilation
                part = shifted(windows, row_shift, col_shift) * grad_z
                part = jnp.sum(part.reshape(-1, width), axis=0)
                tap_sum = tap_sum + onehot[dilation - 1] * part
            tap_sums.append(tap_sum)
        return pw_part, jnp.stack(tap_sums, axis=0)

    slots = recv_start.shape[0]
    chunk = min(slots, CHUNK)
    chunks = slots // chunk
    place = (sample_of, inner_row, first_col)
    if chunks == 1:
        windows = gather_windows(place)
        depth_flat, preact, grad_rows, loss_sum, grad_head = forward(
            windows, recv_tiles, row_weight
        )
    else:
        split = lambda v: v.reshape((chunks, chunk) + v.shape[1:])
        outs = lax.map(
            lambda xs: forward(gather_windows(xs[0]), xs[1], xs[2]),
            (tuple(split(v) for v in place), split(recv_tiles), split(row_weight)),
        )
        depth_flat, preact, grad_rows = (v.reshape((-1, width)) for v in outs[:3])
        loss_sum, grad_head = jnp.sum(outs[3]), jnp.sum(outs[4], axis=0)
    cell = (recv_start[:, None] + offsets[None, :]).reshape(-1)
    row_ids = jnp.arange(cell.shape[0], dtype=jnp.int32)
    if cell.shape[0] <= 512:
        same_cell = cell[:, None] == cell[None, :]
        grad_y = jnp.dot(
            same_cell.astype(jnp.float32),
            grad_rows,
            precision=lax.Precision.HIGHEST,
            preferred_element_type=jnp.float32,
        )
        repeated = jnp.any(same_cell & (row_ids[None, :] < row_ids[:, None]), axis=1)
    else:
        cells_here = micro_batch * band_rows * block_cols
        grid = jnp.zeros((cells_here, width), jnp.float32).at[cell].add(grad_rows)
        grad_y = grid[cell]
        owner = jnp.full((cells_here,), cell.shape[0], jnp.int32).at[cell].min(row_ids)
        repeated = owner[cell] != row_ids
    sigmoid_u = jax.nn.sigmoid(preact)
    grad_u = (grad_y * sigmoid_u * (1.0 + preact * (1.0 - sigmoid_u))).astype(jnp.bfloat16)
    grad_u = jnp.where(repeated[:, None], jnp.zeros_like(grad_u), grad_u)
    if chunks == 1:
        windows_again, grad_u = lax.optimization_barrier((windows, grad_u))
        grad_pw, grad_dw = backward(windows_again, depth_flat, grad_u)
    else:
        rows_split = lambda v: v.reshape((chunks, chunk * TILE) + v.shape[1:])
        outs = lax.map(
            lambda xs: backward(gather_windows(xs[0]), xs[1], xs[2]),
            (tuple(split(v) for v in place), rows_split(depth_flat), rows_split(grad_u)),
        )
        grad_pw, grad_dw = jnp.sum(outs[0], axis=0), jnp.sum(outs[1], axis=0)
    grad_dw, grad_pw, grad_head, loss_sum = packed_sum(
        (grad_dw, grad_pw, grad_head, loss_sum), ("lat", "lon")
    )
    return (grad_dw, grad_pw, grad_head, (loss_sum / teach_width).reshape(1))


def solution(mesh):
    in_specs = (
        P("groups", "lat", "lon", None),
        P(),
        P(),
        P(),
        P(),
        P(("groups", "lon", "lat"), None, None),
        P(("groups", "lon", "lat"), None),
        P(("groups", "lon", "lat")),
        P(("groups", "lon", "lat")),
    )
    out_specs = (P("groups", None), P("groups", None), P("groups", None), P("groups"))
    return jax.shard_map(local, mesh=mesh, in_specs=in_specs, out_specs=out_specs, check_vma=False)
```

```python
import jax
import jax.numpy as jnp
from jax import lax
from jax.sharding import PartitionSpec as P

DMAX = 4
TILE = 8
CAP = 2
CHUNK = 32


LANES = 128
EXCHANGED = 2


def halve(x, axis, bit):
    count = lax.axis_size(axis)
    rows = x.shape[0] // 2
    upper = (lax.axis_index(axis) // bit) % 2
    keep = lax.dynamic_slice_in_dim(x, upper * rows, rows, 0)
    send = lax.dynamic_slice_in_dim(x, (1 - upper) * rows, rows, 0)
    return keep + lax.ppermute(send, axis, [(i, i ^ bit) for i in range(count)])


def double(x, axis, bit):
    count = lax.axis_size(axis)
    rows = x.shape[0]
    upper = (lax.axis_index(axis) // bit) % 2
    got = lax.ppermute(x, axis, [(i, i ^ bit) for i in range(count)])
    whole = jnp.zeros((2 * rows,) + x.shape[1:], x.dtype)
    whole = lax.dynamic_update_slice_in_dim(whole, x, upper * rows, 0)
    return lax.dynamic_update_slice_in_dim(whole, got, (1 - upper) * rows, 0)


def packed_sum(values, axes):
    steps = []
    rest = []
    for axis in axes:
        count = lax.axis_size(axis)
        if count & (count - 1):
            rest.append(axis)
            continue
        bit = 1
        while bit < count:
            steps.append((axis, bit))
            bit *= 2
    flat = jnp.concatenate([jnp.ravel(v).astype(jnp.float32) for v in values])
    unit = 8 * LANES * (2 ** len(steps))
    total = -(-flat.shape[0] // unit) * unit
    x = jnp.pad(flat, (0, total - flat.shape[0])).reshape(-1, LANES)
    halved = steps[: max(0, len(steps) - EXCHANGED)]
    for axis, bit in halved:
        x = halve(x, axis, bit)
    for axis, bit in steps[len(halved) :]:
        count = lax.axis_size(axis)
        x = x + lax.ppermute(x, axis, [(i, i ^ bit) for i in range(count)])
    if rest:
        x = lax.psum(x, tuple(rest))
    for axis, bit in reversed(halved):
        x = double(x, axis, bit)
    flat = x.reshape(-1)
    out = []
    offset = 0
    for v in values:
        out.append(flat[offset : offset + v.size].reshape(v.shape))
        offset += v.size
    return tuple(out)


def padded_2(cells, sides, width, closed):
    for axis, dim in sides:
        count = lax.axis_size(axis)
        ends = count if closed else count - 1
        head = lax.slice_in_dim(cells, 0, width, axis=dim)
        tail = lax.slice_in_dim(cells, cells.shape[dim] - width, cells.shape[dim], axis=dim)
        cells = jnp.concatenate(
            [
                lax.ppermute(tail, axis, [(i, (i + 1) % count) for i in range(ends)]),
                cells,
                lax.ppermute(head, axis, [((i + 1) % count, i) for i in range(ends)]),
            ],
            axis=dim,
        )
    return cells


def local(
    acts, rates, dw_kernel, pw_weight, head_weight, teacher_tiles, tile_dest, tile_start, tile_count
):
    micro_batch, band_rows, block_cols, width = acts.shape
    teach_width = head_weight.shape[1]
    lat_index = lax.axis_index("lat")
    lat_count = lax.axis_size("lat")
    lon_count = lax.axis_size("lon")
    devices = lon_count * lat_count
    lon_padded = padded_2(acts, (("lon", 2),), DMAX, True)
    tiles_here = teacher_tiles.shape[0]
    destination = tile_dest[:, 0]
    positions = jnp.arange(tiles_here, dtype=jnp.int32)
    same_dest = destination[:, None] == destination[None, :]
    earlier = positions[:, None] > positions[None, :]
    slot_rank = jnp.sum((same_dest & earlier).astype(jnp.int32), axis=1)
    slot_index = destination * CAP + slot_rank
    slots = devices * CAP
    base = 64
    blank = jnp.zeros_like(tile_count)
    column = jnp.stack(
        [tile_start // base, tile_start % base, tile_count] + [blank] * (TILE - 3), axis=1
    )
    packed = jnp.concatenate([teacher_tiles, column.astype(jnp.bfloat16)[:, :, None]], axis=2)
    chooser = (slot_index[None, :] == jnp.arange(slots, dtype=jnp.int32)[:, None]).astype(
        jnp.bfloat16
    )
    send = jnp.dot(
        chooser, packed.reshape(tiles_here, -1), preferred_element_type=jnp.float32
    ).astype(jnp.bfloat16)
    send, lon_padded = lax.optimization_barrier((send, lon_padded))
    padded = padded_2(lon_padded, (("lat", 1),), DMAX, False)
    recv = lax.all_to_all(
        send.reshape(slots, TILE, teach_width + 1),
        ("lon", "lat"),
        split_axis=0,
        concat_axis=0,
        tiled=True,
    )
    recv_tiles = recv[:, :, :teach_width]
    meta = recv[:, :3, teach_width].astype(jnp.int32)
    recv_start = meta[:, 0] * base + meta[:, 1]
    recv_count = meta[:, 2]
    offsets = jnp.arange(TILE, dtype=jnp.int32)
    is_valid = offsets[None, :] < recv_count[:, None]
    sample_of = recv_start // (block_cols * band_rows)
    inner_row = recv_start // block_cols % band_rows
    first_col = recv_start % block_cols
    glob_row = lat_index * band_rows + inner_row
    area_weight = jnp.cos(
        jnp.pi * ((glob_row.astype(jnp.float32) + 0.5) / (band_rows * lat_count) - 0.5)
    )
    row_weight = jnp.where(is_valid, area_weight[:, None], jnp.float32(0.0)) / jnp.float32(
        devices * tiles_here * TILE
    )
    kernel = dw_kernel.astype(jnp.float32)
    onehot = (
        rates[None, :] == jnp.arange(1, DMAX + 1, dtype=jnp.int32)[:, None]
    ).astype(jnp.float32)
    span = 2 * DMAX + 1
    reach = TILE + 2 * DMAX

    def gather_windows(place):
        b, h, w = place
        return jax.vmap(
            lambda b, h, w: lax.dynamic_slice(
                padded, (b, h, w, jnp.int32(0)), (1, span, reach, width)
            )[0]
        )(b, h, w)

    def shifted(source, row_shift, col_shift):
        return source[:, DMAX + row_shift, DMAX + col_shift : DMAX + col_shift + TILE, :].astype(
            jnp.float32
        )

    def forward(windows, tiles, weight):
        center = shifted(windows, 0, 0)
        accum_sum = center * kernel[4]
        for dilation in range(1, DMAX + 1):
            for tap_index in range(9):
                if tap_index == 4:
                    continue
                row_shift = (tap_index // 3 - 1) * dilation
                col_shift = (tap_index % 3 - 1) * dilation
                accum_sum = accum_sum + kernel[tap_index] * onehot[dilation - 1] * shifted(
                    windows, row_shift, col_shift
                )
        depth_flat = accum_sum.astype(jnp.bfloat16).reshape(-1, width)
        preact = jnp.dot(depth_flat, pw_weight, preferred_element_type=jnp.float32)
        y_rows = (center.reshape(-1, width) + jax.nn.silu(preact)).astype(jnp.bfloat16)
        weight = weight.reshape(-1, 1)
        predicted = jnp.dot(y_rows, head_weight, preferred_element_type=jnp.float32)
        residual = predicted - tiles.reshape(-1, teach_width).astype(jnp.float32)
        loss_part = jnp.sum(weight * residual * residual)
        grad_pred = (2.0 * weight * residual).astype(jnp.bfloat16)
        head_part = lax.dot_general(
            y_rows, grad_pred, (((0,), (0,)), ((), ())), preferred_element_type=jnp.float32
        )
        grad_rows = jnp.dot(grad_pred, head_weight.T, preferred_element_type=jnp.float32)
        return depth_flat, preact, grad_rows, loss_part, head_part

    def backward(windows, depth_flat, grad_u):
        pw_part = lax.dot_general(
            depth_flat, grad_u, (((0,), (0,)), ((), ())), preferred_element_type=jnp.float32
        )
        grad_z = jnp.dot(grad_u, pw_weight.T, preferred_element_type=jnp.float32)
        grad_z = grad_z.reshape(windows.shape[0], TILE, width)
        tap_sums = []
        for tap_index in range(9):
            if tap_index == 4:
                part = shifted(windows, 0, 0) * grad_z
                tap_sums.append(jnp.sum(part.reshape(-1, width), axis=0))
                continue
            tap_sum = jnp.zeros((width,), jnp.float32)
            for dilation in range(1, DMAX + 1):
                row_shift = (tap_index // 3 - 1) * dilation
                col_shift = (tap_index % 3 - 1) * dilation
                part = shifted(windows, row_shift, col_shift) * grad_z
                part = jnp.sum(part.reshape(-1, width), axis=0)
                tap_sum = tap_sum + onehot[dilation - 1] * part
            tap_sums.append(tap_sum)
        return pw_part, jnp.stack(tap_sums, axis=0)

    slots = recv_start.shape[0]
    chunk = min(slots, CHUNK)
    chunks = slots // chunk
    place = (sample_of, inner_row, first_col)
    if chunks == 1:
        windows = gather_windows(place)
        depth_flat, preact, grad_rows, loss_sum, grad_head = forward(
            windows, recv_tiles, row_weight
        )
    else:
        split = lambda v: v.reshape((chunks, chunk) + v.shape[1:])
        outs = lax.map(
            lambda xs: forward(gather_windows(xs[0]), xs[1], xs[2]),
            (tuple(split(v) for v in place), split(recv_tiles), split(row_weight)),
        )
        depth_flat, preact, grad_rows = (v.reshape((-1, width)) for v in outs[:3])
        loss_sum, grad_head = jnp.sum(outs[3]), jnp.sum(outs[4], axis=0)
    cell = (recv_start[:, None] + offsets[None, :]).reshape(-1)
    row_ids = jnp.arange(cell.shape[0], dtype=jnp.int32)
    if cell.shape[0] <= 512:
        same_cell = cell[:, None] == cell[None, :]
        grad_y = jnp.dot(
            same_cell.astype(jnp.float32),
            grad_rows,
            precision=lax.Precision.HIGHEST,
            preferred_element_type=jnp.float32,
        )
        repeated = jnp.any(same_cell & (row_ids[None, :] < row_ids[:, None]), axis=1)
    else:
        cells_here = micro_batch * band_rows * block_cols
        grid = jnp.zeros((cells_here, width), jnp.float32).at[cell].add(grad_rows)
        grad_y = grid[cell]
        owner = jnp.full((cells_here,), cell.shape[0], jnp.int32).at[cell].min(row_ids)
        repeated = owner[cell] != row_ids
    sigmoid_u = jax.nn.sigmoid(preact)
    grad_u = (grad_y * sigmoid_u * (1.0 + preact * (1.0 - sigmoid_u))).astype(jnp.bfloat16)
    grad_u = jnp.where(repeated[:, None], jnp.zeros_like(grad_u), grad_u)
    if chunks == 1:
        windows_again, grad_u = lax.optimization_barrier((windows, grad_u))
        grad_pw, grad_dw = backward(windows_again, depth_flat, grad_u)
    else:
        rows_split = lambda v: v.reshape((chunks, chunk * TILE) + v.shape[1:])
        outs = lax.map(
            lambda xs: backward(gather_windows(xs[0]), xs[1], xs[2]),
            (tuple(split(v) for v in place), rows_split(depth_flat), rows_split(grad_u)),
        )
        grad_pw, grad_dw = jnp.sum(outs[0], axis=0), jnp.sum(outs[1], axis=0)
    grad_dw, grad_pw, grad_head, loss_sum = packed_sum(
        (grad_dw, grad_pw, grad_head, loss_sum), ("lat", "lon")
    )
    return (grad_dw, grad_pw, grad_head, (loss_sum / teach_width).reshape(1))


def solution(mesh):
    in_specs = (
        P("groups", "lat", "lon", None),
        P(),
        P(),
        P(),
        P(),
        P(("groups", "lon", "lat"), None, None),
        P(("groups", "lon", "lat"), None),
        P(("groups", "lon", "lat")),
        P(("groups", "lon", "lat")),
    )
    out_specs = (P("groups", None), P("groups", None), P("groups", None), P("groups"))
    return jax.shard_map(local, mesh=mesh, in_specs=in_specs, out_specs=out_specs, check_vma=False)
```

```python
import jax
import jax.numpy as jnp
from jax import lax
from jax.sharding import PartitionSpec as P

DMAX = 4
TILE = 8
CAP = 2
CHUNK = 32


LANES = 128
EXCHANGED = 2


def halve(x, axis, bit):
    count = lax.axis_size(axis)
    rows = x.shape[0] // 2
    upper = (lax.axis_index(axis) // bit) % 2
    keep = lax.dynamic_slice_in_dim(x, upper * rows, rows, 0)
    send = lax.dynamic_slice_in_dim(x, (1 - upper) * rows, rows, 0)
    return keep + lax.ppermute(send, axis, [(i, i ^ bit) for i in range(count)])


def double(x, axis, bit):
    count = lax.axis_size(axis)
    rows = x.shape[0]
    upper = (lax.axis_index(axis) // bit) % 2
    got = lax.ppermute(x, axis, [(i, i ^ bit) for i in range(count)])
    whole = jnp.zeros((2 * rows,) + x.shape[1:], x.dtype)
    whole = lax.dynamic_update_slice_in_dim(whole, x, upper * rows, 0)
    return lax.dynamic_update_slice_in_dim(whole, got, (1 - upper) * rows, 0)


def packed_sum(values, axes):
    steps = []
    rest = []
    for axis in axes:
        count = lax.axis_size(axis)
        if count & (count - 1):
            rest.append(axis)
            continue
        bit = 1
        while bit < count:
            steps.append((axis, bit))
            bit *= 2
    flat = jnp.concatenate([jnp.ravel(v).astype(jnp.float32) for v in values])
    unit = 8 * LANES * (2 ** len(steps))
    total = -(-flat.shape[0] // unit) * unit
    x = jnp.pad(flat, (0, total - flat.shape[0])).reshape(-1, LANES)
    halved = steps[: max(0, len(steps) - EXCHANGED)]
    for axis, bit in halved:
        x = halve(x, axis, bit)
    for axis, bit in steps[len(halved) :]:
        count = lax.axis_size(axis)
        x = x + lax.ppermute(x, axis, [(i, i ^ bit) for i in range(count)])
    if rest:
        x = lax.psum(x, tuple(rest))
    for axis, bit in reversed(halved):
        x = double(x, axis, bit)
    flat = x.reshape(-1)
    out = []
    offset = 0
    for v in values:
        out.append(flat[offset : offset + v.size].reshape(v.shape))
        offset += v.size
    return tuple(out)


def padded_2(cells, sides, width, closed):
    for axis, dim in sides:
        count = lax.axis_size(axis)
        ends = count if closed else count - 1
        head = lax.slice_in_dim(cells, 0, width, axis=dim)
        tail = lax.slice_in_dim(cells, cells.shape[dim] - width, cells.shape[dim], axis=dim)
        cells = jnp.concatenate(
            [
                lax.ppermute(tail, axis, [(i, (i + 1) % count) for i in range(ends)]),
                cells,
                lax.ppermute(head, axis, [((i + 1) % count, i) for i in range(ends)]),
            ],
            axis=dim,
        )
    return cells


def local(
    acts, rates, dw_kernel, pw_weight, head_weight, teacher_tiles, tile_dest, tile_start, tile_count
):
    micro_batch, band_rows, block_cols, width = acts.shape
    teach_width = head_weight.shape[1]
    lat_index = lax.axis_index("lat")
    lat_count = lax.axis_size("lat")
    lon_count = lax.axis_size("lon")
    devices = lon_count * lat_count
    lon_padded = padded_2(acts, (("lon", 2),), DMAX, True)
    padded = padded_2(lon_padded, (("lat", 1),), DMAX, False)
    tiles_here = teacher_tiles.shape[0]
    destination = tile_dest[:, 0]
    positions = jnp.arange(tiles_here, dtype=jnp.int32)
    same_dest = destination[:, None] == destination[None, :]
    earlier = positions[:, None] > positions[None, :]
    slot_rank = jnp.sum((same_dest & earlier).astype(jnp.int32), axis=1)
    slot_index = destination * CAP + slot_rank
    slots = devices * CAP
    base = 64
    blank = jnp.zeros_like(tile_count)
    column = jnp.stack(
        [tile_start // base, tile_start % base, tile_count] + [blank] * (TILE - 3), axis=1
    )
    packed = jnp.concatenate([teacher_tiles, column.astype(jnp.bfloat16)[:, :, None]], axis=2)
    chooser = (slot_index[None, :] == jnp.arange(slots, dtype=jnp.int32)[:, None]).astype(
        jnp.bfloat16
    )
    send = jnp.dot(
        chooser, packed.reshape(tiles_here, -1), preferred_element_type=jnp.float32
    ).astype(jnp.bfloat16)
    recv = lax.all_to_all(
        send.reshape(slots, TILE, teach_width + 1),
        ("lon", "lat"),
        split_axis=0,
        concat_axis=0,
        tiled=True,
    )
    recv_tiles = recv[:, :, :teach_width]
    meta = recv[:, :3, teach_width].astype(jnp.int32)
    recv_start = meta[:, 0] * base + meta[:, 1]
    recv_count = meta[:, 2]
    offsets = jnp.arange(TILE, dtype=jnp.int32)
    is_valid = offsets[None, :] < recv_count[:, None]
    sample_of = recv_start // (block_cols * band_rows)
    inner_row = recv_start // block_cols % band_rows
    first_col = recv_start % block_cols
    glob_row = lat_index * band_rows + inner_row
    area_weight = jnp.cos(
        jnp.pi * ((glob_row.astype(jnp.float32) + 0.5) / (band_rows * lat_count) - 0.5)
    )
    row_weight = jnp.where(is_valid, area_weight[:, None], jnp.float32(0.0)) / jnp.float32(
        devices * tiles_here * TILE
    )
    kernel = dw_kernel.astype(jnp.float32)
    onehot = (
        rates[None, :] == jnp.arange(1, DMAX + 1, dtype=jnp.int32)[:, None]
    ).astype(jnp.float32)
    span = 2 * DMAX + 1
    reach = TILE + 2 * DMAX

    def gather_windows(place):
        b, h, w = place
        return jax.vmap(
            lambda b, h, w: lax.dynamic_slice(
                padded, (b, h, w, jnp.int32(0)), (1, span, reach, width)
            )[0]
        )(b, h, w)

    def shifted(source, row_shift, col_shift):
        return source[:, DMAX + row_shift, DMAX + col_shift : DMAX + col_shift + TILE, :].astype(
            jnp.float32
        )

    def forward(windows, tiles, weight):
        center = shifted(windows, 0, 0)
        accum_sum = center * kernel[4]
        for dilation in range(1, DMAX + 1):
            for tap_index in range(9):
                if tap_index == 4:
                    continue
                row_shift = (tap_index // 3 - 1) * dilation
                col_shift = (tap_index % 3 - 1) * dilation
                accum_sum = accum_sum + kernel[tap_index] * onehot[dilation - 1] * shifted(
                    windows, row_shift, col_shift
                )
        depth_flat = accum_sum.astype(jnp.bfloat16).reshape(-1, width)
        preact = jnp.dot(depth_flat, pw_weight, preferred_element_type=jnp.float32)
        y_rows = (center.reshape(-1, width) + jax.nn.silu(preact)).astype(jnp.bfloat16)
        weight = weight.reshape(-1, 1)
        predicted = jnp.dot(y_rows, head_weight, preferred_element_type=jnp.float32)
        residual = predicted - tiles.reshape(-1, teach_width).astype(jnp.float32)
        loss_part = jnp.sum(weight * residual * residual)
        grad_pred = (2.0 * weight * residual).astype(jnp.bfloat16)
        head_part = lax.dot_general(
            y_rows, grad_pred, (((0,), (0,)), ((), ())), preferred_element_type=jnp.float32
        )
        grad_rows = jnp.dot(grad_pred, head_weight.T, preferred_element_type=jnp.float32)
        return depth_flat, preact, grad_rows, loss_part, head_part

    def backward(windows, depth_flat, grad_u):
        pw_part = lax.dot_general(
            depth_flat, grad_u, (((0,), (0,)), ((), ())), preferred_element_type=jnp.float32
        )
        grad_z = jnp.dot(grad_u, pw_weight.T, preferred_element_type=jnp.float32)
        grad_z = grad_z.reshape(windows.shape[0], TILE, width)
        tap_sums = []
        for tap_index in range(9):
            if tap_index == 4:
                part = shifted(windows, 0, 0) * grad_z
                tap_sums.append(jnp.sum(part.reshape(-1, width), axis=0))
                continue
            tap_sum = jnp.zeros((width,), jnp.float32)
            for dilation in range(1, DMAX + 1):
                row_shift = (tap_index // 3 - 1) * dilation
                col_shift = (tap_index % 3 - 1) * dilation
                part = shifted(windows, row_shift, col_shift) * grad_z
                part = jnp.sum(part.reshape(-1, width), axis=0)
                tap_sum = tap_sum + onehot[dilation - 1] * part
            tap_sums.append(tap_sum)
        return pw_part, jnp.stack(tap_sums, axis=0)

    slots = recv_start.shape[0]
    chunk = min(slots, CHUNK)
    chunks = slots // chunk
    place = (sample_of, inner_row, first_col)
    if chunks == 1:
        windows = gather_windows(place)
        depth_flat, preact, grad_rows, loss_sum, grad_head = forward(
            windows, recv_tiles, row_weight
        )
    else:
        split = lambda v: v.reshape((chunks, chunk) + v.shape[1:])
        outs = lax.map(
            lambda xs: forward(gather_windows(xs[0]), xs[1], xs[2]),
            (tuple(split(v) for v in place), split(recv_tiles), split(row_weight)),
        )
        depth_flat, preact, grad_rows = (v.reshape((-1, width)) for v in outs[:3])
        loss_sum, grad_head = jnp.sum(outs[3]), jnp.sum(outs[4], axis=0)
    cell = (recv_start[:, None] + offsets[None, :]).reshape(-1)
    row_ids = jnp.arange(cell.shape[0], dtype=jnp.int32)
    if cell.shape[0] <= 512:
        same_cell = cell[:, None] == cell[None, :]
        grad_y = jnp.dot(
            same_cell.astype(jnp.float32),
            grad_rows,
            precision=lax.Precision.HIGHEST,
            preferred_element_type=jnp.float32,
        )
        repeated = jnp.any(same_cell & (row_ids[None, :] < row_ids[:, None]), axis=1)
    else:
        cells_here = micro_batch * band_rows * block_cols
        grid = jnp.zeros((cells_here, width), jnp.float32).at[cell].add(grad_rows)
        grad_y = grid[cell]
        owner = jnp.full((cells_here,), cell.shape[0], jnp.int32).at[cell].min(row_ids)
        repeated = owner[cell] != row_ids
    sigmoid_u = jax.nn.sigmoid(preact)
    grad_u = (grad_y * sigmoid_u * (1.0 + preact * (1.0 - sigmoid_u))).astype(jnp.bfloat16)
    grad_u = jnp.where(repeated[:, None], jnp.zeros_like(grad_u), grad_u)
    if chunks == 1:
        windows_again, grad_u = lax.optimization_barrier((windows, grad_u))
        grad_pw, grad_dw = backward(windows_again, depth_flat, grad_u)
    else:
        rows_split = lambda v: v.reshape((chunks, chunk * TILE) + v.shape[1:])
        outs = lax.map(
            lambda xs: backward(gather_windows(xs[0]), xs[1], xs[2]),
            (tuple(split(v) for v in place), rows_split(depth_flat), rows_split(grad_u)),
        )
        grad_pw, grad_dw = jnp.sum(outs[0], axis=0), jnp.sum(outs[1], axis=0)
    grad_pw, grad_head, grad_dw, loss_sum = packed_sum(
        (grad_pw, grad_head, grad_dw, loss_sum), ("lat", "lon")
    )
    return (grad_dw, grad_pw, grad_head, (loss_sum / teach_width).reshape(1))


def solution(mesh):
    in_specs = (
        P("groups", "lat", "lon", None),
        P(),
        P(),
        P(),
        P(),
        P(("groups", "lon", "lat"), None, None),
        P(("groups", "lon", "lat"), None),
        P(("groups", "lon", "lat")),
        P(("groups", "lon", "lat")),
    )
    out_specs = (P("groups", None), P("groups", None), P("groups", None), P("groups"))
    return jax.shard_map(local, mesh=mesh, in_specs=in_specs, out_specs=out_specs, check_vma=False)
```

```python
import jax
import jax.numpy as jnp
from jax import lax
from jax.sharding import PartitionSpec as P

DMAX = 4
TILE = 8
CAP = 2
CHUNK = 32


LANES = 128
EXCHANGED = 2


def halve(x, axis, bit):
    count = lax.axis_size(axis)
    rows = x.shape[0] // 2
    upper = (lax.axis_index(axis) // bit) % 2
    keep = lax.dynamic_slice_in_dim(x, upper * rows, rows, 0)
    send = lax.dynamic_slice_in_dim(x, (1 - upper) * rows, rows, 0)
    return keep + lax.ppermute(send, axis, [(i, i ^ bit) for i in range(count)])


def double(x, axis, bit):
    count = lax.axis_size(axis)
    rows = x.shape[0]
    upper = (lax.axis_index(axis) // bit) % 2
    got = lax.ppermute(x, axis, [(i, i ^ bit) for i in range(count)])
    whole = jnp.zeros((2 * rows,) + x.shape[1:], x.dtype)
    whole = lax.dynamic_update_slice_in_dim(whole, x, upper * rows, 0)
    return lax.dynamic_update_slice_in_dim(whole, got, (1 - upper) * rows, 0)


def packed_sum(values, axes):
    steps = []
    rest = []
    for axis in axes:
        count = lax.axis_size(axis)
        if count & (count - 1):
            rest.append(axis)
            continue
        bit = 1
        while bit < count:
            steps.append((axis, bit))
            bit *= 2
    flat = jnp.concatenate([jnp.ravel(v).astype(jnp.float32) for v in values])
    unit = 8 * LANES * (2 ** len(steps))
    total = -(-flat.shape[0] // unit) * unit
    x = jnp.pad(flat, (0, total - flat.shape[0])).reshape(-1, LANES)
    halved = steps[: max(0, len(steps) - EXCHANGED)]
    for axis, bit in halved:
        x = halve(x, axis, bit)
    for axis, bit in steps[len(halved) :]:
        count = lax.axis_size(axis)
        x = x + lax.ppermute(x, axis, [(i, i ^ bit) for i in range(count)])
    if rest:
        x = lax.psum(x, tuple(rest))
    for axis, bit in reversed(halved):
        x = double(x, axis, bit)
    flat = x.reshape(-1)
    out = []
    offset = 0
    for v in values:
        out.append(flat[offset : offset + v.size].reshape(v.shape))
        offset += v.size
    return tuple(out)


def padded_2(cells, sides, width, closed):
    for axis, dim in sides:
        count = lax.axis_size(axis)
        ends = count if closed else count - 1
        head = lax.slice_in_dim(cells, 0, width, axis=dim)
        tail = lax.slice_in_dim(cells, cells.shape[dim] - width, cells.shape[dim], axis=dim)
        cells = jnp.concatenate(
            [
                lax.ppermute(tail, axis, [(i, (i + 1) % count) for i in range(ends)]),
                cells,
                lax.ppermute(head, axis, [((i + 1) % count, i) for i in range(ends)]),
            ],
            axis=dim,
        )
    return cells


def local(
    acts, rates, dw_kernel, pw_weight, head_weight, teacher_tiles, tile_dest, tile_start, tile_count
):
    micro_batch, band_rows, block_cols, width = acts.shape
    teach_width = head_weight.shape[1]
    lat_index = lax.axis_index("lat")
    lat_count = lax.axis_size("lat")
    lon_count = lax.axis_size("lon")
    devices = lon_count * lat_count
    lon_padded = padded_2(acts, (("lon", 2),), DMAX, True)
    padded = padded_2(lon_padded, (("lat", 1),), DMAX, False)
    tiles_here = teacher_tiles.shape[0]
    destination = tile_dest[:, 0]
    positions = jnp.arange(tiles_here, dtype=jnp.int32)
    same_dest = destination[:, None] == destination[None, :]
    earlier = positions[:, None] > positions[None, :]
    slot_rank = jnp.sum((same_dest & earlier).astype(jnp.int32), axis=1)
    slot_index = destination * CAP + slot_rank
    slots = devices * CAP
    base = 64
    blank = jnp.zeros_like(tile_count)
    column = jnp.stack(
        [tile_start // base, tile_start % base, tile_count] + [blank] * (TILE - 3), axis=1
    )
    packed = jnp.concatenate([teacher_tiles, column.astype(jnp.bfloat16)[:, :, None]], axis=2)
    chooser = (slot_index[None, :] == jnp.arange(slots, dtype=jnp.int32)[:, None]).astype(
        jnp.bfloat16
    )
    send = jnp.dot(
        chooser, packed.reshape(tiles_here, -1), preferred_element_type=jnp.float32
    ).astype(jnp.bfloat16)
    recv = lax.all_to_all(
        send.reshape(slots, TILE, teach_width + 1),
        ("lon", "lat"),
        split_axis=0,
        concat_axis=0,
        tiled=True,
    )
    recv_tiles = recv[:, :, :teach_width]
    meta = recv[:, :3, teach_width].astype(jnp.int32)
    recv_start = meta[:, 0] * base + meta[:, 1]
    recv_count = meta[:, 2]
    offsets = jnp.arange(TILE, dtype=jnp.int32)
    is_valid = offsets[None, :] < recv_count[:, None]
    sample_of = recv_start // (block_cols * band_rows)
    inner_row = recv_start // block_cols % band_rows
    first_col = recv_start % block_cols
    glob_row = lat_index * band_rows + inner_row
    area_weight = jnp.cos(
        jnp.pi * ((glob_row.astype(jnp.float32) + 0.5) / (band_rows * lat_count) - 0.5)
    )
    row_weight = jnp.where(is_valid, area_weight[:, None], jnp.float32(0.0)) / jnp.float32(
        devices * tiles_here * TILE
    )
    kernel = dw_kernel.astype(jnp.float32)
    onehot = (
        rates[None, :] == jnp.arange(1, DMAX + 1, dtype=jnp.int32)[:, None]
    ).astype(jnp.float32)
    span = 2 * DMAX + 1
    reach = TILE + 2 * DMAX

    def gather_windows(place):
        b, h, w = place
        return jax.vmap(
            lambda b, h, w: lax.dynamic_slice(
                padded, (b, h, w, jnp.int32(0)), (1, span, reach, width)
            )[0]
        )(b, h, w)

    def shifted(source, row_shift, col_shift):
        return source[:, DMAX + row_shift, DMAX + col_shift : DMAX + col_shift + TILE, :].astype(
            jnp.float32
        )

    def forward(windows, tiles, weight):
        center = shifted(windows, 0, 0)
        accum_sum = center * kernel[4]
        for dilation in range(1, DMAX + 1):
            for tap_index in range(9):
                if tap_index == 4:
                    continue
                row_shift = (tap_index // 3 - 1) * dilation
                col_shift = (tap_index % 3 - 1) * dilation
                accum_sum = accum_sum + kernel[tap_index] * onehot[dilation - 1] * shifted(
                    windows, row_shift, col_shift
                )
        depth_flat = accum_sum.astype(jnp.bfloat16).reshape(-1, width)
        preact = jnp.dot(depth_flat, pw_weight, preferred_element_type=jnp.float32)
        y_rows = (center.reshape(-1, width) + jax.nn.silu(preact)).astype(jnp.bfloat16)
        weight = weight.reshape(-1, 1)
        predicted = jnp.dot(y_rows, head_weight, preferred_element_type=jnp.float32)
        residual = predicted - tiles.reshape(-1, teach_width).astype(jnp.float32)
        loss_part = jnp.sum(weight * residual * residual)
        grad_pred = (2.0 * weight * residual).astype(jnp.bfloat16)
        head_part = lax.dot_general(
            y_rows, grad_pred, (((0,), (0,)), ((), ())), preferred_element_type=jnp.float32
        )
        grad_rows = jnp.dot(grad_pred, head_weight.T, preferred_element_type=jnp.float32)
        return depth_flat, preact, grad_rows, loss_part, head_part

    def backward(windows, depth_flat, grad_u):
        pw_part = lax.dot_general(
            depth_flat, grad_u, (((0,), (0,)), ((), ())), preferred_element_type=jnp.float32
        )
        grad_z = jnp.dot(grad_u, pw_weight.T, preferred_element_type=jnp.float32)
        grad_z = grad_z.reshape(windows.shape[0], TILE, width)
        tap_sums = []
        for tap_index in range(9):
            if tap_index == 4:
                chosen = shifted(windows, 0, 0)
            else:
                chosen = None
                for dilation in range(1, DMAX + 1):
                    row_shift = (tap_index // 3 - 1) * dilation
                    col_shift = (tap_index % 3 - 1) * dilation
                    term = onehot[dilation - 1] * shifted(windows, row_shift, col_shift)
                    chosen = term if chosen is None else chosen + term
            tap_sums.append(jnp.sum((chosen * grad_z).reshape(-1, width), axis=0))
        return pw_part, jnp.stack(tap_sums, axis=0)

    slots = recv_start.shape[0]
    chunk = min(slots, CHUNK)
    chunks = slots // chunk
    place = (sample_of, inner_row, first_col)
    if chunks == 1:
        windows = gather_windows(place)
        depth_flat, preact, grad_rows, loss_sum, grad_head = forward(
            windows, recv_tiles, row_weight
        )
    else:
        split = lambda v: v.reshape((chunks, chunk) + v.shape[1:])
        outs = lax.map(
            lambda xs: forward(gather_windows(xs[0]), xs[1], xs[2]),
            (tuple(split(v) for v in place), split(recv_tiles), split(row_weight)),
        )
        depth_flat, preact, grad_rows = (v.reshape((-1, width)) for v in outs[:3])
        loss_sum, grad_head = jnp.sum(outs[3]), jnp.sum(outs[4], axis=0)
    cell = (recv_start[:, None] + offsets[None, :]).reshape(-1)
    row_ids = jnp.arange(cell.shape[0], dtype=jnp.int32)
    if cell.shape[0] <= 512:
        same_cell = cell[:, None] == cell[None, :]
        grad_y = jnp.dot(
            same_cell.astype(jnp.float32),
            grad_rows,
            precision=lax.Precision.HIGHEST,
            preferred_element_type=jnp.float32,
        )
        repeated = jnp.any(same_cell & (row_ids[None, :] < row_ids[:, None]), axis=1)
    else:
        cells_here = micro_batch * band_rows * block_cols
        grid = jnp.zeros((cells_here, width), jnp.float32).at[cell].add(grad_rows)
        grad_y = grid[cell]
        owner = jnp.full((cells_here,), cell.shape[0], jnp.int32).at[cell].min(row_ids)
        repeated = owner[cell] != row_ids
    sigmoid_u = jax.nn.sigmoid(preact)
    grad_u = (grad_y * sigmoid_u * (1.0 + preact * (1.0 - sigmoid_u))).astype(jnp.bfloat16)
    grad_u = jnp.where(repeated[:, None], jnp.zeros_like(grad_u), grad_u)
    if chunks == 1:
        windows_again, grad_u = lax.optimization_barrier((windows, grad_u))
        grad_pw, grad_dw = backward(windows_again, depth_flat, grad_u)
    else:
        rows_split = lambda v: v.reshape((chunks, chunk * TILE) + v.shape[1:])
        outs = lax.map(
            lambda xs: backward(gather_windows(xs[0]), xs[1], xs[2]),
            (tuple(split(v) for v in place), rows_split(depth_flat), rows_split(grad_u)),
        )
        grad_pw, grad_dw = jnp.sum(outs[0], axis=0), jnp.sum(outs[1], axis=0)
    grad_dw, grad_pw, grad_head, loss_sum = packed_sum(
        (grad_dw, grad_pw, grad_head, loss_sum), ("lat", "lon")
    )
    return (grad_dw, grad_pw, grad_head, (loss_sum / teach_width).reshape(1))


def solution(mesh):
    in_specs = (
        P("groups", "lat", "lon", None),
        P(),
        P(),
        P(),
        P(),
        P(("groups", "lon", "lat"), None, None),
        P(("groups", "lon", "lat"), None),
        P(("groups", "lon", "lat")),
        P(("groups", "lon", "lat")),
    )
    out_specs = (P("groups", None), P("groups", None), P("groups", None), P("groups"))
    return jax.shard_map(local, mesh=mesh, in_specs=in_specs, out_specs=out_specs, check_vma=False)
```

```python
import jax
import jax.numpy as jnp
from jax import lax
from jax.sharding import PartitionSpec as P

DMAX = 4
TILE = 8
CAP = 2
CHUNK = 32


LANES = 128
EXCHANGED = 2


def halve(x, axis, bit):
    count = lax.axis_size(axis)
    rows = x.shape[0] // 2
    upper = (lax.axis_index(axis) // bit) % 2
    keep = lax.dynamic_slice_in_dim(x, upper * rows, rows, 0)
    send = lax.dynamic_slice_in_dim(x, (1 - upper) * rows, rows, 0)
    return keep + lax.ppermute(send, axis, [(i, i ^ bit) for i in range(count)])


def double(x, axis, bit):
    count = lax.axis_size(axis)
    rows = x.shape[0]
    upper = (lax.axis_index(axis) // bit) % 2
    got = lax.ppermute(x, axis, [(i, i ^ bit) for i in range(count)])
    whole = jnp.zeros((2 * rows,) + x.shape[1:], x.dtype)
    whole = lax.dynamic_update_slice_in_dim(whole, x, upper * rows, 0)
    return lax.dynamic_update_slice_in_dim(whole, got, (1 - upper) * rows, 0)


def packed_sum(values, axes):
    steps = []
    rest = []
    for axis in axes:
        count = lax.axis_size(axis)
        if count & (count - 1):
            rest.append(axis)
            continue
        bit = 1
        while bit < count:
            steps.append((axis, bit))
            bit *= 2
    flat = jnp.concatenate([jnp.ravel(v).astype(jnp.float32) for v in values])
    unit = 8 * LANES * (2 ** len(steps))
    total = -(-flat.shape[0] // unit) * unit
    x = jnp.pad(flat, (0, total - flat.shape[0])).reshape(-1, LANES)
    halved = steps[: max(0, len(steps) - EXCHANGED)]
    for axis, bit in halved:
        x = halve(x, axis, bit)
    for axis, bit in steps[len(halved) :]:
        count = lax.axis_size(axis)
        x = x + lax.ppermute(x, axis, [(i, i ^ bit) for i in range(count)])
    if rest:
        x = lax.psum(x, tuple(rest))
    for axis, bit in reversed(halved):
        x = double(x, axis, bit)
    flat = x.reshape(-1)
    out = []
    offset = 0
    for v in values:
        out.append(flat[offset : offset + v.size].reshape(v.shape))
        offset += v.size
    return tuple(out)


def padded_2(cells, sides, width, closed):
    for axis, dim in sides:
        count = lax.axis_size(axis)
        ends = count if closed else count - 1
        head = lax.slice_in_dim(cells, 0, width, axis=dim)
        tail = lax.slice_in_dim(cells, cells.shape[dim] - width, cells.shape[dim], axis=dim)
        cells = jnp.concatenate(
            [
                lax.ppermute(tail, axis, [(i, (i + 1) % count) for i in range(ends)]),
                cells,
                lax.ppermute(head, axis, [((i + 1) % count, i) for i in range(ends)]),
            ],
            axis=dim,
        )
    return cells


def local(
    acts, rates, dw_kernel, pw_weight, head_weight, teacher_tiles, tile_dest, tile_start, tile_count
):
    micro_batch, band_rows, block_cols, width = acts.shape
    teach_width = head_weight.shape[1]
    lat_index = lax.axis_index("lat")
    lat_count = lax.axis_size("lat")
    lon_count = lax.axis_size("lon")
    devices = lon_count * lat_count
    lon_padded = padded_2(acts, (("lon", 2),), DMAX, True)
    padded = padded_2(lon_padded, (("lat", 1),), DMAX, False)
    tiles_here = teacher_tiles.shape[0]
    destination = tile_dest[:, 0]
    positions = jnp.arange(tiles_here, dtype=jnp.int32)
    same_dest = destination[:, None] == destination[None, :]
    earlier = positions[:, None] > positions[None, :]
    slot_rank = jnp.sum((same_dest & earlier).astype(jnp.int32), axis=1)
    slot_index = destination * CAP + slot_rank
    slots = devices * CAP
    base = 64
    blank = jnp.zeros_like(tile_count)
    column = jnp.stack(
        [tile_start // base, tile_start % base, tile_count] + [blank] * (TILE - 3), axis=1
    )
    packed = jnp.concatenate([teacher_tiles, column.astype(jnp.bfloat16)[:, :, None]], axis=2)
    chooser = (slot_index[None, :] == jnp.arange(slots, dtype=jnp.int32)[:, None]).astype(
        jnp.bfloat16
    )
    send = jnp.dot(
        chooser, packed.reshape(tiles_here, -1), preferred_element_type=jnp.float32
    ).astype(jnp.bfloat16)
    recv = lax.all_to_all(
        send.reshape(slots, TILE, teach_width + 1),
        ("lon", "lat"),
        split_axis=0,
        concat_axis=0,
        tiled=True,
    )
    recv_tiles = recv[:, :, :teach_width]
    meta = recv[:, :3, teach_width].astype(jnp.int32)
    recv_start = meta[:, 0] * base + meta[:, 1]
    recv_count = meta[:, 2]
    offsets = jnp.arange(TILE, dtype=jnp.int32)
    is_valid = offsets[None, :] < recv_count[:, None]
    sample_of = recv_start // (block_cols * band_rows)
    inner_row = recv_start // block_cols % band_rows
    first_col = recv_start % block_cols
    glob_row = lat_index * band_rows + inner_row
    area_weight = jnp.cos(
        jnp.pi * ((glob_row.astype(jnp.float32) + 0.5) / (band_rows * lat_count) - 0.5)
    )
    row_weight = jnp.where(is_valid, area_weight[:, None], jnp.float32(0.0)) / jnp.float32(
        devices * tiles_here * TILE
    )
    kernel = dw_kernel.astype(jnp.float32)
    onehot = (
        rates[None, :] == jnp.arange(1, DMAX + 1, dtype=jnp.int32)[:, None]
    ).astype(jnp.float32)
    span = 2 * DMAX + 1
    reach = TILE + 2 * DMAX

    def gather_windows(place):
        b, h, w = place
        return jax.vmap(
            lambda b, h, w: lax.dynamic_slice(
                padded, (b, h, w, jnp.int32(0)), (1, span, reach, width)
            )[0]
        )(b, h, w)

    def shifted(source, row_shift, col_shift):
        return source[:, DMAX + row_shift, DMAX + col_shift : DMAX + col_shift + TILE, :].astype(
            jnp.float32
        )

    def forward(windows, tiles, weight):
        center = shifted(windows, 0, 0)
        accum_sum = center * kernel[4]
        for dilation in range(1, DMAX + 1):
            for tap_index in range(9):
                if tap_index == 4:
                    continue
                row_shift = (tap_index // 3 - 1) * dilation
                col_shift = (tap_index % 3 - 1) * dilation
                accum_sum = accum_sum + kernel[tap_index] * onehot[dilation - 1] * shifted(
                    windows, row_shift, col_shift
                )
        depth_flat = accum_sum.astype(jnp.bfloat16).reshape(-1, width)
        preact = jnp.dot(depth_flat, pw_weight, preferred_element_type=jnp.float32)
        y_rows = (center.reshape(-1, width) + jax.nn.silu(preact)).astype(jnp.bfloat16)
        weight = weight.reshape(-1, 1)
        predicted = jnp.dot(y_rows, head_weight, preferred_element_type=jnp.float32)
        residual = predicted - tiles.reshape(-1, teach_width).astype(jnp.float32)
        loss_part = jnp.sum(weight * residual * residual)
        grad_pred = (2.0 * weight * residual).astype(jnp.bfloat16)
        head_part = lax.dot_general(
            grad_pred, y_rows, (((0,), (0,)), ((), ())), preferred_element_type=jnp.float32
        )
        grad_rows = jnp.dot(grad_pred, head_weight.T, preferred_element_type=jnp.float32)
        return depth_flat, preact, grad_rows, loss_part, head_part

    def backward(windows, depth_flat, grad_u):
        pw_part = lax.dot_general(
            depth_flat, grad_u, (((0,), (0,)), ((), ())), preferred_element_type=jnp.float32
        )
        grad_z = jnp.dot(grad_u, pw_weight.T, preferred_element_type=jnp.float32)
        grad_z = grad_z.reshape(windows.shape[0], TILE, width)
        tap_sums = []
        for tap_index in range(9):
            if tap_index == 4:
                chosen = shifted(windows, 0, 0)
            else:
                chosen = None
                for dilation in range(1, DMAX + 1):
                    row_shift = (tap_index // 3 - 1) * dilation
                    col_shift = (tap_index % 3 - 1) * dilation
                    term = onehot[dilation - 1] * shifted(windows, row_shift, col_shift)
                    chosen = term if chosen is None else chosen + term
            tap_sums.append(jnp.sum((chosen * grad_z).reshape(-1, width), axis=0))
        return pw_part, jnp.stack(tap_sums, axis=0)

    slots = recv_start.shape[0]
    chunk = min(slots, CHUNK)
    chunks = slots // chunk
    place = (sample_of, inner_row, first_col)
    if chunks == 1:
        windows = gather_windows(place)
        depth_flat, preact, grad_rows, loss_sum, grad_head = forward(
            windows, recv_tiles, row_weight
        )
    else:
        split = lambda v: v.reshape((chunks, chunk) + v.shape[1:])
        outs = lax.map(
            lambda xs: forward(gather_windows(xs[0]), xs[1], xs[2]),
            (tuple(split(v) for v in place), split(recv_tiles), split(row_weight)),
        )
        depth_flat, preact, grad_rows = (v.reshape((-1, width)) for v in outs[:3])
        loss_sum, grad_head = jnp.sum(outs[3]), jnp.sum(outs[4], axis=0)
    cell = (recv_start[:, None] + offsets[None, :]).reshape(-1)
    row_ids = jnp.arange(cell.shape[0], dtype=jnp.int32)
    if cell.shape[0] <= 512:
        same_cell = cell[:, None] == cell[None, :]
        grad_y = jnp.dot(
            same_cell.astype(jnp.float32),
            grad_rows,
            precision=lax.Precision.HIGHEST,
            preferred_element_type=jnp.float32,
        )
        repeated = jnp.any(same_cell & (row_ids[None, :] < row_ids[:, None]), axis=1)
    else:
        cells_here = micro_batch * band_rows * block_cols
        grid = jnp.zeros((cells_here, width), jnp.float32).at[cell].add(grad_rows)
        grad_y = grid[cell]
        owner = jnp.full((cells_here,), cell.shape[0], jnp.int32).at[cell].min(row_ids)
        repeated = owner[cell] != row_ids
    sigmoid_u = jax.nn.sigmoid(preact)
    grad_u = (grad_y * sigmoid_u * (1.0 + preact * (1.0 - sigmoid_u))).astype(jnp.bfloat16)
    grad_u = jnp.where(repeated[:, None], jnp.zeros_like(grad_u), grad_u)
    if chunks == 1:
        windows_again, grad_u = lax.optimization_barrier((windows, grad_u))
        grad_pw, grad_dw = backward(windows_again, depth_flat, grad_u)
    else:
        rows_split = lambda v: v.reshape((chunks, chunk * TILE) + v.shape[1:])
        outs = lax.map(
            lambda xs: backward(gather_windows(xs[0]), xs[1], xs[2]),
            (tuple(split(v) for v in place), rows_split(depth_flat), rows_split(grad_u)),
        )
        grad_pw, grad_dw = jnp.sum(outs[0], axis=0), jnp.sum(outs[1], axis=0)
    grad_dw, grad_pw, grad_head, loss_sum = packed_sum(
        (grad_dw, grad_pw, grad_head, loss_sum), ("lat", "lon")
    )
    grad_head = grad_head.T
    return (grad_dw, grad_pw, grad_head, (loss_sum / teach_width).reshape(1))


def solution(mesh):
    in_specs = (
        P("groups", "lat", "lon", None),
        P(),
        P(),
        P(),
        P(),
        P(("groups", "lon", "lat"), None, None),
        P(("groups", "lon", "lat"), None),
        P(("groups", "lon", "lat")),
        P(("groups", "lon", "lat")),
    )
    out_specs = (P("groups", None), P("groups", None), P("groups", None), P("groups"))
    return jax.shard_map(local, mesh=mesh, in_specs=in_specs, out_specs=out_specs, check_vma=False)
```

```python
import jax
import jax.numpy as jnp
from jax import lax
from jax.sharding import PartitionSpec as P

DMAX = 4
TILE = 8
CAP = 2
CHUNK = 32


LANES = 128
EXCHANGED = 2


def halve(x, axis, bit):
    count = lax.axis_size(axis)
    rows = x.shape[0] // 2
    upper = (lax.axis_index(axis) // bit) % 2
    keep = lax.dynamic_slice_in_dim(x, upper * rows, rows, 0)
    send = lax.dynamic_slice_in_dim(x, (1 - upper) * rows, rows, 0)
    return keep + lax.ppermute(send, axis, [(i, i ^ bit) for i in range(count)])


def double(x, axis, bit):
    count = lax.axis_size(axis)
    rows = x.shape[0]
    upper = (lax.axis_index(axis) // bit) % 2
    got = lax.ppermute(x, axis, [(i, i ^ bit) for i in range(count)])
    whole = jnp.zeros((2 * rows,) + x.shape[1:], x.dtype)
    whole = lax.dynamic_update_slice_in_dim(whole, x, upper * rows, 0)
    return lax.dynamic_update_slice_in_dim(whole, got, (1 - upper) * rows, 0)


def packed_sum(values, axes):
    steps = []
    rest = []
    for axis in axes:
        count = lax.axis_size(axis)
        if count & (count - 1):
            rest.append(axis)
            continue
        bit = 1
        while bit < count:
            steps.append((axis, bit))
            bit *= 2
    flat = jnp.concatenate([jnp.ravel(v).astype(jnp.float32) for v in values])
    unit = 8 * LANES * (2 ** len(steps))
    total = -(-flat.shape[0] // unit) * unit
    x = jnp.pad(flat, (0, total - flat.shape[0])).reshape(-1, LANES)
    halved = steps[: max(0, len(steps) - EXCHANGED)]
    for axis, bit in halved:
        x = halve(x, axis, bit)
    for axis, bit in steps[len(halved) :]:
        count = lax.axis_size(axis)
        x = x + lax.ppermute(x, axis, [(i, i ^ bit) for i in range(count)])
    if rest:
        x = lax.psum(x, tuple(rest))
    for axis, bit in reversed(halved):
        x = double(x, axis, bit)
    flat = x.reshape(-1)
    out = []
    offset = 0
    for v in values:
        out.append(flat[offset : offset + v.size].reshape(v.shape))
        offset += v.size
    return tuple(out)


def padded_2(cells, sides, width, closed):
    for axis, dim in sides:
        count = lax.axis_size(axis)
        ends = count if closed else count - 1
        head = lax.slice_in_dim(cells, 0, width, axis=dim)
        tail = lax.slice_in_dim(cells, cells.shape[dim] - width, cells.shape[dim], axis=dim)
        cells = jnp.concatenate(
            [
                lax.ppermute(tail, axis, [(i, (i + 1) % count) for i in range(ends)]),
                cells,
                lax.ppermute(head, axis, [((i + 1) % count, i) for i in range(ends)]),
            ],
            axis=dim,
        )
    return cells


def local(
    acts, rates, dw_kernel, pw_weight, head_weight, teacher_tiles, tile_dest, tile_start, tile_count
):
    micro_batch, band_rows, block_cols, width = acts.shape
    teach_width = head_weight.shape[1]
    lat_index = lax.axis_index("lat")
    lat_count = lax.axis_size("lat")
    lon_count = lax.axis_size("lon")
    devices = lon_count * lat_count
    lon_padded = padded_2(acts, (("lon", 2),), DMAX, True)
    padded = padded_2(lon_padded, (("lat", 1),), DMAX, False)
    tiles_here = teacher_tiles.shape[0]
    destination = tile_dest[:, 0]
    positions = jnp.arange(tiles_here, dtype=jnp.int32)
    same_dest = destination[:, None] == destination[None, :]
    earlier = positions[:, None] > positions[None, :]
    slot_rank = jnp.sum((same_dest & earlier).astype(jnp.int32), axis=1)
    slot_index = destination * CAP + slot_rank
    slots = devices * CAP
    base = 64
    blank = jnp.zeros_like(tile_count)
    column = jnp.stack(
        [tile_start // base, tile_start % base, tile_count] + [blank] * (TILE - 3), axis=1
    )
    packed = jnp.concatenate([teacher_tiles, column.astype(jnp.bfloat16)[:, :, None]], axis=2)
    chooser = (slot_index[None, :] == jnp.arange(slots, dtype=jnp.int32)[:, None]).astype(
        jnp.bfloat16
    )
    send = jnp.einsum(
        "st,tre->sre", chooser, packed, preferred_element_type=jnp.float32
    ).astype(jnp.bfloat16)
    recv = lax.all_to_all(send, ("lon", "lat"), split_axis=0, concat_axis=0, tiled=True)
    recv_tiles = recv[:, :, :teach_width]
    meta = recv[:, :3, teach_width].astype(jnp.int32)
    recv_start = meta[:, 0] * base + meta[:, 1]
    recv_count = meta[:, 2]
    offsets = jnp.arange(TILE, dtype=jnp.int32)
    is_valid = offsets[None, :] < recv_count[:, None]
    sample_of = recv_start // (block_cols * band_rows)
    inner_row = recv_start // block_cols % band_rows
    first_col = recv_start % block_cols
    glob_row = lat_index * band_rows + inner_row
    area_weight = jnp.cos(
        jnp.pi * ((glob_row.astype(jnp.float32) + 0.5) / (band_rows * lat_count) - 0.5)
    )
    row_weight = jnp.where(is_valid, area_weight[:, None], jnp.float32(0.0)) / jnp.float32(
        devices * tiles_here * TILE
    )
    kernel = dw_kernel.astype(jnp.float32)
    onehot = (
        rates[None, :] == jnp.arange(1, DMAX + 1, dtype=jnp.int32)[:, None]
    ).astype(jnp.float32)
    span = 2 * DMAX + 1
    reach = TILE + 2 * DMAX

    def gather_windows(place):
        b, h, w = place
        return jax.vmap(
            lambda b, h, w: lax.dynamic_slice(
                padded, (b, h, w, jnp.int32(0)), (1, span, reach, width)
            )[0]
        )(b, h, w)

    def shifted(source, row_shift, col_shift):
        return source[:, DMAX + row_shift, DMAX + col_shift : DMAX + col_shift + TILE, :].astype(
            jnp.float32
        )

    def forward(windows, tiles, weight):
        center = shifted(windows, 0, 0)
        accum_sum = center * kernel[4]
        for dilation in range(1, DMAX + 1):
            for tap_index in range(9):
                if tap_index == 4:
                    continue
                row_shift = (tap_index // 3 - 1) * dilation
                col_shift = (tap_index % 3 - 1) * dilation
                accum_sum = accum_sum + kernel[tap_index] * onehot[dilation - 1] * shifted(
                    windows, row_shift, col_shift
                )
        depth_flat = accum_sum.astype(jnp.bfloat16).reshape(-1, width)
        preact = jnp.dot(depth_flat, pw_weight, preferred_element_type=jnp.float32)
        y_rows = (center.reshape(-1, width) + jax.nn.silu(preact)).astype(jnp.bfloat16)
        weight = weight.reshape(-1, 1)
        predicted = jnp.dot(y_rows, head_weight, preferred_element_type=jnp.float32)
        residual = predicted - tiles.reshape(-1, teach_width).astype(jnp.float32)
        loss_part = jnp.sum(weight * residual * residual)
        grad_pred = (2.0 * weight * residual).astype(jnp.bfloat16)
        head_part = lax.dot_general(
            grad_pred, y_rows, (((0,), (0,)), ((), ())), preferred_element_type=jnp.float32
        )
        grad_rows = jnp.dot(grad_pred, head_weight.T, preferred_element_type=jnp.float32)
        return depth_flat, preact, grad_rows, loss_part, head_part

    def backward(windows, depth_flat, grad_u):
        pw_part = lax.dot_general(
            depth_flat, grad_u, (((0,), (0,)), ((), ())), preferred_element_type=jnp.float32
        )
        grad_z = jnp.dot(grad_u, pw_weight.T, preferred_element_type=jnp.float32)
        grad_z = grad_z.reshape(windows.shape[0], TILE, width)
        tap_sums = []
        for tap_index in range(9):
            if tap_index == 4:
                chosen = shifted(windows, 0, 0)
            else:
                chosen = None
                for dilation in range(1, DMAX + 1):
                    row_shift = (tap_index // 3 - 1) * dilation
                    col_shift = (tap_index % 3 - 1) * dilation
                    term = onehot[dilation - 1] * shifted(windows, row_shift, col_shift)
                    chosen = term if chosen is None else chosen + term
            tap_sums.append(jnp.sum((chosen * grad_z).reshape(-1, width), axis=0))
        return pw_part, jnp.stack(tap_sums, axis=0)

    slots = recv_start.shape[0]
    chunk = min(slots, CHUNK)
    chunks = slots // chunk
    place = (sample_of, inner_row, first_col)
    if chunks == 1:
        windows = gather_windows(place)
        depth_flat, preact, grad_rows, loss_sum, grad_head = forward(
            windows, recv_tiles, row_weight
        )
    else:
        split = lambda v: v.reshape((chunks, chunk) + v.shape[1:])
        outs = lax.map(
            lambda xs: forward(gather_windows(xs[0]), xs[1], xs[2]),
            (tuple(split(v) for v in place), split(recv_tiles), split(row_weight)),
        )
        depth_flat, preact, grad_rows = (v.reshape((-1, width)) for v in outs[:3])
        loss_sum, grad_head = jnp.sum(outs[3]), jnp.sum(outs[4], axis=0)
    cell = (recv_start[:, None] + offsets[None, :]).reshape(-1)
    row_ids = jnp.arange(cell.shape[0], dtype=jnp.int32)
    if cell.shape[0] <= 512:
        same_cell = cell[:, None] == cell[None, :]
        grad_y = jnp.dot(
            same_cell.astype(jnp.float32),
            grad_rows,
            precision=lax.Precision.HIGHEST,
            preferred_element_type=jnp.float32,
        )
        repeated = jnp.any(same_cell & (row_ids[None, :] < row_ids[:, None]), axis=1)
    else:
        cells_here = micro_batch * band_rows * block_cols
        grid = jnp.zeros((cells_here, width), jnp.float32).at[cell].add(grad_rows)
        grad_y = grid[cell]
        owner = jnp.full((cells_here,), cell.shape[0], jnp.int32).at[cell].min(row_ids)
        repeated = owner[cell] != row_ids
    sigmoid_u = jax.nn.sigmoid(preact)
    grad_u = (grad_y * sigmoid_u * (1.0 + preact * (1.0 - sigmoid_u))).astype(jnp.bfloat16)
    grad_u = jnp.where(repeated[:, None], jnp.zeros_like(grad_u), grad_u)
    if chunks == 1:
        windows_again, grad_u = lax.optimization_barrier((windows, grad_u))
        grad_pw, grad_dw = backward(windows_again, depth_flat, grad_u)
    else:
        rows_split = lambda v: v.reshape((chunks, chunk * TILE) + v.shape[1:])
        outs = lax.map(
            lambda xs: backward(gather_windows(xs[0]), xs[1], xs[2]),
            (tuple(split(v) for v in place), rows_split(depth_flat), rows_split(grad_u)),
        )
        grad_pw, grad_dw = jnp.sum(outs[0], axis=0), jnp.sum(outs[1], axis=0)
    grad_dw, grad_pw, grad_head, loss_sum = packed_sum(
        (grad_dw, grad_pw, grad_head, loss_sum), ("lat", "lon")
    )
    grad_head = grad_head.T
    return (grad_dw, grad_pw, grad_head, (loss_sum / teach_width).reshape(1))


def solution(mesh):
    in_specs = (
        P("groups", "lat", "lon", None),
        P(),
        P(),
        P(),
        P(),
        P(("groups", "lon", "lat"), None, None),
        P(("groups", "lon", "lat"), None),
        P(("groups", "lon", "lat")),
        P(("groups", "lon", "lat")),
    )
    out_specs = (P("groups", None), P("groups", None), P("groups", None), P("groups"))
    return jax.shard_map(local, mesh=mesh, in_specs=in_specs, out_specs=out_specs, check_vma=False)
```

```python
import jax
import jax.numpy as jnp
from jax import lax
from jax.sharding import PartitionSpec as P

DMAX = 4
TILE = 8
CAP = 2
CHUNK = 32


LANES = 128
EXCHANGED = 2


def halve(x, axis, bit):
    count = lax.axis_size(axis)
    rows = x.shape[0] // 2
    upper = (lax.axis_index(axis) // bit) % 2
    keep = lax.dynamic_slice_in_dim(x, upper * rows, rows, 0)
    send = lax.dynamic_slice_in_dim(x, (1 - upper) * rows, rows, 0)
    return keep + lax.ppermute(send, axis, [(i, i ^ bit) for i in range(count)])


def double(x, axis, bit):
    count = lax.axis_size(axis)
    rows = x.shape[0]
    upper = (lax.axis_index(axis) // bit) % 2
    got = lax.ppermute(x, axis, [(i, i ^ bit) for i in range(count)])
    whole = jnp.zeros((2 * rows,) + x.shape[1:], x.dtype)
    whole = lax.dynamic_update_slice_in_dim(whole, x, upper * rows, 0)
    return lax.dynamic_update_slice_in_dim(whole, got, (1 - upper) * rows, 0)


def packed_sum(values, axes):
    steps = []
    rest = []
    for axis in axes:
        count = lax.axis_size(axis)
        if count & (count - 1):
            rest.append(axis)
            continue
        bit = 1
        while bit < count:
            steps.append((axis, bit))
            bit *= 2
    flat = jnp.concatenate([jnp.ravel(v).astype(jnp.float32) for v in values])
    unit = 8 * LANES * (2 ** len(steps))
    total = -(-flat.shape[0] // unit) * unit
    x = jnp.pad(flat, (0, total - flat.shape[0])).reshape(-1, LANES)
    halved = steps[: max(0, len(steps) - EXCHANGED)]
    for axis, bit in halved:
        x = halve(x, axis, bit)
    for axis, bit in steps[len(halved) :]:
        count = lax.axis_size(axis)
        x = x + lax.ppermute(x, axis, [(i, i ^ bit) for i in range(count)])
    if rest:
        x = lax.psum(x, tuple(rest))
    for axis, bit in reversed(halved):
        x = double(x, axis, bit)
    flat = x.reshape(-1)
    out = []
    offset = 0
    for v in values:
        out.append(flat[offset : offset + v.size].reshape(v.shape))
        offset += v.size
    return tuple(out)


def padded_2(cells, sides, width, closed):
    for axis, dim in sides:
        count = lax.axis_size(axis)
        ends = count if closed else count - 1
        head = lax.slice_in_dim(cells, 0, width, axis=dim)
        tail = lax.slice_in_dim(cells, cells.shape[dim] - width, cells.shape[dim], axis=dim)
        cells = jnp.concatenate(
            [
                lax.ppermute(tail, axis, [(i, (i + 1) % count) for i in range(ends)]),
                cells,
                lax.ppermute(head, axis, [((i + 1) % count, i) for i in range(ends)]),
            ],
            axis=dim,
        )
    return cells


def local(
    acts, rates, dw_kernel, pw_weight, head_weight, teacher_tiles, tile_dest, tile_start, tile_count
):
    micro_batch, band_rows, block_cols, width = acts.shape
    teach_width = head_weight.shape[1]
    lat_index = lax.axis_index("lat")
    lat_count = lax.axis_size("lat")
    lon_count = lax.axis_size("lon")
    devices = lon_count * lat_count
    lon_padded = padded_2(acts, (("lon", 2),), DMAX, True)
    padded = padded_2(lon_padded, (("lat", 1),), DMAX, False)
    tiles_here = teacher_tiles.shape[0]
    destination = tile_dest[:, 0]
    positions = jnp.arange(tiles_here, dtype=jnp.int32)
    same_dest = destination[:, None] == destination[None, :]
    earlier = positions[:, None] > positions[None, :]
    slot_rank = jnp.sum((same_dest & earlier).astype(jnp.int32), axis=1)
    slot_index = destination * CAP + slot_rank
    slots = devices * CAP
    base = 64
    blank = jnp.zeros_like(tile_count)
    column = jnp.stack(
        [tile_start // base, tile_start % base, tile_count] + [blank] * (TILE - 3), axis=1
    )
    packed = jnp.concatenate([teacher_tiles, column.astype(jnp.bfloat16)[:, :, None]], axis=2)
    chooser = (slot_index[None, :] == jnp.arange(slots, dtype=jnp.int32)[:, None]).astype(
        jnp.bfloat16
    )
    send = jnp.einsum(
        "st,tre->sre", chooser, packed, preferred_element_type=jnp.float32
    ).astype(jnp.bfloat16)
    recv = lax.all_to_all(send, ("lon", "lat"), split_axis=0, concat_axis=0, tiled=True)
    recv_tiles = recv[:, :, :teach_width]
    meta = recv[:, :3, teach_width].astype(jnp.int32)
    recv_start = meta[:, 0] * base + meta[:, 1]
    recv_count = meta[:, 2]
    offsets = jnp.arange(TILE, dtype=jnp.int32)
    is_valid = offsets[None, :] < recv_count[:, None]
    sample_of = recv_start // (block_cols * band_rows)
    inner_row = recv_start // block_cols % band_rows
    first_col = recv_start % block_cols
    glob_row = lat_index * band_rows + inner_row
    area_weight = jnp.cos(
        jnp.pi * ((glob_row.astype(jnp.float32) + 0.5) / (band_rows * lat_count) - 0.5)
    )
    row_weight = jnp.where(is_valid, area_weight[:, None], jnp.float32(0.0)) / jnp.float32(
        devices * tiles_here * TILE
    )
    kernel = dw_kernel.astype(jnp.float32)
    onehot = (
        rates[None, :] == jnp.arange(1, DMAX + 1, dtype=jnp.int32)[:, None]
    ).astype(jnp.float32)
    span = 2 * DMAX + 1
    reach = TILE + 2 * DMAX

    def gather_windows(place):
        b, h, w = place
        return jax.vmap(
            lambda b, h, w: lax.dynamic_slice(
                padded, (b, h, w, jnp.int32(0)), (1, span, reach, width)
            )[0]
        )(b, h, w)

    def shifted(source, row_shift, col_shift):
        return source[:, DMAX + row_shift, DMAX + col_shift : DMAX + col_shift + TILE, :].astype(
            jnp.float32
        )

    def forward(windows, tiles, weight):
        center = shifted(windows, 0, 0)
        accum_sum = center * kernel[4]
        for dilation in range(1, DMAX + 1):
            for tap_index in range(9):
                if tap_index == 4:
                    continue
                row_shift = (tap_index // 3 - 1) * dilation
                col_shift = (tap_index % 3 - 1) * dilation
                accum_sum = accum_sum + kernel[tap_index] * onehot[dilation - 1] * shifted(
                    windows, row_shift, col_shift
                )
        depth_flat = accum_sum.astype(jnp.bfloat16).reshape(-1, width)
        preact = jnp.dot(depth_flat, pw_weight, preferred_element_type=jnp.float32)
        y_rows = (center.reshape(-1, width) + jax.nn.silu(preact)).astype(jnp.bfloat16)
        weight = weight.reshape(-1, 1)
        predicted = jnp.dot(y_rows, head_weight, preferred_element_type=jnp.float32)
        residual = predicted - tiles.reshape(-1, teach_width).astype(jnp.float32)
        loss_part = jnp.sum(weight * residual * residual)
        grad_pred = (2.0 * weight * residual).astype(jnp.bfloat16)
        head_part = lax.dot_general(
            grad_pred, y_rows, (((0,), (0,)), ((), ())), preferred_element_type=jnp.float32
        )
        grad_rows = jnp.dot(grad_pred, head_weight.T, preferred_element_type=jnp.float32)
        return depth_flat, preact, grad_rows, loss_part, head_part

    def backward(windows, depth_flat, grad_u):
        pw_part = lax.dot_general(
            depth_flat, grad_u, (((0,), (0,)), ((), ())), preferred_element_type=jnp.float32
        )
        grad_z = jnp.dot(grad_u, pw_weight.T, preferred_element_type=jnp.float32)
        grad_z = grad_z.reshape(windows.shape[0], TILE, width)
        tap_sums = []
        for tap_index in range(9):
            if tap_index == 4:
                chosen = shifted(windows, 0, 0)
            else:
                chosen = None
                for dilation in range(1, DMAX + 1):
                    row_shift = (tap_index // 3 - 1) * dilation
                    col_shift = (tap_index % 3 - 1) * dilation
                    term = onehot[dilation - 1] * shifted(windows, row_shift, col_shift)
                    chosen = term if chosen is None else chosen + term
            tap_sums.append(jnp.sum((chosen * grad_z).reshape(-1, width), axis=0))
        return pw_part, jnp.stack(tap_sums, axis=0)

    slots = recv_start.shape[0]
    chunk = min(slots, CHUNK)
    chunks = slots // chunk
    place = (sample_of, inner_row, first_col)
    if chunks == 1:
        windows = gather_windows(place)
        depth_flat, preact, grad_rows, loss_sum, grad_head = forward(
            windows, recv_tiles, row_weight
        )
    else:
        split = lambda v: v.reshape((chunks, chunk) + v.shape[1:])
        outs = lax.map(
            lambda xs: forward(gather_windows(xs[0]), xs[1], xs[2]),
            (tuple(split(v) for v in place), split(recv_tiles), split(row_weight)),
        )
        depth_flat, preact, grad_rows = (v.reshape((-1, width)) for v in outs[:3])
        loss_sum, grad_head = jnp.sum(outs[3]), jnp.sum(outs[4], axis=0)
    cell = (recv_start[:, None] + offsets[None, :]).reshape(-1)
    row_ids = jnp.arange(cell.shape[0], dtype=jnp.int32)
    if cell.shape[0] <= 512:
        same_cell = cell[:, None] == cell[None, :]
        grad_y = jnp.dot(
            same_cell.astype(jnp.float32),
            grad_rows,
            precision=lax.Precision.HIGHEST,
            preferred_element_type=jnp.float32,
        )
        repeated = jnp.any(same_cell & (row_ids[None, :] < row_ids[:, None]), axis=1)
    else:
        cells_here = micro_batch * band_rows * block_cols
        grid = jnp.zeros((cells_here, width), jnp.float32).at[cell].add(grad_rows)
        grad_y = grid[cell]
        owner = jnp.full((cells_here,), cell.shape[0], jnp.int32).at[cell].min(row_ids)
        repeated = owner[cell] != row_ids
    sigmoid_u = jax.nn.sigmoid(preact)
    grad_u = (grad_y * sigmoid_u * (1.0 + preact * (1.0 - sigmoid_u))).astype(jnp.bfloat16)
    grad_u = jnp.where(repeated[:, None], jnp.zeros_like(grad_u), grad_u)
    if chunks == 1:
        grad_pw, grad_dw = backward(windows, depth_flat, grad_u)
    else:
        rows_split = lambda v: v.reshape((chunks, chunk * TILE) + v.shape[1:])
        outs = lax.map(
            lambda xs: backward(gather_windows(xs[0]), xs[1], xs[2]),
            (tuple(split(v) for v in place), rows_split(depth_flat), rows_split(grad_u)),
        )
        grad_pw, grad_dw = jnp.sum(outs[0], axis=0), jnp.sum(outs[1], axis=0)
    grad_dw, grad_pw, grad_head, loss_sum = packed_sum(
        (grad_dw, grad_pw, grad_head, loss_sum), ("lat", "lon")
    )
    grad_head = grad_head.T
    return (grad_dw, grad_pw, grad_head, (loss_sum / teach_width).reshape(1))


def solution(mesh):
    in_specs = (
        P("groups", "lat", "lon", None),
        P(),
        P(),
        P(),
        P(),
        P(("groups", "lon", "lat"), None, None),
        P(("groups", "lon", "lat"), None),
        P(("groups", "lon", "lat")),
        P(("groups", "lon", "lat")),
    )
    out_specs = (P("groups", None), P("groups", None), P("groups", None), P("groups"))
    return jax.shard_map(local, mesh=mesh, in_specs=in_specs, out_specs=out_specs, check_vma=False)
```

```python
import jax
import jax.numpy as jnp
from jax import lax
from jax.sharding import PartitionSpec as P

DMAX = 4
TILE = 8
CAP = 2
CHUNK = 32


LANES = 128
EXCHANGED = 2


def halve(x, axis, bit):
    count = lax.axis_size(axis)
    rows = x.shape[0] // 2
    upper = (lax.axis_index(axis) // bit) % 2
    keep = lax.dynamic_slice_in_dim(x, upper * rows, rows, 0)
    send = lax.dynamic_slice_in_dim(x, (1 - upper) * rows, rows, 0)
    return keep + lax.ppermute(send, axis, [(i, i ^ bit) for i in range(count)])


def double(x, axis, bit):
    count = lax.axis_size(axis)
    rows = x.shape[0]
    upper = (lax.axis_index(axis) // bit) % 2
    got = lax.ppermute(x, axis, [(i, i ^ bit) for i in range(count)])
    whole = jnp.zeros((2 * rows,) + x.shape[1:], x.dtype)
    whole = lax.dynamic_update_slice_in_dim(whole, x, upper * rows, 0)
    return lax.dynamic_update_slice_in_dim(whole, got, (1 - upper) * rows, 0)


def packed_sum(values, axes):
    steps = []
    rest = []
    for axis in axes:
        count = lax.axis_size(axis)
        if count & (count - 1):
            rest.append(axis)
            continue
        bit = 1
        while bit < count:
            steps.append((axis, bit))
            bit *= 2
    flat = jnp.concatenate([jnp.ravel(v).astype(jnp.float32) for v in values])
    unit = 8 * LANES * (2 ** len(steps))
    total = -(-flat.shape[0] // unit) * unit
    x = jnp.pad(flat, (0, total - flat.shape[0])).reshape(-1, LANES)
    halved = steps[: max(0, len(steps) - EXCHANGED)]
    for axis, bit in halved:
        x = halve(x, axis, bit)
    for axis, bit in steps[len(halved) :]:
        count = lax.axis_size(axis)
        x = x + lax.ppermute(x, axis, [(i, i ^ bit) for i in range(count)])
    if rest:
        x = lax.psum(x, tuple(rest))
    for axis, bit in reversed(halved):
        x = double(x, axis, bit)
    flat = x.reshape(-1)
    out = []
    offset = 0
    for v in values:
        out.append(flat[offset : offset + v.size].reshape(v.shape))
        offset += v.size
    return tuple(out)


def padded_2(cells, sides, width, closed):
    for axis, dim in sides:
        count = lax.axis_size(axis)
        ends = count if closed else count - 1
        head = lax.slice_in_dim(cells, 0, width, axis=dim)
        tail = lax.slice_in_dim(cells, cells.shape[dim] - width, cells.shape[dim], axis=dim)
        cells = jnp.concatenate(
            [
                lax.ppermute(tail, axis, [(i, (i + 1) % count) for i in range(ends)]),
                cells,
                lax.ppermute(head, axis, [((i + 1) % count, i) for i in range(ends)]),
            ],
            axis=dim,
        )
    return cells


def local(
    acts, rates, dw_kernel, pw_weight, head_weight, teacher_tiles, tile_dest, tile_start, tile_count
):
    micro_batch, band_rows, block_cols, width = acts.shape
    teach_width = head_weight.shape[1]
    lat_index = lax.axis_index("lat")
    lat_count = lax.axis_size("lat")
    lon_count = lax.axis_size("lon")
    devices = lon_count * lat_count
    lon_padded = padded_2(acts, (("lon", 2),), DMAX, True)
    padded = padded_2(lon_padded, (("lat", 1),), DMAX, False)
    tiles_here = teacher_tiles.shape[0]
    destination = tile_dest[:, 0]
    positions = jnp.arange(tiles_here, dtype=jnp.int32)
    same_dest = destination[:, None] == destination[None, :]
    earlier = positions[:, None] > positions[None, :]
    slot_rank = jnp.sum((same_dest & earlier).astype(jnp.int32), axis=1)
    slot_index = destination * CAP + slot_rank
    slots = devices * CAP
    base = 64
    blank = jnp.zeros_like(tile_count)
    column = jnp.stack(
        [tile_start // base, tile_start % base, tile_count] + [blank] * (TILE - 3), axis=1
    )
    packed = jnp.concatenate([teacher_tiles, column.astype(jnp.bfloat16)[:, :, None]], axis=2)
    chooser = (slot_index[None, :] == jnp.arange(slots, dtype=jnp.int32)[:, None]).astype(
        jnp.bfloat16
    )
    send = jnp.einsum(
        "st,tre->sre", chooser, packed, preferred_element_type=jnp.float32
    ).astype(jnp.bfloat16)
    recv = lax.all_to_all(send, ("lon", "lat"), split_axis=0, concat_axis=0, tiled=True)
    recv_tiles = recv[:, :, :teach_width]
    meta = recv[:, :3, teach_width].astype(jnp.int32)
    recv_start = meta[:, 0] * base + meta[:, 1]
    recv_count = meta[:, 2]
    offsets = jnp.arange(TILE, dtype=jnp.int32)
    is_valid = offsets[None, :] < recv_count[:, None]
    sample_of = recv_start // (block_cols * band_rows)
    inner_row = recv_start // block_cols % band_rows
    first_col = recv_start % block_cols
    glob_row = lat_index * band_rows + inner_row
    area_weight = jnp.cos(
        jnp.pi * ((glob_row.astype(jnp.float32) + 0.5) / (band_rows * lat_count) - 0.5)
    )
    row_weight = jnp.where(is_valid, area_weight[:, None], jnp.float32(0.0)) / jnp.float32(
        devices * tiles_here * TILE
    )
    kernel = dw_kernel.astype(jnp.float32)
    onehot = (
        rates[None, :] == jnp.arange(1, DMAX + 1, dtype=jnp.int32)[:, None]
    ).astype(jnp.float32)
    span = 2 * DMAX + 1
    reach = TILE + 2 * DMAX

    def gather_windows(place):
        b, h, w = place
        return jax.vmap(
            lambda b, h, w: lax.dynamic_slice(
                padded, (b, h, w, jnp.int32(0)), (1, span, reach, width)
            )[0]
        )(b, h, w)

    def shifted(source, row_shift, col_shift):
        return source[:, DMAX + row_shift, DMAX + col_shift : DMAX + col_shift + TILE, :].astype(
            jnp.float32
        )

    def chosen_tap(windows, tap_index):
        if tap_index == 4:
            return shifted(windows, 0, 0)
        chosen = None
        for dilation in range(1, DMAX + 1):
            row_shift = (tap_index // 3 - 1) * dilation
            col_shift = (tap_index % 3 - 1) * dilation
            term = onehot[dilation - 1] * shifted(windows, row_shift, col_shift)
            chosen = term if chosen is None else chosen + term
        return chosen

    def forward(windows, tiles, weight):
        center = shifted(windows, 0, 0)
        accum_sum = center * kernel[4]
        for tap_index in range(9):
            if tap_index != 4:
                accum_sum = accum_sum + kernel[tap_index] * chosen_tap(windows, tap_index)
        depth_flat = accum_sum.astype(jnp.bfloat16).reshape(-1, width)
        preact = jnp.dot(depth_flat, pw_weight, preferred_element_type=jnp.float32)
        y_rows = (center.reshape(-1, width) + jax.nn.silu(preact)).astype(jnp.bfloat16)
        weight = weight.reshape(-1, 1)
        predicted = jnp.dot(y_rows, head_weight, preferred_element_type=jnp.float32)
        residual = predicted - tiles.reshape(-1, teach_width).astype(jnp.float32)
        loss_part = jnp.sum(weight * residual * residual)
        grad_pred = (2.0 * weight * residual).astype(jnp.bfloat16)
        head_part = lax.dot_general(
            grad_pred, y_rows, (((0,), (0,)), ((), ())), preferred_element_type=jnp.float32
        )
        grad_rows = jnp.dot(grad_pred, head_weight.T, preferred_element_type=jnp.float32)
        return depth_flat, preact, grad_rows, loss_part, head_part

    def backward(windows, depth_flat, grad_u):
        pw_part = lax.dot_general(
            depth_flat, grad_u, (((0,), (0,)), ((), ())), preferred_element_type=jnp.float32
        )
        grad_z = jnp.dot(grad_u, pw_weight.T, preferred_element_type=jnp.float32)
        grad_z = grad_z.reshape(windows.shape[0], TILE, width)
        tap_sums = []
        for tap_index in range(9):
            chosen = chosen_tap(windows, tap_index)
            tap_sums.append(jnp.sum((chosen * grad_z).reshape(-1, width), axis=0))
        return pw_part, jnp.stack(tap_sums, axis=0)

    slots = recv_start.shape[0]
    chunk = min(slots, CHUNK)
    chunks = slots // chunk
    place = (sample_of, inner_row, first_col)
    if chunks == 1:
        windows = gather_windows(place)
        depth_flat, preact, grad_rows, loss_sum, grad_head = forward(
            windows, recv_tiles, row_weight
        )
    else:
        split = lambda v: v.reshape((chunks, chunk) + v.shape[1:])
        outs = lax.map(
            lambda xs: forward(gather_windows(xs[0]), xs[1], xs[2]),
            (tuple(split(v) for v in place), split(recv_tiles), split(row_weight)),
        )
        depth_flat, preact, grad_rows = (v.reshape((-1, width)) for v in outs[:3])
        loss_sum, grad_head = jnp.sum(outs[3]), jnp.sum(outs[4], axis=0)
    cell = (recv_start[:, None] + offsets[None, :]).reshape(-1)
    row_ids = jnp.arange(cell.shape[0], dtype=jnp.int32)
    if cell.shape[0] <= 512:
        same_cell = cell[:, None] == cell[None, :]
        grad_y = jnp.dot(
            same_cell.astype(jnp.float32),
            grad_rows,
            precision=lax.Precision.HIGHEST,
            preferred_element_type=jnp.float32,
        )
        repeated = jnp.any(same_cell & (row_ids[None, :] < row_ids[:, None]), axis=1)
    else:
        cells_here = micro_batch * band_rows * block_cols
        grid = jnp.zeros((cells_here, width), jnp.float32).at[cell].add(grad_rows)
        grad_y = grid[cell]
        owner = jnp.full((cells_here,), cell.shape[0], jnp.int32).at[cell].min(row_ids)
        repeated = owner[cell] != row_ids
    sigmoid_u = jax.nn.sigmoid(preact)
    grad_u = (grad_y * sigmoid_u * (1.0 + preact * (1.0 - sigmoid_u))).astype(jnp.bfloat16)
    grad_u = jnp.where(repeated[:, None], jnp.zeros_like(grad_u), grad_u)
    if chunks == 1:
        grad_pw, grad_dw = backward(windows, depth_flat, grad_u)
    else:
        rows_split = lambda v: v.reshape((chunks, chunk * TILE) + v.shape[1:])
        outs = lax.map(
            lambda xs: backward(gather_windows(xs[0]), xs[1], xs[2]),
            (tuple(split(v) for v in place), rows_split(depth_flat), rows_split(grad_u)),
        )
        grad_pw, grad_dw = jnp.sum(outs[0], axis=0), jnp.sum(outs[1], axis=0)
    grad_dw, grad_pw, grad_head, loss_sum = packed_sum(
        (grad_dw, grad_pw, grad_head, loss_sum), ("lat", "lon")
    )
    grad_head = grad_head.T
    return (grad_dw, grad_pw, grad_head, (loss_sum / teach_width).reshape(1))


def solution(mesh):
    in_specs = (
        P("groups", "lat", "lon", None),
        P(),
        P(),
        P(),
        P(),
        P(("groups", "lon", "lat"), None, None),
        P(("groups", "lon", "lat"), None),
        P(("groups", "lon", "lat")),
        P(("groups", "lon", "lat")),
    )
    out_specs = (P("groups", None), P("groups", None), P("groups", None), P("groups"))
    return jax.shard_map(local, mesh=mesh, in_specs=in_specs, out_specs=out_specs, check_vma=False)
```

```python
import jax
import jax.numpy as jnp
from jax import lax
from jax.sharding import PartitionSpec as P

DMAX = 4
TILE = 8
CAP = 2
CHUNK = 32


LANES = 128
EXCHANGED = 2


def halve(x, axis, bit):
    count = lax.axis_size(axis)
    rows = x.shape[0] // 2
    upper = (lax.axis_index(axis) // bit) % 2
    keep = lax.dynamic_slice_in_dim(x, upper * rows, rows, 0)
    send = lax.dynamic_slice_in_dim(x, (1 - upper) * rows, rows, 0)
    return keep + lax.ppermute(send, axis, [(i, i ^ bit) for i in range(count)])


def double(x, axis, bit):
    count = lax.axis_size(axis)
    rows = x.shape[0]
    upper = (lax.axis_index(axis) // bit) % 2
    got = lax.ppermute(x, axis, [(i, i ^ bit) for i in range(count)])
    whole = jnp.zeros((2 * rows,) + x.shape[1:], x.dtype)
    whole = lax.dynamic_update_slice_in_dim(whole, x, upper * rows, 0)
    return lax.dynamic_update_slice_in_dim(whole, got, (1 - upper) * rows, 0)


def packed_sum(values, axes):
    steps = []
    rest = []
    for axis in axes:
        count = lax.axis_size(axis)
        if count & (count - 1):
            rest.append(axis)
            continue
        bit = 1
        while bit < count:
            steps.append((axis, bit))
            bit *= 2
    flat = jnp.concatenate([jnp.ravel(v).astype(jnp.float32) for v in values])
    unit = 8 * LANES * (2 ** len(steps))
    total = -(-flat.shape[0] // unit) * unit
    x = jnp.pad(flat, (0, total - flat.shape[0])).reshape(-1, LANES)
    halved = steps[: max(0, len(steps) - EXCHANGED)]
    for axis, bit in halved:
        x = halve(x, axis, bit)
    for axis, bit in steps[len(halved) :]:
        count = lax.axis_size(axis)
        x = x + lax.ppermute(x, axis, [(i, i ^ bit) for i in range(count)])
    if rest:
        x = lax.psum(x, tuple(rest))
    for axis, bit in reversed(halved):
        x = double(x, axis, bit)
    flat = x.reshape(-1)
    out = []
    offset = 0
    for v in values:
        out.append(flat[offset : offset + v.size].reshape(v.shape))
        offset += v.size
    return tuple(out)


def padded_2(cells, sides, width, closed):
    for axis, dim in sides:
        count = lax.axis_size(axis)
        ends = count if closed else count - 1
        head = lax.slice_in_dim(cells, 0, width, axis=dim)
        tail = lax.slice_in_dim(cells, cells.shape[dim] - width, cells.shape[dim], axis=dim)
        cells = jnp.concatenate(
            [
                lax.ppermute(tail, axis, [(i, (i + 1) % count) for i in range(ends)]),
                cells,
                lax.ppermute(head, axis, [((i + 1) % count, i) for i in range(ends)]),
            ],
            axis=dim,
        )
    return cells


def local(
    acts, rates, dw_kernel, pw_weight, head_weight, teacher_tiles, tile_dest, tile_start, tile_count
):
    micro_batch, band_rows, block_cols, width = acts.shape
    teach_width = head_weight.shape[1]
    lat_index = lax.axis_index("lat")
    lat_count = lax.axis_size("lat")
    lon_count = lax.axis_size("lon")
    devices = lon_count * lat_count
    lon_padded = padded_2(acts, (("lon", 2),), DMAX, True)
    padded = padded_2(lon_padded, (("lat", 1),), DMAX, False)
    tiles_here = teacher_tiles.shape[0]
    destination = tile_dest[:, 0]
    positions = jnp.arange(tiles_here, dtype=jnp.int32)
    same_dest = destination[:, None] == destination[None, :]
    earlier = positions[:, None] > positions[None, :]
    slot_rank = jnp.sum((same_dest & earlier).astype(jnp.int32), axis=1)
    slot_index = destination * CAP + slot_rank
    slots = devices * CAP
    base = 64
    blank = jnp.zeros_like(tile_count)
    column = jnp.stack(
        [tile_start // base, tile_start % base, tile_count] + [blank] * (TILE - 3), axis=1
    )
    packed = jnp.concatenate([teacher_tiles, column.astype(jnp.bfloat16)[:, :, None]], axis=2)
    chooser = (slot_index[None, :] == jnp.arange(slots, dtype=jnp.int32)[:, None]).astype(
        jnp.bfloat16
    )
    send = jnp.einsum(
        "st,tre->sre", chooser, packed, preferred_element_type=jnp.float32
    ).astype(jnp.bfloat16)
    recv = lax.all_to_all(send, ("lon", "lat"), split_axis=0, concat_axis=0, tiled=True)
    recv_tiles = recv[:, :, :teach_width]
    meta = recv[:, :3, teach_width].astype(jnp.int32)
    recv_start = meta[:, 0] * base + meta[:, 1]
    recv_count = meta[:, 2]
    offsets = jnp.arange(TILE, dtype=jnp.int32)
    is_valid = offsets[None, :] < recv_count[:, None]
    sample_of = recv_start // (block_cols * band_rows)
    inner_row = recv_start // block_cols % band_rows
    first_col = recv_start % block_cols
    glob_row = lat_index * band_rows + inner_row
    area_weight = jnp.cos(
        jnp.pi * ((glob_row.astype(jnp.float32) + 0.5) / (band_rows * lat_count) - 0.5)
    )
    row_weight = jnp.where(is_valid, area_weight[:, None], jnp.float32(0.0)) / jnp.float32(
        devices * tiles_here * TILE
    )
    kernel = dw_kernel.astype(jnp.float32)
    onehot = (
        rates[None, :] == jnp.arange(1, DMAX + 1, dtype=jnp.int32)[:, None]
    ).astype(jnp.float32)
    span = 2 * DMAX + 1
    reach = TILE + 2 * DMAX

    def gather_windows(place):
        b, h, w = place
        return jax.vmap(
            lambda b, h, w: lax.dynamic_slice(
                padded, (b, h, w, jnp.int32(0)), (1, span, reach, width)
            )[0]
        )(b, h, w)

    def shifted(source, row_shift, col_shift):
        return source[:, DMAX + row_shift, DMAX + col_shift : DMAX + col_shift + TILE, :].astype(
            jnp.float32
        )

    def chosen_tap(windows, tap_index):
        if tap_index == 4:
            return shifted(windows, 0, 0)
        chosen = None
        for dilation in range(1, DMAX + 1):
            row_shift = (tap_index // 3 - 1) * dilation
            col_shift = (tap_index % 3 - 1) * dilation
            piece = windows[:, DMAX + row_shift, DMAX + col_shift : DMAX + col_shift + TILE, :]
            term = onehot[dilation - 1].astype(jnp.bfloat16) * piece
            chosen = term if chosen is None else chosen + term
        return chosen.astype(jnp.float32)

    def forward(windows, tiles, weight):
        center = shifted(windows, 0, 0)
        accum_sum = center * kernel[4]
        for tap_index in range(9):
            if tap_index != 4:
                accum_sum = accum_sum + kernel[tap_index] * chosen_tap(windows, tap_index)
        depth_flat = accum_sum.astype(jnp.bfloat16).reshape(-1, width)
        preact = jnp.dot(depth_flat, pw_weight, preferred_element_type=jnp.float32)
        y_rows = (center.reshape(-1, width) + jax.nn.silu(preact)).astype(jnp.bfloat16)
        weight = weight.reshape(-1, 1)
        predicted = jnp.dot(y_rows, head_weight, preferred_element_type=jnp.float32)
        residual = predicted - tiles.reshape(-1, teach_width).astype(jnp.float32)
        loss_part = jnp.sum(weight * residual * residual)
        grad_pred = (2.0 * weight * residual).astype(jnp.bfloat16)
        head_part = lax.dot_general(
            grad_pred, y_rows, (((0,), (0,)), ((), ())), preferred_element_type=jnp.float32
        )
        grad_rows = jnp.dot(grad_pred, head_weight.T, preferred_element_type=jnp.float32)
        return depth_flat, preact, grad_rows, loss_part, head_part

    def backward(windows, depth_flat, grad_u):
        pw_part = lax.dot_general(
            depth_flat, grad_u, (((0,), (0,)), ((), ())), preferred_element_type=jnp.float32
        )
        grad_z = jnp.dot(grad_u, pw_weight.T, preferred_element_type=jnp.float32)
        grad_z = grad_z.reshape(windows.shape[0], TILE, width)
        tap_sums = []
        for tap_index in range(9):
            chosen = chosen_tap(windows, tap_index)
            tap_sums.append(jnp.sum((chosen * grad_z).reshape(-1, width), axis=0))
        return pw_part, jnp.stack(tap_sums, axis=0)

    slots = recv_start.shape[0]
    chunk = min(slots, CHUNK)
    chunks = slots // chunk
    place = (sample_of, inner_row, first_col)
    if chunks == 1:
        windows = gather_windows(place)
        depth_flat, preact, grad_rows, loss_sum, grad_head = forward(
            windows, recv_tiles, row_weight
        )
    else:
        split = lambda v: v.reshape((chunks, chunk) + v.shape[1:])
        outs = lax.map(
            lambda xs: forward(gather_windows(xs[0]), xs[1], xs[2]),
            (tuple(split(v) for v in place), split(recv_tiles), split(row_weight)),
        )
        depth_flat, preact, grad_rows = (v.reshape((-1, width)) for v in outs[:3])
        loss_sum, grad_head = jnp.sum(outs[3]), jnp.sum(outs[4], axis=0)
    cell = (recv_start[:, None] + offsets[None, :]).reshape(-1)
    row_ids = jnp.arange(cell.shape[0], dtype=jnp.int32)
    if cell.shape[0] <= 512:
        same_cell = cell[:, None] == cell[None, :]
        grad_y = jnp.dot(
            same_cell.astype(jnp.float32),
            grad_rows,
            precision=lax.Precision.HIGHEST,
            preferred_element_type=jnp.float32,
        )
        repeated = jnp.any(same_cell & (row_ids[None, :] < row_ids[:, None]), axis=1)
    else:
        cells_here = micro_batch * band_rows * block_cols
        grid = jnp.zeros((cells_here, width), jnp.float32).at[cell].add(grad_rows)
        grad_y = grid[cell]
        owner = jnp.full((cells_here,), cell.shape[0], jnp.int32).at[cell].min(row_ids)
        repeated = owner[cell] != row_ids
    sigmoid_u = jax.nn.sigmoid(preact)
    grad_u = (grad_y * sigmoid_u * (1.0 + preact * (1.0 - sigmoid_u))).astype(jnp.bfloat16)
    grad_u = jnp.where(repeated[:, None], jnp.zeros_like(grad_u), grad_u)
    if chunks == 1:
        grad_pw, grad_dw = backward(windows, depth_flat, grad_u)
    else:
        rows_split = lambda v: v.reshape((chunks, chunk * TILE) + v.shape[1:])
        outs = lax.map(
            lambda xs: backward(gather_windows(xs[0]), xs[1], xs[2]),
            (tuple(split(v) for v in place), rows_split(depth_flat), rows_split(grad_u)),
        )
        grad_pw, grad_dw = jnp.sum(outs[0], axis=0), jnp.sum(outs[1], axis=0)
    grad_dw, grad_pw, grad_head, loss_sum = packed_sum(
        (grad_dw, grad_pw, grad_head, loss_sum), ("lat", "lon")
    )
    grad_head = grad_head.T
    return (grad_dw, grad_pw, grad_head, (loss_sum / teach_width).reshape(1))


def solution(mesh):
    in_specs = (
        P("groups", "lat", "lon", None),
        P(),
        P(),
        P(),
        P(),
        P(("groups", "lon", "lat"), None, None),
        P(("groups", "lon", "lat"), None),
        P(("groups", "lon", "lat")),
        P(("groups", "lon", "lat")),
    )
    out_specs = (P("groups", None), P("groups", None), P("groups", None), P("groups"))
    return jax.shard_map(local, mesh=mesh, in_specs=in_specs, out_specs=out_specs, check_vma=False)
```

```python
import jax
import jax.numpy as jnp
from jax import lax
from jax.sharding import PartitionSpec as P

DMAX = 4
TILE = 8
CAP = 2
CHUNK = 32


LANES = 128
EXCHANGED = 2


def halve(x, axis, bit):
    count = lax.axis_size(axis)
    rows = x.shape[0] // 2
    upper = (lax.axis_index(axis) // bit) % 2
    keep = lax.dynamic_slice_in_dim(x, upper * rows, rows, 0)
    send = lax.dynamic_slice_in_dim(x, (1 - upper) * rows, rows, 0)
    return keep + lax.ppermute(send, axis, [(i, i ^ bit) for i in range(count)])


def double(x, axis, bit):
    count = lax.axis_size(axis)
    rows = x.shape[0]
    upper = (lax.axis_index(axis) // bit) % 2
    got = lax.ppermute(x, axis, [(i, i ^ bit) for i in range(count)])
    whole = jnp.zeros((2 * rows,) + x.shape[1:], x.dtype)
    whole = lax.dynamic_update_slice_in_dim(whole, x, upper * rows, 0)
    return lax.dynamic_update_slice_in_dim(whole, got, (1 - upper) * rows, 0)


def packed_sum(values, axes):
    steps = []
    rest = []
    for axis in axes:
        count = lax.axis_size(axis)
        if count & (count - 1):
            rest.append(axis)
            continue
        bit = 1
        while bit < count:
            steps.append((axis, bit))
            bit *= 2
    flat = jnp.concatenate([jnp.ravel(v).astype(jnp.float32) for v in values])
    unit = 8 * LANES * (2 ** len(steps))
    total = -(-flat.shape[0] // unit) * unit
    x = jnp.pad(flat, (0, total - flat.shape[0])).reshape(-1, LANES)
    halved = steps[: max(0, len(steps) - EXCHANGED)]
    for axis, bit in halved:
        x = halve(x, axis, bit)
    for axis, bit in steps[len(halved) :]:
        count = lax.axis_size(axis)
        x = x + lax.ppermute(x, axis, [(i, i ^ bit) for i in range(count)])
    if rest:
        x = lax.psum(x, tuple(rest))
    for axis, bit in reversed(halved):
        x = double(x, axis, bit)
    flat = x.reshape(-1)
    out = []
    offset = 0
    for v in values:
        out.append(flat[offset : offset + v.size].reshape(v.shape))
        offset += v.size
    return tuple(out)


def padded_2(cells, sides, width, closed):
    for axis, dim in sides:
        count = lax.axis_size(axis)
        ends = count if closed else count - 1
        head = lax.slice_in_dim(cells, 0, width, axis=dim)
        tail = lax.slice_in_dim(cells, cells.shape[dim] - width, cells.shape[dim], axis=dim)
        cells = jnp.concatenate(
            [
                lax.ppermute(tail, axis, [(i, (i + 1) % count) for i in range(ends)]),
                cells,
                lax.ppermute(head, axis, [((i + 1) % count, i) for i in range(ends)]),
            ],
            axis=dim,
        )
    return cells


def local(
    acts, rates, dw_kernel, pw_weight, head_weight, teacher_tiles, tile_dest, tile_start, tile_count
):
    micro_batch, band_rows, block_cols, width = acts.shape
    teach_width = head_weight.shape[1]
    lat_index = lax.axis_index("lat")
    lat_count = lax.axis_size("lat")
    lon_count = lax.axis_size("lon")
    devices = lon_count * lat_count
    lon_padded = padded_2(acts, (("lon", 2),), DMAX, True)
    padded = padded_2(lon_padded, (("lat", 1),), DMAX, False)
    tiles_here = teacher_tiles.shape[0]
    destination = tile_dest[:, 0]
    positions = jnp.arange(tiles_here, dtype=jnp.int32)
    same_dest = destination[:, None] == destination[None, :]
    earlier = positions[:, None] > positions[None, :]
    slot_rank = jnp.sum((same_dest & earlier).astype(jnp.int32), axis=1)
    slot_index = destination * CAP + slot_rank
    slots = devices * CAP
    base = 64
    blank = jnp.zeros_like(tile_count)
    column = jnp.stack(
        [tile_start // base, tile_start % base, tile_count] + [blank] * (TILE - 3), axis=1
    )
    packed = jnp.concatenate([teacher_tiles, column.astype(jnp.bfloat16)[:, :, None]], axis=2)
    chooser = (slot_index[None, :] == jnp.arange(slots, dtype=jnp.int32)[:, None]).astype(
        jnp.bfloat16
    )
    send = jnp.einsum(
        "st,tre->sre", chooser, packed, preferred_element_type=jnp.float32
    ).astype(jnp.bfloat16)
    recv = lax.all_to_all(send, ("lon", "lat"), split_axis=0, concat_axis=0, tiled=True)
    recv_tiles = recv[:, :, :teach_width]
    meta = recv[:, :3, teach_width].astype(jnp.int32)
    recv_start = meta[:, 0] * base + meta[:, 1]
    recv_count = meta[:, 2]
    offsets = jnp.arange(TILE, dtype=jnp.int32)
    is_valid = offsets[None, :] < recv_count[:, None]
    sample_of = recv_start // (block_cols * band_rows)
    inner_row = recv_start // block_cols % band_rows
    first_col = recv_start % block_cols
    glob_row = lat_index * band_rows + inner_row
    area_weight = jnp.cos(
        jnp.pi * ((glob_row.astype(jnp.float32) + 0.5) / (band_rows * lat_count) - 0.5)
    )
    row_weight = jnp.where(is_valid, area_weight[:, None], jnp.float32(0.0)) / jnp.float32(
        devices * tiles_here * TILE
    )
    kernel = dw_kernel.astype(jnp.float32)
    onehot = (
        rates[None, :] == jnp.arange(1, DMAX + 1, dtype=jnp.int32)[:, None]
    ).astype(jnp.float32)
    span = 2 * DMAX + 1
    reach = TILE + 2 * DMAX

    def gather_windows(place):
        b, h, w = place
        return jax.vmap(
            lambda b, h, w: lax.dynamic_slice(
                padded, (b, h, w, jnp.int32(0)), (1, span, reach, width)
            )[0]
        )(b, h, w)

    def shifted(source, row_shift, col_shift):
        return source[:, DMAX + row_shift, DMAX + col_shift : DMAX + col_shift + TILE, :].astype(
            jnp.float32
        )

    def chosen_tap(windows, tap_index):
        if tap_index == 4:
            return shifted(windows, 0, 0)
        chosen = None
        for dilation in range(DMAX, 0, -1):
            row_shift = (tap_index // 3 - 1) * dilation
            col_shift = (tap_index % 3 - 1) * dilation
            piece = windows[:, DMAX + row_shift, DMAX + col_shift : DMAX + col_shift + TILE, :]
            if chosen is None:
                chosen = jnp.where(rates == dilation, piece, jnp.zeros_like(piece))
            else:
                chosen = jnp.where(rates == dilation, piece, chosen)
        return chosen.astype(jnp.float32)

    def forward(windows, tiles, weight):
        center = shifted(windows, 0, 0)
        accum_sum = center * kernel[4]
        for tap_index in range(9):
            if tap_index != 4:
                accum_sum = accum_sum + kernel[tap_index] * chosen_tap(windows, tap_index)
        depth_flat = accum_sum.astype(jnp.bfloat16).reshape(-1, width)
        preact = jnp.dot(depth_flat, pw_weight, preferred_element_type=jnp.float32)
        y_rows = (center.reshape(-1, width) + jax.nn.silu(preact)).astype(jnp.bfloat16)
        weight = weight.reshape(-1, 1)
        predicted = jnp.dot(y_rows, head_weight, preferred_element_type=jnp.float32)
        residual = predicted - tiles.reshape(-1, teach_width).astype(jnp.float32)
        loss_part = jnp.sum(weight * residual * residual)
        grad_pred = (2.0 * weight * residual).astype(jnp.bfloat16)
        head_part = lax.dot_general(
            grad_pred, y_rows, (((0,), (0,)), ((), ())), preferred_element_type=jnp.float32
        )
        grad_rows = jnp.dot(grad_pred, head_weight.T, preferred_element_type=jnp.float32)
        return depth_flat, preact, grad_rows, loss_part, head_part

    def backward(windows, depth_flat, grad_u):
        pw_part = lax.dot_general(
            depth_flat, grad_u, (((0,), (0,)), ((), ())), preferred_element_type=jnp.float32
        )
        grad_z = jnp.dot(grad_u, pw_weight.T, preferred_element_type=jnp.float32)
        grad_z = grad_z.reshape(windows.shape[0], TILE, width)
        tap_sums = []
        for tap_index in range(9):
            chosen = chosen_tap(windows, tap_index)
            tap_sums.append(jnp.sum((chosen * grad_z).reshape(-1, width), axis=0))
        return pw_part, jnp.stack(tap_sums, axis=0)

    slots = recv_start.shape[0]
    chunk = min(slots, CHUNK)
    chunks = slots // chunk
    place = (sample_of, inner_row, first_col)
    if chunks == 1:
        windows = gather_windows(place)
        depth_flat, preact, grad_rows, loss_sum, grad_head = forward(
            windows, recv_tiles, row_weight
        )
    else:
        split = lambda v: v.reshape((chunks, chunk) + v.shape[1:])
        outs = lax.map(
            lambda xs: forward(gather_windows(xs[0]), xs[1], xs[2]),
            (tuple(split(v) for v in place), split(recv_tiles), split(row_weight)),
        )
        depth_flat, preact, grad_rows = (v.reshape((-1, width)) for v in outs[:3])
        loss_sum, grad_head = jnp.sum(outs[3]), jnp.sum(outs[4], axis=0)
    cell = (recv_start[:, None] + offsets[None, :]).reshape(-1)
    row_ids = jnp.arange(cell.shape[0], dtype=jnp.int32)
    if cell.shape[0] <= 512:
        same_cell = cell[:, None] == cell[None, :]
        grad_y = jnp.dot(
            same_cell.astype(jnp.float32),
            grad_rows,
            precision=lax.Precision.HIGHEST,
            preferred_element_type=jnp.float32,
        )
        repeated = jnp.any(same_cell & (row_ids[None, :] < row_ids[:, None]), axis=1)
    else:
        cells_here = micro_batch * band_rows * block_cols
        grid = jnp.zeros((cells_here, width), jnp.float32).at[cell].add(grad_rows)
        grad_y = grid[cell]
        owner = jnp.full((cells_here,), cell.shape[0], jnp.int32).at[cell].min(row_ids)
        repeated = owner[cell] != row_ids
    sigmoid_u = jax.nn.sigmoid(preact)
    grad_u = (grad_y * sigmoid_u * (1.0 + preact * (1.0 - sigmoid_u))).astype(jnp.bfloat16)
    grad_u = jnp.where(repeated[:, None], jnp.zeros_like(grad_u), grad_u)
    if chunks == 1:
        grad_pw, grad_dw = backward(windows, depth_flat, grad_u)
    else:
        rows_split = lambda v: v.reshape((chunks, chunk * TILE) + v.shape[1:])
        outs = lax.map(
            lambda xs: backward(gather_windows(xs[0]), xs[1], xs[2]),
            (tuple(split(v) for v in place), rows_split(depth_flat), rows_split(grad_u)),
        )
        grad_pw, grad_dw = jnp.sum(outs[0], axis=0), jnp.sum(outs[1], axis=0)
    grad_dw, grad_pw, grad_head, loss_sum = packed_sum(
        (grad_dw, grad_pw, grad_head, loss_sum), ("lat", "lon")
    )
    grad_head = grad_head.T
    return (grad_dw, grad_pw, grad_head, (loss_sum / teach_width).reshape(1))


def solution(mesh):
    in_specs = (
        P("groups", "lat", "lon", None),
        P(),
        P(),
        P(),
        P(),
        P(("groups", "lon", "lat"), None, None),
        P(("groups", "lon", "lat"), None),
        P(("groups", "lon", "lat")),
        P(("groups", "lon", "lat")),
    )
    out_specs = (P("groups", None), P("groups", None), P("groups", None), P("groups"))
    return jax.shard_map(local, mesh=mesh, in_specs=in_specs, out_specs=out_specs, check_vma=False)
```

```python
import jax
import jax.numpy as jnp
from jax import lax
from jax.sharding import PartitionSpec as P

DMAX = 4
TILE = 8
CAP = 2
CHUNK = 32


LANES = 128
EXCHANGED = 2


def halve(x, axis, bit):
    count = lax.axis_size(axis)
    rows = x.shape[0] // 2
    upper = (lax.axis_index(axis) // bit) % 2
    keep = lax.dynamic_slice_in_dim(x, upper * rows, rows, 0)
    send = lax.dynamic_slice_in_dim(x, (1 - upper) * rows, rows, 0)
    return keep + lax.ppermute(send, axis, [(i, i ^ bit) for i in range(count)])


def double(x, axis, bit):
    count = lax.axis_size(axis)
    rows = x.shape[0]
    upper = (lax.axis_index(axis) // bit) % 2
    got = lax.ppermute(x, axis, [(i, i ^ bit) for i in range(count)])
    whole = jnp.zeros((2 * rows,) + x.shape[1:], x.dtype)
    whole = lax.dynamic_update_slice_in_dim(whole, x, upper * rows, 0)
    return lax.dynamic_update_slice_in_dim(whole, got, (1 - upper) * rows, 0)


def packed_sum(values, axes):
    steps = []
    rest = []
    for axis in axes:
        count = lax.axis_size(axis)
        if count & (count - 1):
            rest.append(axis)
            continue
        bit = 1
        while bit < count:
            steps.append((axis, bit))
            bit *= 2
    flat = jnp.concatenate([jnp.ravel(v).astype(jnp.float32) for v in values])
    unit = 8 * LANES * (2 ** len(steps))
    total = -(-flat.shape[0] // unit) * unit
    x = jnp.pad(flat, (0, total - flat.shape[0])).reshape(-1, LANES)
    halved = steps[: max(0, len(steps) - EXCHANGED)]
    for axis, bit in halved:
        x = halve(x, axis, bit)
    for axis, bit in steps[len(halved) :]:
        count = lax.axis_size(axis)
        x = x + lax.ppermute(x, axis, [(i, i ^ bit) for i in range(count)])
    if rest:
        x = lax.psum(x, tuple(rest))
    for axis, bit in reversed(halved):
        x = double(x, axis, bit)
    flat = x.reshape(-1)
    out = []
    offset = 0
    for v in values:
        out.append(flat[offset : offset + v.size].reshape(v.shape))
        offset += v.size
    return tuple(out)


def padded_2(cells, sides, width, closed):
    for axis, dim in sides:
        count = lax.axis_size(axis)
        ends = count if closed else count - 1
        head = lax.slice_in_dim(cells, 0, width, axis=dim)
        tail = lax.slice_in_dim(cells, cells.shape[dim] - width, cells.shape[dim], axis=dim)
        cells = jnp.concatenate(
            [
                lax.ppermute(tail, axis, [(i, (i + 1) % count) for i in range(ends)]),
                cells,
                lax.ppermute(head, axis, [((i + 1) % count, i) for i in range(ends)]),
            ],
            axis=dim,
        )
    return cells


def local(
    acts, rates, dw_kernel, pw_weight, head_weight, teacher_tiles, tile_dest, tile_start, tile_count
):
    micro_batch, band_rows, block_cols, width = acts.shape
    teach_width = head_weight.shape[1]
    lat_index = lax.axis_index("lat")
    lat_count = lax.axis_size("lat")
    lon_count = lax.axis_size("lon")
    devices = lon_count * lat_count
    lon_padded = padded_2(acts, (("lon", 2),), DMAX, True)
    padded = padded_2(lon_padded, (("lat", 1),), DMAX, False)
    tiles_here = teacher_tiles.shape[0]
    destination = tile_dest[:, 0]
    positions = jnp.arange(tiles_here, dtype=jnp.int32)
    same_dest = destination[:, None] == destination[None, :]
    earlier = positions[:, None] > positions[None, :]
    slot_rank = jnp.sum((same_dest & earlier).astype(jnp.int32), axis=1)
    slot_index = destination * CAP + slot_rank
    slots = devices * CAP
    base = 64
    blank = jnp.zeros_like(tile_count)
    column = jnp.stack(
        [tile_start // base, tile_start % base, tile_count] + [blank] * (TILE - 3), axis=1
    )
    packed = jnp.concatenate([teacher_tiles, column.astype(jnp.bfloat16)[:, :, None]], axis=2)
    chooser = (slot_index[None, :] == jnp.arange(slots, dtype=jnp.int32)[:, None]).astype(
        jnp.bfloat16
    )
    send = jnp.einsum(
        "st,tre->sre", chooser, packed, preferred_element_type=jnp.float32
    ).astype(jnp.bfloat16)
    recv = lax.all_to_all(send, ("lon", "lat"), split_axis=0, concat_axis=0, tiled=True)
    recv_tiles = recv[:, :, :teach_width]
    meta = recv[:, :3, teach_width].astype(jnp.int32)
    recv_start = meta[:, 0] * base + meta[:, 1]
    recv_count = meta[:, 2]
    offsets = jnp.arange(TILE, dtype=jnp.int32)
    is_valid = offsets[None, :] < recv_count[:, None]
    sample_of = recv_start // (block_cols * band_rows)
    inner_row = recv_start // block_cols % band_rows
    first_col = recv_start % block_cols
    glob_row = lat_index * band_rows + inner_row
    area_weight = jnp.cos(
        jnp.pi * ((glob_row.astype(jnp.float32) + 0.5) / (band_rows * lat_count) - 0.5)
    )
    row_weight = jnp.where(is_valid, area_weight[:, None], jnp.float32(0.0)) / jnp.float32(
        devices * tiles_here * TILE
    )
    kernel = dw_kernel.astype(jnp.float32)
    onehot = (
        rates[None, :] == jnp.arange(1, DMAX + 1, dtype=jnp.int32)[:, None]
    ).astype(jnp.float32)
    span = 2 * DMAX + 1
    reach = TILE + 2 * DMAX

    def gather_windows(place):
        b, h, w = place
        return jax.vmap(
            lambda b, h, w: lax.dynamic_slice(
                padded, (b, h, w, jnp.int32(0)), (1, span, reach, width)
            )[0]
        )(b, h, w)

    def shifted(source, row_shift, col_shift):
        return source[:, DMAX + row_shift, DMAX + col_shift : DMAX + col_shift + TILE, :].astype(
            jnp.float32
        )

    def chosen_tap(windows, tap_index):
        if tap_index == 4:
            return shifted(windows, 0, 0)
        chosen = None
        for dilation in range(1, DMAX + 1):
            row_shift = (tap_index // 3 - 1) * dilation
            col_shift = (tap_index % 3 - 1) * dilation
            piece = windows[:, DMAX + row_shift, DMAX + col_shift : DMAX + col_shift + TILE, :]
            term = onehot[dilation - 1].astype(jnp.bfloat16) * piece
            chosen = term if chosen is None else chosen + term
        return chosen.astype(jnp.float32)

    def forward(windows, tiles, weight):
        center = shifted(windows, 0, 0)
        accum_sum = center * kernel[4]
        for tap_index in range(9):
            if tap_index != 4:
                accum_sum = accum_sum + kernel[tap_index] * chosen_tap(windows, tap_index)
        depth_flat = accum_sum.astype(jnp.bfloat16).reshape(-1, width)
        preact = jnp.dot(depth_flat, pw_weight, preferred_element_type=jnp.float32)
        y_rows = (center.reshape(-1, width) + jax.nn.silu(preact)).astype(jnp.bfloat16)
        weight = weight.reshape(-1, 1)
        predicted = jnp.dot(y_rows, head_weight, preferred_element_type=jnp.float32)
        residual = predicted - tiles.reshape(-1, teach_width).astype(jnp.float32)
        loss_part = jnp.sum(weight * residual * residual)
        grad_pred = (2.0 * weight * residual).astype(jnp.bfloat16)
        head_part = lax.dot_general(
            grad_pred, y_rows, (((0,), (0,)), ((), ())), preferred_element_type=jnp.float32
        )
        grad_rows = jnp.dot(grad_pred, head_weight.T, preferred_element_type=jnp.float32)
        return depth_flat, preact, grad_rows, loss_part, head_part

    def backward(windows, depth_flat, grad_u):
        pw_part = lax.dot_general(
            depth_flat, grad_u, (((0,), (0,)), ((), ())), preferred_element_type=jnp.float32
        )
        grad_z = jnp.dot(grad_u, pw_weight.T, preferred_element_type=jnp.float32)
        grad_z = grad_z.reshape(windows.shape[0], TILE, width)
        tap_sums = []
        for tap_index in range(9):
            chosen = chosen_tap(windows, tap_index)
            tap_sums.append(jnp.sum((chosen * grad_z).reshape(-1, width), axis=0))
        return pw_part, jnp.stack(tap_sums, axis=0)

    slots = recv_start.shape[0]
    chunk = min(slots, CHUNK)
    chunks = slots // chunk
    place = (sample_of, inner_row, first_col)
    if chunks == 1:
        windows = gather_windows(place)
        depth_flat, preact, grad_rows, loss_sum, grad_head = forward(
            windows, recv_tiles, row_weight
        )
    else:
        split = lambda v: v.reshape((chunks, chunk) + v.shape[1:])
        outs = lax.map(
            lambda xs: forward(gather_windows(xs[0]), xs[1], xs[2]),
            (tuple(split(v) for v in place), split(recv_tiles), split(row_weight)),
        )
        depth_flat, preact, grad_rows = (v.reshape((-1, width)) for v in outs[:3])
        loss_sum, grad_head = jnp.sum(outs[3]), jnp.sum(outs[4], axis=0)
    cell = (recv_start[:, None] + offsets[None, :]).reshape(-1)
    row_ids = jnp.arange(cell.shape[0], dtype=jnp.int32)
    if cell.shape[0] <= 512:
        same_cell = cell[:, None] == cell[None, :]
        grad_y = jnp.dot(
            same_cell.astype(jnp.float32),
            grad_rows,
            precision=lax.Precision.HIGH,
            preferred_element_type=jnp.float32,
        )
        repeated = jnp.any(same_cell & (row_ids[None, :] < row_ids[:, None]), axis=1)
    else:
        cells_here = micro_batch * band_rows * block_cols
        grid = jnp.zeros((cells_here, width), jnp.float32).at[cell].add(grad_rows)
        grad_y = grid[cell]
        owner = jnp.full((cells_here,), cell.shape[0], jnp.int32).at[cell].min(row_ids)
        repeated = owner[cell] != row_ids
    sigmoid_u = jax.nn.sigmoid(preact)
    grad_u = (grad_y * sigmoid_u * (1.0 + preact * (1.0 - sigmoid_u))).astype(jnp.bfloat16)
    grad_u = jnp.where(repeated[:, None], jnp.zeros_like(grad_u), grad_u)
    if chunks == 1:
        grad_pw, grad_dw = backward(windows, depth_flat, grad_u)
    else:
        rows_split = lambda v: v.reshape((chunks, chunk * TILE) + v.shape[1:])
        outs = lax.map(
            lambda xs: backward(gather_windows(xs[0]), xs[1], xs[2]),
            (tuple(split(v) for v in place), rows_split(depth_flat), rows_split(grad_u)),
        )
        grad_pw, grad_dw = jnp.sum(outs[0], axis=0), jnp.sum(outs[1], axis=0)
    grad_dw, grad_pw, grad_head, loss_sum = packed_sum(
        (grad_dw, grad_pw, grad_head, loss_sum), ("lat", "lon")
    )
    grad_head = grad_head.T
    return (grad_dw, grad_pw, grad_head, (loss_sum / teach_width).reshape(1))


def solution(mesh):
    in_specs = (
        P("groups", "lat", "lon", None),
        P(),
        P(),
        P(),
        P(),
        P(("groups", "lon", "lat"), None, None),
        P(("groups", "lon", "lat"), None),
        P(("groups", "lon", "lat")),
        P(("groups", "lon", "lat")),
    )
    out_specs = (P("groups", None), P("groups", None), P("groups", None), P("groups"))
    return jax.shard_map(local, mesh=mesh, in_specs=in_specs, out_specs=out_specs, check_vma=False)
```

```python
import jax
import jax.numpy as jnp
from jax import lax
from jax.sharding import PartitionSpec as P

DMAX = 4
TILE = 8
CAP = 2
CHUNK = 32


LANES = 128
EXCHANGED = 2


def halve(x, axis, bit):
    count = lax.axis_size(axis)
    rows = x.shape[0] // 2
    upper = (lax.axis_index(axis) // bit) % 2
    keep = lax.dynamic_slice_in_dim(x, upper * rows, rows, 0)
    send = lax.dynamic_slice_in_dim(x, (1 - upper) * rows, rows, 0)
    return keep + lax.ppermute(send, axis, [(i, i ^ bit) for i in range(count)])


def double(x, axis, bit):
    count = lax.axis_size(axis)
    rows = x.shape[0]
    upper = (lax.axis_index(axis) // bit) % 2
    got = lax.ppermute(x, axis, [(i, i ^ bit) for i in range(count)])
    whole = jnp.zeros((2 * rows,) + x.shape[1:], x.dtype)
    whole = lax.dynamic_update_slice_in_dim(whole, x, upper * rows, 0)
    return lax.dynamic_update_slice_in_dim(whole, got, (1 - upper) * rows, 0)


def packed_sum(values, axes):
    steps = []
    rest = []
    for axis in axes:
        count = lax.axis_size(axis)
        if count & (count - 1):
            rest.append(axis)
            continue
        bit = 1
        while bit < count:
            steps.append((axis, bit))
            bit *= 2
    flat = jnp.concatenate([jnp.ravel(v).astype(jnp.float32) for v in values])
    unit = 8 * LANES * (2 ** len(steps))
    total = -(-flat.shape[0] // unit) * unit
    x = jnp.pad(flat, (0, total - flat.shape[0])).reshape(-1, LANES)
    halved = steps[: max(0, len(steps) - EXCHANGED)]
    for axis, bit in halved:
        x = halve(x, axis, bit)
    for axis, bit in steps[len(halved) :]:
        count = lax.axis_size(axis)
        x = x + lax.ppermute(x, axis, [(i, i ^ bit) for i in range(count)])
    if rest:
        x = lax.psum(x, tuple(rest))
    for axis, bit in reversed(halved):
        x = double(x, axis, bit)
    flat = x.reshape(-1)
    out = []
    offset = 0
    for v in values:
        out.append(flat[offset : offset + v.size].reshape(v.shape))
        offset += v.size
    return tuple(out)


def padded_2(cells, sides, width, closed):
    for axis, dim in sides:
        count = lax.axis_size(axis)
        ends = count if closed else count - 1
        head = lax.slice_in_dim(cells, 0, width, axis=dim)
        tail = lax.slice_in_dim(cells, cells.shape[dim] - width, cells.shape[dim], axis=dim)
        cells = jnp.concatenate(
            [
                lax.ppermute(tail, axis, [(i, (i + 1) % count) for i in range(ends)]),
                cells,
                lax.ppermute(head, axis, [((i + 1) % count, i) for i in range(ends)]),
            ],
            axis=dim,
        )
    return cells


def local(
    acts, rates, dw_kernel, pw_weight, head_weight, teacher_tiles, tile_dest, tile_start, tile_count
):
    micro_batch, band_rows, block_cols, width = acts.shape
    teach_width = head_weight.shape[1]
    lat_index = lax.axis_index("lat")
    lat_count = lax.axis_size("lat")
    lon_count = lax.axis_size("lon")
    devices = lon_count * lat_count
    lon_padded = padded_2(acts, (("lon", 2),), DMAX, True)
    padded = padded_2(lon_padded, (("lat", 1),), DMAX, False)
    tiles_here = teacher_tiles.shape[0]
    destination = tile_dest[:, 0]
    positions = jnp.arange(tiles_here, dtype=jnp.int32)
    same_dest = destination[:, None] == destination[None, :]
    earlier = positions[:, None] > positions[None, :]
    slot_rank = jnp.sum((same_dest & earlier).astype(jnp.int32), axis=1)
    slot_index = destination * CAP + slot_rank
    slots = devices * CAP
    base = 64
    blank = jnp.zeros_like(tile_count)
    column = jnp.stack(
        [tile_start // base, tile_start % base, tile_count] + [blank] * (TILE - 3), axis=1
    )
    packed = jnp.concatenate([teacher_tiles, column.astype(jnp.bfloat16)[:, :, None]], axis=2)
    chooser = (slot_index[None, :] == jnp.arange(slots, dtype=jnp.int32)[:, None]).astype(
        jnp.bfloat16
    )
    send = jnp.einsum(
        "st,tre->sre", chooser, packed, preferred_element_type=jnp.float32
    ).astype(jnp.bfloat16)
    recv = lax.all_to_all(send, ("lon", "lat"), split_axis=0, concat_axis=0, tiled=True)
    recv_tiles = recv[:, :, :teach_width]
    meta = recv[:, :3, teach_width].astype(jnp.int32)
    recv_start = meta[:, 0] * base + meta[:, 1]
    recv_count = meta[:, 2]
    offsets = jnp.arange(TILE, dtype=jnp.int32)
    is_valid = offsets[None, :] < recv_count[:, None]
    sample_of = recv_start // (block_cols * band_rows)
    inner_row = recv_start // block_cols % band_rows
    first_col = recv_start % block_cols
    glob_row = lat_index * band_rows + inner_row
    area_weight = jnp.cos(
        jnp.pi * ((glob_row.astype(jnp.float32) + 0.5) / (band_rows * lat_count) - 0.5)
    )
    row_weight = jnp.where(is_valid, area_weight[:, None], jnp.float32(0.0)) / jnp.float32(
        devices * tiles_here * TILE
    )
    kernel = dw_kernel.astype(jnp.float32)
    onehot = (
        rates[None, :] == jnp.arange(1, DMAX + 1, dtype=jnp.int32)[:, None]
    ).astype(jnp.float32)
    span = 2 * DMAX + 1
    reach = TILE + 2 * DMAX

    def gather_windows(place):
        b, h, w = place
        return jax.vmap(
            lambda b, h, w: lax.dynamic_slice(
                padded, (b, h, w, jnp.int32(0)), (1, span, reach, width)
            )[0]
        )(b, h, w)

    def shifted(source, row_shift, col_shift):
        return source[:, DMAX + row_shift, DMAX + col_shift : DMAX + col_shift + TILE, :].astype(
            jnp.float32
        )

    def chosen_tap(windows, tap_index):
        if tap_index == 4:
            return shifted(windows, 0, 0)
        chosen = None
        for dilation in range(1, DMAX + 1):
            row_shift = (tap_index // 3 - 1) * dilation
            col_shift = (tap_index % 3 - 1) * dilation
            piece = windows[:, DMAX + row_shift, DMAX + col_shift : DMAX + col_shift + TILE, :]
            term = onehot[dilation - 1].astype(jnp.bfloat16) * piece
            chosen = term if chosen is None else chosen + term
        return chosen.astype(jnp.float32)

    def forward(windows, tiles, weight):
        center = shifted(windows, 0, 0)
        accum_sum = center * kernel[4]
        for tap_index in range(9):
            if tap_index != 4:
                accum_sum = accum_sum + kernel[tap_index] * chosen_tap(windows, tap_index)
        depth_flat = accum_sum.astype(jnp.bfloat16).reshape(-1, width)
        preact = jnp.dot(depth_flat, pw_weight, preferred_element_type=jnp.float32)
        y_rows = (center.reshape(-1, width) + jax.nn.silu(preact)).astype(jnp.bfloat16)
        weight = weight.reshape(-1, 1)
        predicted = jnp.dot(y_rows, head_weight, preferred_element_type=jnp.float32)
        residual = predicted - tiles.reshape(-1, teach_width).astype(jnp.float32)
        loss_part = jnp.sum(weight * residual * residual)
        grad_pred = (2.0 * weight * residual).astype(jnp.bfloat16)
        head_part = lax.dot_general(
            grad_pred, y_rows, (((0,), (0,)), ((), ())), preferred_element_type=jnp.float32
        )
        grad_rows = jnp.dot(grad_pred, head_weight.T, preferred_element_type=jnp.float32)
        return depth_flat, preact, grad_rows, loss_part, head_part

    def backward(windows, depth_flat, grad_u):
        pw_part = lax.dot_general(
            depth_flat, grad_u, (((0,), (0,)), ((), ())), preferred_element_type=jnp.float32
        )
        grad_z = jnp.dot(grad_u, pw_weight.T, preferred_element_type=jnp.float32)
        grad_z = grad_z.reshape(windows.shape[0], TILE, width)
        stacked = jnp.stack([chosen_tap(windows, tap_index) for tap_index in range(9)])
        tap_sums = jnp.sum((stacked * grad_z[None]).reshape(9, -1, width), axis=1)
        return pw_part, tap_sums

    slots = recv_start.shape[0]
    chunk = min(slots, CHUNK)
    chunks = slots // chunk
    place = (sample_of, inner_row, first_col)
    if chunks == 1:
        windows = gather_windows(place)
        depth_flat, preact, grad_rows, loss_sum, grad_head = forward(
            windows, recv_tiles, row_weight
        )
    else:
        split = lambda v: v.reshape((chunks, chunk) + v.shape[1:])
        outs = lax.map(
            lambda xs: forward(gather_windows(xs[0]), xs[1], xs[2]),
            (tuple(split(v) for v in place), split(recv_tiles), split(row_weight)),
        )
        depth_flat, preact, grad_rows = (v.reshape((-1, width)) for v in outs[:3])
        loss_sum, grad_head = jnp.sum(outs[3]), jnp.sum(outs[4], axis=0)
    cell = (recv_start[:, None] + offsets[None, :]).reshape(-1)
    row_ids = jnp.arange(cell.shape[0], dtype=jnp.int32)
    if cell.shape[0] <= 512:
        same_cell = cell[:, None] == cell[None, :]
        grad_y = jnp.dot(
            same_cell.astype(jnp.float32),
            grad_rows,
            precision=lax.Precision.HIGHEST,
            preferred_element_type=jnp.float32,
        )
        repeated = jnp.any(same_cell & (row_ids[None, :] < row_ids[:, None]), axis=1)
    else:
        cells_here = micro_batch * band_rows * block_cols
        grid = jnp.zeros((cells_here, width), jnp.float32).at[cell].add(grad_rows)
        grad_y = grid[cell]
        owner = jnp.full((cells_here,), cell.shape[0], jnp.int32).at[cell].min(row_ids)
        repeated = owner[cell] != row_ids
    sigmoid_u = jax.nn.sigmoid(preact)
    grad_u = (grad_y * sigmoid_u * (1.0 + preact * (1.0 - sigmoid_u))).astype(jnp.bfloat16)
    grad_u = jnp.where(repeated[:, None], jnp.zeros_like(grad_u), grad_u)
    if chunks == 1:
        grad_pw, grad_dw = backward(windows, depth_flat, grad_u)
    else:
        rows_split = lambda v: v.reshape((chunks, chunk * TILE) + v.shape[1:])
        outs = lax.map(
            lambda xs: backward(gather_windows(xs[0]), xs[1], xs[2]),
            (tuple(split(v) for v in place), rows_split(depth_flat), rows_split(grad_u)),
        )
        grad_pw, grad_dw = jnp.sum(outs[0], axis=0), jnp.sum(outs[1], axis=0)
    grad_dw, grad_pw, grad_head, loss_sum = packed_sum(
        (grad_dw, grad_pw, grad_head, loss_sum), ("lat", "lon")
    )
    grad_head = grad_head.T
    return (grad_dw, grad_pw, grad_head, (loss_sum / teach_width).reshape(1))


def solution(mesh):
    in_specs = (
        P("groups", "lat", "lon", None),
        P(),
        P(),
        P(),
        P(),
        P(("groups", "lon", "lat"), None, None),
        P(("groups", "lon", "lat"), None),
        P(("groups", "lon", "lat")),
        P(("groups", "lon", "lat")),
    )
    out_specs = (P("groups", None), P("groups", None), P("groups", None), P("groups"))
    return jax.shard_map(local, mesh=mesh, in_specs=in_specs, out_specs=out_specs, check_vma=False)
```
